32 devices in a mesh: group: 2 (over x), tm: 16 (over z, y, core).
Axes of the slice: x: 2, y: 2, z: 4, core: 2. Of those that a mesh axis runs over, the one named last changes fastest.
Arguments:
- queries: bfloat16 [8192, 1536], P(('group', 'tm')), parts along dimension 0, may hold values from -7 to 7, as said below
- keys: bfloat16 [8192, 1536], P(('group', 'tm')), parts along dimension 0, may hold values from -6 to 6, as said below
- values: bfloat16 [8192, 1536], P(('group', 'tm')), parts along dimension 0, may hold values from -6 to 6
- grad_out: bfloat16 [8192, 1536], P(('group', 'tm')), parts along dimension 0, may hold values from -96 to 96
- block_list: int32 [128, 30], P(('group', 'tm')), parts along dimension 0, may hold values 0 or 1
Outputs:
- grad_queries: bfloat16 [8192, 1536], P(('group', 'tm')), parts along dimension 0
- grad_keys: bfloat16 [8192, 1536], P(('group', 'tm')), parts along dimension 0
- grad_values: bfloat16 [8192, 1536], P(('group', 'tm')), parts along dimension 0
The draws below stay inside these ranges and needn't reach their ends.
There are 2 independent parts, one for each index of `group`. The reference program is written for one: setup_inputs(seed, part) draws one part's arguments, and reference() takes and returns one part's arrays. A program takes and returns all parts, laid end to end along the dimension named above; each array names one. Nothing has to cross between parts.
Inputs may be any that keep to these rules, and one draw needn't show every extreme that they name: `queries`: entries of order one. `keys`: entries of order one. `block_list`: columns follow the candidate order of the steps.
All inputs are finite; a program needn't handle non-finite values. No bound on the sum of `block_list` on one device may be relied on, other than what follows from the above.
Results may differ from the reference program's by a relative error of at most 0.0073.
Values may be sent and summed in bfloat16 or wider, within the bound.
No kernel may reach another device: no remote copies, remote signals or barrier semaphores. Data moves between devices by JAX's collectives and lax.ppermute only.
A program may use at most 128 MiB of HBM per device.

```python
import jax
import jax.numpy as jnp
import numpy as np
from jax import lax

HEADS = 12
HDIM = 128
BLOCK = 64
REACH = 2
FRAMES = 2
BANDS = 2
TOKENS = 4096
QBLOCKS = 64
CANDS = 30
N_TM = 16


def draw_pair(key):
    base = jax.random.fold_in(key, 11)
    key_query, key_key = jax.random.split(base, 2)
    width = HEADS * HDIM
    query_vals = jnp.clip(jax.random.normal(key_query, (TOKENS, width), jnp.float32), -6.0, 6.0)
    key_vals = jnp.clip(jax.random.normal(key_key, (TOKENS, width), jnp.float32), -6.0, 6.0)
    return (query_vals, key_vals)


def draw_queries(key, part):
    return draw_pair(key)[0].astype(jnp.bfloat16)


def draw_keys(key, part):
    return draw_pair(key)[1].astype(jnp.bfloat16)


def with_ends(entries, rng, smallest, high):
    spot = [jax.random.randint(jax.random.fold_in(rng, axis), (), 0, length) for axis, length in enumerate(entries.shape)]
    main_axis = entries.shape.index(max(entries.shape))
    beside = spot[:main_axis] + [(spot[main_axis] + 1) % entries.shape[main_axis]] + spot[main_axis + 1:]
    return entries.at[tuple(spot)].set(smallest).at[tuple(beside)].set(high)


def block_levels(rng, extent, cuts, low, top_value):
    level, own = 1.0, jax.random.fold_in(rng, 6)
    for dim, blocks in cuts:
        heights = jnp.exp(jax.random.uniform(jax.random.fold_in(own, dim), (blocks,), jnp.float32, low / len(cuts), top_value / len(cuts)))
        level = level * jnp.repeat(heights, extent[dim] // blocks).reshape([-1 if axis == dim else 1 for axis in range(len(extent))])
    return level


def gaussian(rng, shape, scale, most, pieces=(), kind=jnp.bfloat16):
    result = jax.random.normal(rng, shape, jnp.float32) * scale
    if len(pieces) > 0:
        result = block_levels(rng, shape, pieces, -0.22, 0.18) * result
    return jnp.clip(result, min=-most, max=most).astype(kind)


def setup_inputs(seed: int = 0, part: int = 0) -> dict:
    arg_keys = jax.random.split(jax.random.key(seed), 6)
    part_splits = jax.random.split(jax.random.fold_in(arg_keys[5], part), 6)
    return {
        "queries": draw_queries(jax.random.fold_in(jax.random.fold_in(arg_keys[5], part), 71), part),
        "keys": draw_keys(jax.random.fold_in(jax.random.fold_in(arg_keys[5], part), 71), part),
        "values": gaussian(part_splits[2], (TOKENS, HEADS * HDIM), 1.0, 6.0, ((0, 16),)),
        "grad_out": gaussian(part_splits[3], (TOKENS, HEADS * HDIM), 16.0, 96.0, ((0, 16),)),
        "block_list": with_ends((jax.random.randint(part_splits[4], (QBLOCKS, CANDS), 0, 3) < 2).astype(jnp.int32), jax.random.fold_in(part_splits[4], 1), 0, 1),
    }


def settle(tensor):
    return lax.optimization_barrier(tensor.astype(jnp.bfloat16)).astype(jnp.float32)


def pair_tables(slots):
    blocks_group = FRAMES * BANDS
    query_block = np.arange(blocks_group)[:, None]
    key_block = np.arange(slots * blocks_group)[None, :]
    slot_of = key_block // blocks_group
    frame_key = (key_block // BANDS) % FRAMES
    band_key = key_block % BANDS
    frame_query = query_block // BANDS
    band_query = query_block % BANDS
    cand = (slot_of * FRAMES + frame_key) * 3 + band_key - band_query + 1
    own_block = (slot_of == REACH) & (frame_key == frame_query) & (band_key == band_query)
    cand = cand + 0 * query_block
    slot_full = slot_of + 0 * query_block
    return cand, own_block, slot_full


def listed_mask(block_rows, group_index, groups):
    slots = 2 * REACH + 1
    cand, own_block, slot_full = pair_tables(slots)
    chosen = (block_rows > 0)[np.arange(FRAMES * BANDS)[:, None], cand]
    group_pos = group_index + jnp.asarray(slot_full, jnp.int32) - REACH
    group_ok = (group_pos >= 0) & (group_pos < groups)
    allowed = (chosen & group_ok) | jnp.asarray(own_block)
    return allowed[:, None, :, None]


def group_grads(query_rows, grad_rows, key_window, value_window, block_rows, group_index, groups):
    scaling = HDIM ** -0.5
    allowed = listed_mask(block_rows, group_index, groups)
    slots = key_window.shape[0]
    tok_dev = FRAMES * BANDS * BLOCK
    width = HEADS * HDIM
    key_flat = key_window.reshape(slots * tok_dev, width)
    value_flat = value_window.reshape(slots * tok_dev, width)
    query_list, key_list, value_list = [], [], []
    for head_index in range(HEADS):
        cols = slice(head_index * HDIM, (head_index + 1) * HDIM)
        query_head = query_rows[:, cols].astype(jnp.float32)
        grad_head = grad_rows[:, cols].astype(jnp.float32)
        key_head = key_flat[:, cols].astype(jnp.float32)
        value_head = value_flat[:, cols].astype(jnp.float32)
        scores = jnp.einsum('qd,kd->qk', query_head, key_head) * scaling
        shaped = jnp.where(allowed, scores.reshape(FRAMES * BANDS, BLOCK, slots * FRAMES * BANDS, BLOCK), -jnp.inf)
        row_max = jnp.max(shaped, axis=(2, 3), keepdims=True)
        log_total = row_max + jnp.log(jnp.sum(jnp.exp(shaped - row_max), axis=(2, 3), keepdims=True))
        weights = jnp.exp(shaped - log_total).reshape(scores.shape)
        weights_low = settle(weights)
        attended = jnp.einsum('qk,kd->qd', weights_low, value_head)
        deltas = jnp.sum(grad_head * attended, axis=-1, keepdims=True)
        grad_probs = jnp.einsum('qd,kd->qk', grad_head, value_head)
        grad_scores = settle(weights * (grad_probs - deltas))
        query_list.append(jnp.einsum('qk,kd->qd', grad_scores, key_head) * scaling)
        key_list.append((jnp.einsum('qk,qd->kd', grad_scores, query_head) * scaling).reshape(slots, tok_dev, HDIM))
        value_list.append(jnp.einsum('qk,qd->kd', weights_low, grad_head).reshape(slots, tok_dev, HDIM))
    return jnp.concatenate(query_list, axis=-1), jnp.concatenate(key_list, axis=-1), jnp.concatenate(value_list, axis=-1)


def reference(queries, keys, values, grad_out, block_list):
    groups = N_TM
    tok_dev = FRAMES * BANDS * BLOCK
    width = HEADS * HDIM
    slots = 2 * REACH + 1
    key_pad = jnp.pad(keys.reshape(groups, tok_dev, width), ((REACH, REACH), (0, 0), (0, 0)))
    value_pad = jnp.pad(values.reshape(groups, tok_dev, width), ((REACH, REACH), (0, 0), (0, 0)))
    query_groups = queries.reshape(groups, tok_dev, width)
    grad_groups = grad_out.reshape(groups, tok_dev, width)
    list_groups = block_list.reshape(groups, FRAMES * BANDS, CANDS)

    def visit_group(totals, inputs):
        key_total, value_total = totals
        query_rows, grad_rows, block_rows, group_index = inputs
        key_window = lax.dynamic_slice_in_dim(key_pad, group_index, slots, 0)
        value_window = lax.dynamic_slice_in_dim(value_pad, group_index, slots, 0)
        query_grad, key_grad, value_grad = group_grads(query_rows, grad_rows, key_window, value_window, block_rows, group_index, groups)
        key_now = lax.dynamic_slice_in_dim(key_total, group_index, slots, 0) + settle(key_grad)
        value_now = lax.dynamic_slice_in_dim(value_total, group_index, slots, 0) + settle(value_grad)
        key_total = lax.dynamic_update_slice_in_dim(key_total, key_now, group_index, 0)
        value_total = lax.dynamic_update_slice_in_dim(value_total, value_now, group_index, 0)
        return (key_total, value_total), query_grad.astype(jnp.bfloat16)

    zeros_acc = jnp.zeros((groups + 2 * REACH, tok_dev, width), jnp.float32)
    (key_total, value_total), query_grads = lax.scan(visit_group, (zeros_acc, zeros_acc), (query_groups, grad_groups, list_groups, jnp.arange(groups, dtype=jnp.int32)))
    grad_queries = query_grads.reshape(TOKENS, width)
    grad_keys = key_total[REACH:REACH + groups].reshape(TOKENS, width).astype(jnp.bfloat16)
    grad_values = value_total[REACH:REACH + groups].reshape(TOKENS, width).astype(jnp.bfloat16)
    return (grad_queries, grad_keys, grad_values)
```

```python
import jax
import jax.numpy as jnp
import numpy as np
from jax import lax
from jax.sharding import PartitionSpec as P

HEADS = 12
HDIM = 128
BLOCK = 64
REACH = 2
FRAMES = 2
BANDS = 2
NEG = -1e30


def from_behind(value, axis, steps):
    count = lax.axis_size(axis)
    first, last = (max(0, -steps), min(count, count - steps))
    return lax.ppermute(value, axis, [(source, source + steps) for source in range(first, last)])


def pick_table(offset):
    blocks = FRAMES * BANDS
    slot = REACH - offset
    table = np.zeros((blocks, 30, blocks), np.float32)
    own = np.zeros((blocks, blocks), bool)
    for qb in range(blocks):
        for kb in range(blocks):
            cand = (slot * FRAMES + kb // BANDS) * 3 + kb % BANDS - qb % BANDS + 1
            table[qb, cand, kb] = 1.0
            own[qb, kb] = offset == 0 and qb == kb
    return table, own


def pair_mask(block_rows, offset, valid):
    table, own = pick_table(offset)
    chosen = jnp.einsum("qc,qck->qk", block_rows.astype(jnp.float32), jnp.asarray(table)) > 0
    return (chosen & valid) | jnp.asarray(own)


def expand(mask4):
    return mask4[None, :, None, :, None]


def blocked(x):
    return x.reshape(HEADS, FRAMES * BANDS, BLOCK, FRAMES * BANDS, BLOCK)


def local(queries, keys, values, grad_out, block_list):
    groups = lax.axis_size("tm")
    here = lax.axis_index("tm")
    scaling = HDIM ** (-0.5)
    tok = queries.shape[0]
    key_h = keys.reshape(tok, HEADS, HDIM)
    value_h = values.reshape(tok, HEADS, HDIM)
    offsets = list(range(-REACH, REACH + 1))

    arrived = {}
    for offset in offsets:
        if offset == 0:
            arrived[offset] = (queries, grad_out, block_list)
        else:
            arrived[offset] = from_behind((queries, grad_out, block_list), "tm", -offset)

    parts = {}
    stats_back = {}
    for offset in offsets:
        q_rows, g_rows, b_rows = arrived[offset]
        source = here + offset
        valid = (source >= 0) & (source < groups)
        mask = expand(pair_mask(b_rows, offset, valid))
        q_h = q_rows.reshape(tok, HEADS, HDIM)
        g_h = g_rows.reshape(tok, HEADS, HDIM)
        scores = blocked(
            jnp.einsum("qhd,khd->hqk", q_h, key_h, preferred_element_type=jnp.float32) * scaling
        )
        grad_probs = blocked(
            jnp.einsum("qhd,khd->hqk", g_h, value_h, preferred_element_type=jnp.float32)
        )
        masked = jnp.where(mask, scores, NEG)
        row_max = jnp.max(masked, axis=(3, 4))
        expd = jnp.where(mask, jnp.exp(masked - row_max[:, :, :, None, None]), 0.0)
        row_sum = jnp.sum(expd, axis=(3, 4))
        row_dot = jnp.sum(expd * grad_probs, axis=(3, 4))
        stats = jnp.stack([row_max, row_sum, row_dot]).reshape(3, HEADS, tok)
        parts[offset] = (q_h, g_h, mask, scores, grad_probs)
        stats_back[offset] = stats if offset == 0 else from_behind(stats, "tm", offset)

    all_stats = jnp.stack([stats_back[offset] for offset in offsets])
    maxes, sums, dots = all_stats[:, 0], all_stats[:, 1], all_stats[:, 2]
    top = jnp.max(maxes, axis=0)
    scale = jnp.exp(maxes - top[None])
    total = jnp.sum(sums * scale, axis=0)
    log_total = top + jnp.log(total)
    deltas = jnp.sum(dots * scale, axis=0) / total
    final = jnp.stack([log_total, deltas])

    key_grad = jnp.zeros((tok, HEADS, HDIM), jnp.float32)
    value_grad = jnp.zeros((tok, HEADS, HDIM), jnp.float32)
    query_grad = None
    for offset in offsets:
        q_h, g_h, mask, scores, grad_probs = parts[offset]
        got = final if offset == 0 else from_behind(final, "tm", -offset)
        lse = got[0].reshape(HEADS, FRAMES * BANDS, BLOCK)[:, :, :, None, None]
        dlt = got[1].reshape(HEADS, FRAMES * BANDS, BLOCK)[:, :, :, None, None]
        weights = jnp.where(mask, jnp.exp(scores - lse), 0.0)
        weights_low = weights.astype(jnp.bfloat16).reshape(HEADS, tok, tok)
        grad_scores = (weights * (grad_probs - dlt)).astype(jnp.bfloat16).reshape(HEADS, tok, tok)
        key_grad = key_grad + jnp.einsum(
            "hqk,qhd->khd", grad_scores, q_h, preferred_element_type=jnp.float32
        ) * scaling
        value_grad = value_grad + jnp.einsum(
            "hqk,qhd->khd", weights_low, g_h, preferred_element_type=jnp.float32
        )
        q_part = jnp.einsum(
            "hqk,khd->qhd", grad_scores, key_h, preferred_element_type=jnp.float32
        ) * scaling
        if offset == 0:
            own_part = q_part
        else:
            sent = from_behind(q_part.astype(jnp.bfloat16), "tm", offset).astype(jnp.float32)
            query_grad = sent if query_grad is None else query_grad + sent
    query_grad = query_grad + own_part
    return (
        query_grad.reshape(tok, HEADS * HDIM).astype(jnp.bfloat16),
        key_grad.reshape(tok, HEADS * HDIM).astype(jnp.bfloat16),
        value_grad.reshape(tok, HEADS * HDIM).astype(jnp.bfloat16),
    )


def solution(mesh):
    placed = (
        P(("group", "tm"), None),
        P(("group", "tm"), None),
        P(("group", "tm"), None),
        P(("group", "tm"), None),
        P(("group", "tm"), None),
    )
    return jax.shard_map(
        local,
        mesh=mesh,
        in_specs=placed,
        out_specs=(P(("group", "tm"), None), P(("group", "tm"), None), P(("group", "tm"), None)),
        check_vma=False,
    )
```

```python
import jax
import jax.numpy as jnp
import numpy as np
from jax import lax
from jax.sharding import PartitionSpec as P

HEADS = 12
HDIM = 128
BLOCK = 64
REACH = 2
FRAMES = 2
BANDS = 2
NEG = -1e30
LIST_ROWS = 16


def from_behind(value, axis, steps):
    count = lax.axis_size(axis)
    first, last = (max(0, -steps), min(count, count - steps))
    return lax.ppermute(value, axis, [(source, source + steps) for source in range(first, last)])


def swap_cores(value):
    count = lax.axis_size("tm")
    return lax.ppermute(value, "tm", [(source, source ^ 1) for source in range(count)])


def swap_chips(value):
    count = lax.axis_size("tm")
    pairs = []
    for source in range(count):
        target = source - 1 if source % 2 == 0 else source + 1
        if 0 <= target < count:
            pairs.append((source, target))
    return lax.ppermute(value, "tm", pairs)


def pick_table(offset):
    blocks = FRAMES * BANDS
    slot = REACH - offset
    table = np.zeros((blocks, 30, blocks), np.float32)
    own = np.zeros((blocks, blocks), bool)
    for qb in range(blocks):
        for kb in range(blocks):
            cand = (slot * FRAMES + kb // BANDS) * 3 + kb % BANDS - qb % BANDS + 1
            table[qb, cand, kb] = 1.0
            own[qb, kb] = offset == 0 and qb == kb
    return table, own


def pair_mask(list_rows, table, own, valid):
    chosen = jnp.einsum("qc,qck->qk", list_rows, table) > 0
    return (chosen & valid) | own


def blocked(x):
    return x.reshape(HEADS, FRAMES * BANDS, BLOCK, FRAMES * BANDS, BLOCK)


def local(queries, keys, values, grad_out, block_list):
    groups = lax.axis_size("tm")
    here = lax.axis_index("tm")
    even = here % 2 == 0
    scaling = HDIM ** (-0.5)
    tok, width = queries.shape
    blocks = FRAMES * BANDS
    cands = block_list.shape[1]
    key_h = keys.reshape(tok, HEADS, HDIM)
    value_h = values.reshape(tok, HEADS, HDIM)

    flags = (block_list > 0).astype(jnp.bfloat16).reshape(1, blocks * cands)
    flags = jnp.pad(flags, ((0, LIST_ROWS - 1), (0, width - blocks * cands)))
    pack = jnp.concatenate([queries, grad_out, flags], axis=0)

    from_below = from_behind(pack, "tm", 2)
    from_above = from_behind(pack, "tm", -2)
    relay = jnp.where(even, from_above, from_below)
    partner, relayed = swap_cores((pack, relay))

    up = jnp.where(even, 1, -1)
    slots = {
        "own": (pack, 0),
        "below": (from_below, -2),
        "above": (from_above, 2),
        "partner": (partner, up),
        "relayed": (relayed, -up),
    }
    static_tables = {offset: pick_table(offset) for offset in (-2, -1, 0, 1, 2)}

    def tables_for(offset):
        if isinstance(offset, int):
            table, own = static_tables[offset]
            return jnp.asarray(table), jnp.asarray(own)
        t_up, o_up = static_tables[1]
        t_dn, o_dn = static_tables[-1]
        return (
            jnp.where(offset > 0, jnp.asarray(t_up), jnp.asarray(t_dn)),
            jnp.where(offset > 0, jnp.asarray(o_up), jnp.asarray(o_dn)),
        )

    parts = {}
    stats_out = {}
    for name, (data, offset) in slots.items():
        q_h = data[:tok].reshape(tok, HEADS, HDIM)
        g_h = data[tok : 2 * tok].reshape(tok, HEADS, HDIM)
        list_rows = data[2 * tok, : blocks * cands].astype(jnp.float32).reshape(blocks, cands)
        source = here + offset
        valid = (source >= 0) & (source < groups)
        table, own = tables_for(offset)
        mask = pair_mask(list_rows, table, own, valid)[None, :, None, :, None]
        scores = blocked(
            jnp.einsum("qhd,khd->hqk", q_h, key_h, preferred_element_type=jnp.float32) * scaling
        )
        grad_probs = blocked(
            jnp.einsum("qhd,khd->hqk", g_h, value_h, preferred_element_type=jnp.float32)
        )
        masked = jnp.where(mask, scores, NEG)
        row_max = jnp.max(masked, axis=(3, 4))
        expd = jnp.where(mask, jnp.exp(masked - row_max[:, :, :, None, None]), 0.0)
        row_sum = jnp.sum(expd, axis=(3, 4))
        row_dot = jnp.sum(expd * grad_probs, axis=(3, 4))
        parts[name] = (q_h, g_h, mask, scores, grad_probs)
        stats_out[name] = jnp.stack([row_max, row_sum, row_dot]).reshape(3, HEADS, tok)

    stats_in = {
        "own": (stats_out["own"], 0),
        "below": (from_behind(stats_out["above"], "tm", 2), -2),
        "above": (from_behind(stats_out["below"], "tm", -2), 2),
        "partner": (swap_cores(stats_out["partner"]), up),
        "relayed": (swap_chips(stats_out["relayed"]), -up),
    }
    maxes, sums, dots = [], [], []
    for name, (stats, offset) in stats_in.items():
        source = here + offset
        valid = (source >= 0) & (source < groups)
        maxes.append(jnp.where(valid, stats[0], NEG))
        sums.append(jnp.where(valid, stats[1], 0.0))
        dots.append(jnp.where(valid, stats[2], 0.0))
    maxes, sums, dots = jnp.stack(maxes), jnp.stack(sums), jnp.stack(dots)
    top = jnp.max(maxes, axis=0)
    scale = jnp.exp(maxes - top[None])
    total = jnp.sum(sums * scale, axis=0)
    log_total = top + jnp.log(total)
    deltas = jnp.sum(dots * scale, axis=0) / total
    final = jnp.stack([log_total, deltas])

    finals = {
        "own": final,
        "below": from_behind(final, "tm", 2),
        "above": from_behind(final, "tm", -2),
        "partner": swap_cores(final),
        "relayed": swap_chips(final),
    }

    key_grad = jnp.zeros((tok, HEADS, HDIM), jnp.float32)
    value_grad = jnp.zeros((tok, HEADS, HDIM), jnp.float32)
    q_parts = {}
    for name in slots:
        q_h, g_h, mask, scores, grad_probs = parts[name]
        got = finals[name]
        lse = got[0].reshape(HEADS, blocks, BLOCK)[:, :, :, None, None]
        dlt = got[1].reshape(HEADS, blocks, BLOCK)[:, :, :, None, None]
        weights = jnp.where(mask, jnp.exp(scores - lse), 0.0)
        weights_low = weights.astype(jnp.bfloat16).reshape(HEADS, tok, tok)
        grad_scores = (weights * (grad_probs - dlt)).astype(jnp.bfloat16).reshape(HEADS, tok, tok)
        key_grad = key_grad + jnp.einsum(
            "hqk,qhd->khd", grad_scores, q_h, preferred_element_type=jnp.float32
        ) * scaling
        value_grad = value_grad + jnp.einsum(
            "hqk,qhd->khd", weights_low, g_h, preferred_element_type=jnp.float32
        )
        q_parts[name] = jnp.einsum(
            "hqk,khd->qhd", grad_scores, key_h, preferred_element_type=jnp.float32
        ) * scaling

    from_partner, relay_part = swap_cores((q_parts["partner"], q_parts["relayed"]))
    zero = jnp.zeros_like(relay_part)
    send_up = q_parts["above"] + jnp.where(even, relay_part, zero)
    send_down = q_parts["below"] + jnp.where(even, zero, relay_part)
    got_below = from_behind(send_up.astype(jnp.bfloat16), "tm", 2).astype(jnp.float32)
    got_above = from_behind(send_down.astype(jnp.bfloat16), "tm", -2).astype(jnp.float32)
    query_grad = q_parts["own"] + from_partner + got_below + got_above
    return (
        query_grad.reshape(tok, width).astype(jnp.bfloat16),
        key_grad.reshape(tok, width).astype(jnp.bfloat16),
        value_grad.reshape(tok, width).astype(jnp.bfloat16),
    )


def solution(mesh):
    placed = (
        P(("group", "tm"), None),
        P(("group", "tm"), None),
        P(("group", "tm"), None),
        P(("group", "tm"), None),
        P(("group", "tm"), None),
    )
    return jax.shard_map(
        local,
        mesh=mesh,
        in_specs=placed,
        out_specs=(P(("group", "tm"), None), P(("group", "tm"), None), P(("group", "tm"), None)),
        check_vma=False,
    )
```

```python
import jax
import jax.numpy as jnp
import numpy as np
from jax import lax
from jax.sharding import PartitionSpec as P

HEADS = 12
HDIM = 128
BLOCK = 64
REACH = 2
FRAMES = 2
BANDS = 2
NEG = -1e30
LIST_ROWS = 16


def permute(value, rule):
    count = lax.axis_size("tm")
    pairs = []
    for source in range(count):
        target = rule(source)
        if 0 <= target < count:
            pairs.append((source, target))
    return lax.ppermute(value, "tm", pairs)


def swap_cores(value):
    return permute(value, lambda s: s ^ 1)


def down_even(value):
    return permute(value, lambda s: s - 2 if s % 2 == 0 else s + 2)


def up_even(value):
    return permute(value, lambda s: s + 2 if s % 2 == 0 else s - 2)


def pick_table(offset):
    blocks = FRAMES * BANDS
    slot = REACH - offset
    table = np.zeros((blocks, 30, blocks), np.float32)
    own = np.zeros((blocks, blocks), bool)
    if abs(offset) <= REACH:
        for qb in range(blocks):
            for kb in range(blocks):
                cand = (slot * FRAMES + kb // BANDS) * 3 + kb % BANDS - qb % BANDS + 1
                table[qb, cand, kb] = 1.0
                own[qb, kb] = offset == 0 and qb == kb
    return table, own


def parity_tables(even, even_offsets, odd_offsets):
    tables, owns = [], []
    for off_e, off_o in zip(even_offsets, odd_offsets):
        t_e, o_e = pick_table(off_e)
        t_o, o_o = pick_table(off_o)
        tables.append(jnp.where(even, jnp.asarray(t_e), jnp.asarray(t_o)))
        owns.append(jnp.where(even, jnp.asarray(o_e), jnp.asarray(o_o)))
    return jnp.concatenate(tables, axis=2), jnp.concatenate(owns, axis=1)


def local(queries, keys, values, grad_out, block_list):
    groups = lax.axis_size("tm")
    here = lax.axis_index("tm")
    even = here % 2 == 0
    up = jnp.where(even, 1, -1)
    scaling = HDIM ** (-0.5)
    tok, width = queries.shape
    blocks = FRAMES * BANDS
    cands = block_list.shape[1]

    flags = (block_list > 0).astype(jnp.bfloat16).reshape(1, blocks * cands)
    flags = jnp.pad(flags, ((0, LIST_ROWS - 1), (0, width - blocks * cands)))
    pack = jnp.concatenate([queries, grad_out, flags], axis=0)

    far_data = down_even(pack)
    near_data = up_even(pack)
    partner_keys, partner_values = swap_cores((keys, values))

    key_own = keys.reshape(tok, HEADS, HDIM)
    value_own = values.reshape(tok, HEADS, HDIM)
    key_both = jnp.concatenate([keys, partner_keys], axis=0).reshape(2 * tok, HEADS, HDIM)
    value_both = jnp.concatenate([values, partner_values], axis=0).reshape(2 * tok, HEADS, HDIM)

    slots = {
        "far": (far_data, 2 * up, "both", (2, 1), (-2, -1)),
        "near": (near_data, -2 * up, "own", (-2,), (2,)),
        "own": (pack, 0, "own_both", (0, -1), (0, 1)),
    }

    parts = {}
    stats_out = {}
    for name in ("own", "far", "near"):
        data, q_off, key_set, offs_e, offs_o = slots[name]
        if key_set == "own":
            key_h, value_h = key_own, value_own
        else:
            key_h, value_h = key_both, value_both
        nkb = key_h.shape[0] // BLOCK
        q_h = data[:tok].reshape(tok, HEADS, HDIM)
        g_h = data[tok : 2 * tok].reshape(tok, HEADS, HDIM)
        list_rows = data[2 * tok, : blocks * cands].astype(jnp.float32).reshape(blocks, cands)
        source = here + q_off
        valid = (source >= 0) & (source < groups)
        table, own = parity_tables(even, offs_e, offs_o)
        chosen = jnp.einsum("qc,qck->qk", list_rows, table) > 0
        mask = ((chosen & valid) | own)[None, :, None, :, None]
        shape5 = (HEADS, blocks, BLOCK, nkb, BLOCK)
        scores = (
            jnp.einsum("qhd,khd->hqk", q_h, key_h, preferred_element_type=jnp.float32) * scaling
        ).reshape(shape5)
        grad_probs = jnp.einsum(
            "qhd,khd->hqk", g_h, value_h, preferred_element_type=jnp.float32
        ).reshape(shape5)
        masked = jnp.where(mask, scores, NEG)
        row_max = jnp.max(masked, axis=(3, 4))
        expd = jnp.where(mask, jnp.exp(masked - row_max[:, :, :, None, None]), 0.0)
        row_sum = jnp.sum(expd, axis=(3, 4))
        row_dot = jnp.sum(expd * grad_probs, axis=(3, 4))
        parts[name] = (q_h, g_h, key_h, mask, scores, grad_probs)
        stats_out[name] = jnp.stack([row_max, row_sum, row_dot]).reshape(3, HEADS, tok)

    stats_in = [
        (stats_out["own"], 0),
        (up_even(stats_out["far"]), -2 * up),
        (down_even(stats_out["near"]), 2 * up),
    ]
    maxes, sums, dots = [], [], []
    for stats, offset in stats_in:
        source = here + offset
        valid = (source >= 0) & (source < groups)
        maxes.append(jnp.where(valid, stats[0], NEG))
        sums.append(jnp.where(valid, stats[1], 0.0))
        dots.append(jnp.where(valid, stats[2], 0.0))
    maxes, sums, dots = jnp.stack(maxes), jnp.stack(sums), jnp.stack(dots)
    top = jnp.max(maxes, axis=0)
    scale = jnp.exp(maxes - top[None])
    total = jnp.sum(sums * scale, axis=0)
    log_total = top + jnp.log(total)
    deltas = jnp.sum(dots * scale, axis=0) / total
    final = jnp.stack([log_total, deltas])
    finals = {"own": final, "far": down_even(final), "near": up_even(final)}

    def backward(name, got):
        q_h, g_h, key_h, mask, scores, grad_probs = parts[name]
        lse = got[0].reshape(HEADS, blocks, BLOCK)[:, :, :, None, None]
        dlt = got[1].reshape(HEADS, blocks, BLOCK)[:, :, :, None, None]
        weights = jnp.where(mask, jnp.exp(scores - lse), 0.0)
        nk = key_h.shape[0]
        weights_low = weights.astype(jnp.bfloat16).reshape(HEADS, tok, nk)
        grad_scores = (weights * (grad_probs - dlt)).astype(jnp.bfloat16).reshape(HEADS, tok, nk)
        q_part = jnp.einsum(
            "hqk,khd->qhd", grad_scores, key_h, preferred_element_type=jnp.float32
        ) * scaling
        return q_h, g_h, weights_low, grad_scores, q_part

    far_b = backward("far", finals["far"])
    near_b = backward("near", finals["near"])
    far_send, near_send, far_b, near_b, own_final = lax.optimization_barrier(
        (far_b[4].astype(jnp.bfloat16), near_b[4].astype(jnp.bfloat16), far_b, near_b, final)
    )
    from_far = up_even(far_send)
    from_near = down_even(near_send)
    own_b = backward("own", own_final)

    def key_value(b):
        q_h, g_h, weights_low, grad_scores, _ = b
        kg = jnp.einsum("hqk,qhd->khd", grad_scores, q_h, preferred_element_type=jnp.float32)
        vg = jnp.einsum("hqk,qhd->khd", weights_low, g_h, preferred_element_type=jnp.float32)
        return kg * scaling, vg

    kg_far, vg_far = key_value(far_b)
    kg_own, vg_own = key_value(own_b)
    kg_near, vg_near = key_value(near_b)
    partner_kg = kg_far[tok:] + kg_own[tok:]
    partner_vg = vg_far[tok:] + vg_own[tok:]
    back_kg, back_vg = swap_cores((partner_kg, partner_vg))
    key_grad = kg_far[:tok] + kg_own[:tok] + kg_near + back_kg
    value_grad = vg_far[:tok] + vg_own[:tok] + vg_near + back_vg
    query_grad = (
        own_b[4] + from_far.astype(jnp.float32) + from_near.astype(jnp.float32)
    )
    return (
        query_grad.reshape(tok, width).astype(jnp.bfloat16),
        key_grad.reshape(tok, width).astype(jnp.bfloat16),
        value_grad.reshape(tok, width).astype(jnp.bfloat16),
    )


def solution(mesh):
    placed = (
        P(("group", "tm"), None),
        P(("group", "tm"), None),
        P(("group", "tm"), None),
        P(("group", "tm"), None),
        P(("group", "tm"), None),
    )
    return jax.shard_map(
        local,
        mesh=mesh,
        in_specs=placed,
        out_specs=(P(("group", "tm"), None), P(("group", "tm"), None), P(("group", "tm"), None)),
        check_vma=False,
    )
```

```python
import jax
import jax.numpy as jnp
import numpy as np
from jax import lax
from jax.sharding import PartitionSpec as P

HEADS = 12
HDIM = 128
BLOCK = 64
REACH = 2
FRAMES = 2
BANDS = 2
NEG = -1e30
LIST_ROWS = 16


def permute(value, rule):
    count = lax.axis_size("tm")
    pairs = []
    for source in range(count):
        target = rule(source)
        if 0 <= target < count:
            pairs.append((source, target))
    return lax.ppermute(value, "tm", pairs)


def swap_cores(value):
    return permute(value, lambda s: s ^ 1)


def down_even(value):
    return permute(value, lambda s: s - 2 if s % 2 == 0 else s + 2)


def up_even(value):
    return permute(value, lambda s: s + 2 if s % 2 == 0 else s - 2)


def pick_table(offset):
    blocks = FRAMES * BANDS
    slot = REACH - offset
    table = np.zeros((blocks, 30, blocks), np.float32)
    own = np.zeros((blocks, blocks), bool)
    if abs(offset) <= REACH:
        for qb in range(blocks):
            for kb in range(blocks):
                cand = (slot * FRAMES + kb // BANDS) * 3 + kb % BANDS - qb % BANDS + 1
                table[qb, cand, kb] = 1.0
                own[qb, kb] = offset == 0 and qb == kb
    return table, own


def parity_tables(even, even_offsets, odd_offsets):
    tables, owns = [], []
    for off_e, off_o in zip(even_offsets, odd_offsets):
        t_e, o_e = pick_table(off_e)
        t_o, o_o = pick_table(off_o)
        tables.append(jnp.where(even, jnp.asarray(t_e), jnp.asarray(t_o)))
        owns.append(jnp.where(even, jnp.asarray(o_e), jnp.asarray(o_o)))
    return jnp.concatenate(tables, axis=2), jnp.concatenate(owns, axis=1)


def chunk_grads(here, groups, data, key_own, value_own, key_partner, value_partner):
    even = here % 2 == 0
    up = jnp.where(even, 1, -1)
    scaling = HDIM ** (-0.5)
    tok, heads, _ = key_own.shape
    blocks = FRAMES * BANDS
    key_both = jnp.concatenate([key_own, key_partner], axis=0)
    value_both = jnp.concatenate([value_own, value_partner], axis=0)

    slots = {
        "own": (0, "both", (0, -1), (0, 1)),
        "far": (2 * up, "both", (2, 1), (-2, -1)),
        "near": (-2 * up, "own", (-2,), (2,)),
    }
    parts = {}
    stats_out = {}
    for name, (q_off, key_set, offs_e, offs_o) in slots.items():
        q_h, g_h, list_rows = data[name]
        if key_set == "own":
            key_h, value_h = key_own, value_own
        else:
            key_h, value_h = key_both, value_both
        nkb = key_h.shape[0] // BLOCK
        source = here + q_off
        valid = (source >= 0) & (source < groups)
        table, own = parity_tables(even, offs_e, offs_o)
        chosen = jnp.einsum("qc,qck->qk", (list_rows > 0).astype(jnp.float32), table) > 0
        mask = ((chosen & valid) | own)[None, :, None, :, None]
        shape5 = (heads, blocks, BLOCK, nkb, BLOCK)
        scores = (
            jnp.einsum("qhd,khd->hqk", q_h, key_h, preferred_element_type=jnp.float32) * scaling
        ).reshape(shape5)
        grad_probs = jnp.einsum(
            "qhd,khd->hqk", g_h, value_h, preferred_element_type=jnp.float32
        ).reshape(shape5)
        masked = jnp.where(mask, scores, NEG)
        row_max = jnp.max(masked, axis=(3, 4))
        expd = jnp.where(mask, jnp.exp(masked - row_max[:, :, :, None, None]), 0.0)
        row_sum = jnp.sum(expd, axis=(3, 4))
        row_dot = jnp.sum(expd * grad_probs, axis=(3, 4))
        parts[name] = (q_h, g_h, key_h, mask, scores, grad_probs)
        stats_out[name] = jnp.stack([row_max, row_sum, row_dot]).reshape(3, heads, tok)

    stats_in = [
        (stats_out["own"], 0),
        (up_even(stats_out["far"]), -2 * up),
        (down_even(stats_out["near"]), 2 * up),
    ]
    maxes, sums, dots = [], [], []
    for stats, offset in stats_in:
        source = here + offset
        valid = (source >= 0) & (source < groups)
        maxes.append(jnp.where(valid, stats[0], NEG))
        sums.append(jnp.where(valid, stats[1], 0.0))
        dots.append(jnp.where(valid, stats[2], 0.0))
    maxes, sums, dots = jnp.stack(maxes), jnp.stack(sums), jnp.stack(dots)
    top = jnp.max(maxes, axis=0)
    scale = jnp.exp(maxes - top[None])
    total = jnp.sum(sums * scale, axis=0)
    log_total = top + jnp.log(total)
    deltas = jnp.sum(dots * scale, axis=0) / total
    final = jnp.stack([log_total, deltas])
    finals = {"far": down_even(final), "near": up_even(final)}

    def backward(name, got):
        q_h, g_h, key_h, mask, scores, grad_probs = parts[name]
        lse = got[0].reshape(heads, blocks, BLOCK)[:, :, :, None, None]
        dlt = got[1].reshape(heads, blocks, BLOCK)[:, :, :, None, None]
        weights = jnp.where(mask, jnp.exp(scores - lse), 0.0)
        nk = key_h.shape[0]
        weights_low = weights.astype(jnp.bfloat16).reshape(heads, tok, nk)
        grad_scores = (weights * (grad_probs - dlt)).astype(jnp.bfloat16).reshape(heads, tok, nk)
        q_part = jnp.einsum(
            "hqk,khd->qhd", grad_scores, key_h, preferred_element_type=jnp.float32
        ) * scaling
        return q_h, g_h, weights_low, grad_scores, q_part

    far_b = backward("far", finals["far"])
    near_b = backward("near", finals["near"])
    far_send, near_send, far_b, near_b, own_final = lax.optimization_barrier(
        (far_b[4].astype(jnp.bfloat16), near_b[4].astype(jnp.bfloat16), far_b, near_b, final)
    )
    from_far = up_even(far_send)
    from_near = down_even(near_send)
    own_b = backward("own", own_final)

    def key_value(b):
        q_h, g_h, weights_low, grad_scores, _ = b
        kg = jnp.einsum("hqk,qhd->khd", grad_scores, q_h, preferred_element_type=jnp.float32)
        vg = jnp.einsum("hqk,qhd->khd", weights_low, g_h, preferred_element_type=jnp.float32)
        return kg * scaling, vg

    kg_far, vg_far = key_value(far_b)
    kg_own, vg_own = key_value(own_b)
    kg_near, vg_near = key_value(near_b)
    partner_kg = kg_far[tok:] + kg_own[tok:]
    partner_vg = vg_far[tok:] + vg_own[tok:]
    back_kg, back_vg = swap_cores((partner_kg, partner_vg))
    key_grad = kg_far[:tok] + kg_own[:tok] + kg_near + back_kg
    value_grad = vg_far[:tok] + vg_own[:tok] + vg_near + back_vg
    query_grad = own_b[4] + from_far.astype(jnp.float32) + from_near.astype(jnp.float32)
    return query_grad, key_grad, value_grad


def local(queries, keys, values, grad_out, block_list):
    groups = lax.axis_size("tm")
    here = lax.axis_index("tm")
    tok, width = queries.shape
    blocks = FRAMES * BANDS
    chunks = 2
    per = HEADS // chunks

    def heads_of(x, c):
        return x.reshape(tok, HEADS, HDIM)[:, c * per : (c + 1) * per]

    lists = {"own": block_list, "far": down_even(block_list), "near": up_even(block_list)}
    partner_keys, partner_values = swap_cores((keys, values))

    results = []
    held = None
    for c in range(chunks):
        q_c = heads_of(queries, c)
        g_c = heads_of(grad_out, c)
        if held is not None:
            q_c, g_c, _ = lax.optimization_barrier((q_c, g_c, held))
        far_q, far_g = down_even((q_c, g_c))
        near_q, near_g = up_even((q_c, g_c))
        held = (far_q, far_g, near_q, near_g)
        data = {
            "own": (q_c, g_c, lists["own"]),
            "far": (far_q, far_g, lists["far"]),
            "near": (near_q, near_g, lists["near"]),
        }
        results.append(
            chunk_grads(
                here,
                groups,
                data,
                heads_of(keys, c),
                heads_of(values, c),
                heads_of(partner_keys, c),
                heads_of(partner_values, c),
            )
        )
    outs = []
    for i in range(3):
        joined = jnp.concatenate([r[i] for r in results], axis=1)
        outs.append(joined.reshape(tok, width).astype(jnp.bfloat16))
    return tuple(outs)


def solution(mesh):
    placed = (
        P(("group", "tm"), None),
        P(("group", "tm"), None),
        P(("group", "tm"), None),
        P(("group", "tm"), None),
        P(("group", "tm"), None),
    )
    return jax.shard_map(
        local,
        mesh=mesh,
        in_specs=placed,
        out_specs=(P(("group", "tm"), None), P(("group", "tm"), None), P(("group", "tm"), None)),
        check_vma=False,
    )
```

```python
import jax
import jax.numpy as jnp
import numpy as np
from jax import lax
from jax.experimental import pallas as pl
from jax.experimental.pallas import tpu as pltpu
from jax.sharding import PartitionSpec as P

HEADS = 12
HDIM = 128
BLOCK = 64
REACH = 2
FRAMES = 2
BANDS = 2
NEG = -1e30
LIST_ROWS = 16


def permute(value, rule):
    count = lax.axis_size("tm")
    pairs = []
    for source in range(count):
        target = rule(source)
        if 0 <= target < count:
            pairs.append((source, target))
    return lax.ppermute(value, "tm", pairs)


def swap_cores(value):
    return permute(value, lambda s: s ^ 1)


def down_even(value):
    return permute(value, lambda s: s - 2 if s % 2 == 0 else s + 2)


def up_even(value):
    return permute(value, lambda s: s + 2 if s % 2 == 0 else s - 2)


def pick_table(offset):
    blocks = FRAMES * BANDS
    slot = REACH - offset
    table = np.zeros((blocks, 30, blocks), np.float32)
    own = np.zeros((blocks, blocks), bool)
    if abs(offset) <= REACH:
        for qb in range(blocks):
            for kb in range(blocks):
                cand = (slot * FRAMES + kb // BANDS) * 3 + kb % BANDS - qb % BANDS + 1
                table[qb, cand, kb] = 1.0
                own[qb, kb] = offset == 0 and qb == kb
    return table, own


def parity_tables(even, even_offsets, odd_offsets):
    tables, owns = [], []
    for off_e, off_o in zip(even_offsets, odd_offsets):
        t_e, o_e = pick_table(off_e)
        t_o, o_o = pick_table(off_o)
        tables.append(jnp.where(even, jnp.asarray(t_e), jnp.asarray(t_o)))
        owns.append(jnp.where(even, jnp.asarray(o_e), jnp.asarray(o_o)))
    return jnp.concatenate(tables, axis=2), jnp.concatenate(owns, axis=1)


SCALE = HDIM ** (-0.5)
NT = (((1,), (1,)), ((), ()))


def slot_scores(q_ref, g_ref, k_ref, v_ref):
    q = q_ref[...]
    g = g_ref[...]
    s = lax.dot_general(k_ref[...], q, NT, preferred_element_type=jnp.float32) * SCALE
    dp = lax.dot_general(v_ref[...], g, NT, preferred_element_type=jnp.float32)
    return q, g, s, dp


def stats_kernel(q_ref, g_ref, k_ref, v_ref, m_ref, out_ref):
    _, _, s, dp = slot_scores(q_ref, g_ref, k_ref, v_ref)
    m = m_ref[...] > 0
    masked = jnp.where(m, s, NEG)
    mx = jnp.max(masked, axis=0, keepdims=True)
    e = jnp.where(m, jnp.exp(masked - mx), 0.0)
    total = jnp.sum(e, axis=0, keepdims=True)
    dot = jnp.sum(e * dp, axis=0, keepdims=True)
    out_ref[0] = jnp.concatenate([mx, total, dot], axis=0)


def back_kernel(q_ref, g_ref, k_ref, v_ref, m_ref, f_ref, dq_ref, dk_ref, dv_ref):
    q, g, s, dp = slot_scores(q_ref, g_ref, k_ref, v_ref)
    m = m_ref[...] > 0
    fin = f_ref[0]
    p = jnp.where(m, jnp.exp(s - fin[0:1]), 0.0)
    ds = (p * (dp - fin[1:2])).astype(jnp.bfloat16)
    dk_ref[...] = jnp.dot(ds, q, preferred_element_type=jnp.float32) * SCALE
    dv_ref[...] = jnp.dot(p.astype(jnp.bfloat16), g, preferred_element_type=jnp.float32)
    dq = lax.dot_general(ds, k_ref[...], (((0,), (0,)), ((), ())), preferred_element_type=jnp.float32)
    dq_ref[...] = (dq * SCALE).astype(dq_ref.dtype)


def slot_specs(q_rows, g_rows, nk, tok):
    return [
        pl.BlockSpec((tok, HDIM), lambda h: (q_rows, h)),
        pl.BlockSpec((tok, HDIM), lambda h: (g_rows, h)),
        pl.BlockSpec((nk, HDIM), lambda h: (0, h)),
        pl.BlockSpec((nk, HDIM), lambda h: (0, h)),
        pl.BlockSpec((nk, tok), lambda h: (0, 0)),
    ]


def slot_stats(q_arr, g_arr, q_rows, g_rows, key_arr, value_arr, mask_t, tok):
    nk = key_arr.shape[0]
    flops = 4 * tok * nk * HDIM * HEADS
    return pl.pallas_call(
        stats_kernel,
        grid=(HEADS,),
        in_specs=slot_specs(q_rows, g_rows, nk, tok),
        out_specs=pl.BlockSpec((1, 3, tok), lambda h: (h, 0, 0)),
        out_shape=jax.ShapeDtypeStruct((HEADS, 3, tok), jnp.float32),
        cost_estimate=pl.CostEstimate(
            flops=flops, transcendentals=tok * nk * HEADS, bytes_accessed=4 * (tok + nk) * HDIM * HEADS
        ),
    )(q_arr, g_arr, key_arr, value_arr, mask_t)


def slot_back(q_arr, g_arr, q_rows, g_rows, key_arr, value_arr, mask_t, fin, tok, dq_type):
    nk = key_arr.shape[0]
    width = HEADS * HDIM
    flops = 10 * tok * nk * HDIM * HEADS
    return pl.pallas_call(
        back_kernel,
        grid=(HEADS,),
        in_specs=slot_specs(q_rows, g_rows, nk, tok)
        + [pl.BlockSpec((1, 2, tok), lambda h: (h, 0, 0))],
        out_specs=[
            pl.BlockSpec((tok, HDIM), lambda h: (0, h)),
            pl.BlockSpec((nk, HDIM), lambda h: (0, h)),
            pl.BlockSpec((nk, HDIM), lambda h: (0, h)),
        ],
        out_shape=[
            jax.ShapeDtypeStruct((tok, width), dq_type),
            jax.ShapeDtypeStruct((nk, width), jnp.float32),
            jax.ShapeDtypeStruct((nk, width), jnp.float32),
        ],
        cost_estimate=pl.CostEstimate(
            flops=flops, transcendentals=tok * nk * HEADS, bytes_accessed=12 * (tok + nk) * HDIM * HEADS
        ),
    )(q_arr, g_arr, key_arr, value_arr, mask_t, fin)


def local(queries, keys, values, grad_out, block_list):
    groups = lax.axis_size("tm")
    here = lax.axis_index("tm")
    even = here % 2 == 0
    up = jnp.where(even, 1, -1)
    tok, width = queries.shape
    blocks = FRAMES * BANDS
    cands = block_list.shape[1]

    flags = (block_list > 0).astype(jnp.bfloat16).reshape(1, blocks * cands)
    flags = jnp.pad(flags, ((0, LIST_ROWS - 1), (0, width - blocks * cands)))
    pack = jnp.concatenate([queries, grad_out, flags], axis=0)

    far_data = down_even(pack)
    near_data = up_even(pack)
    partner_keys, partner_values = swap_cores((keys, values))
    key_both = jnp.concatenate([keys, partner_keys], axis=0)
    value_both = jnp.concatenate([values, partner_values], axis=0)

    slots = {
        "own": (queries, grad_out, 0, 0, block_list, 0, True, (0, -1), (0, 1)),
        "far": (far_data, far_data, 0, 1, None, 2 * up, True, (2, 1), (-2, -1)),
        "near": (near_data, near_data, 0, 1, None, -2 * up, False, (-2,), (2,)),
    }

    args = {}
    stats_out = {}
    for name, (q_arr, g_arr, q_rows, g_rows, rows, q_off, both, offs_e, offs_o) in slots.items():
        if rows is None:
            rows = q_arr[2 * tok, : blocks * cands].reshape(blocks, cands)
        key_arr, value_arr = (key_both, value_both) if both else (keys, values)
        nkb = key_arr.shape[0] // BLOCK
        source = here + q_off
        valid = (source >= 0) & (source < groups)
        table, own = parity_tables(even, offs_e, offs_o)
        chosen = jnp.einsum("qc,qck->qk", (rows > 0).astype(jnp.float32), table) > 0
        mask4 = (chosen & valid) | own
        mask_t = jnp.broadcast_to(
            mask4.T[:, None, :, None], (nkb, BLOCK, blocks, BLOCK)
        ).reshape(nkb * BLOCK, tok).astype(jnp.float32)
        args[name] = (q_arr, g_arr, q_rows, g_rows, key_arr, value_arr, mask_t)
        stats_out[name] = slot_stats(*args[name], tok)

    stats_in = [
        (stats_out["own"], 0),
        (up_even(stats_out["far"]), -2 * up),
        (down_even(stats_out["near"]), 2 * up),
    ]
    maxes, sums, dots = [], [], []
    for stats, offset in stats_in:
        source = here + offset
        valid = (source >= 0) & (source < groups)
        maxes.append(jnp.where(valid, stats[:, 0], NEG))
        sums.append(jnp.where(valid, stats[:, 1], 0.0))
        dots.append(jnp.where(valid, stats[:, 2], 0.0))
    maxes, sums, dots = jnp.stack(maxes), jnp.stack(sums), jnp.stack(dots)
    top = jnp.max(maxes, axis=0)
    scale = jnp.exp(maxes - top[None])
    total = jnp.sum(sums * scale, axis=0)
    log_total = top + jnp.log(total)
    deltas = jnp.sum(dots * scale, axis=0) / total
    final = jnp.stack([log_total, deltas], axis=1)
    finals = {"far": down_even(final), "near": up_even(final)}

    far_q, far_k, far_v = slot_back(*args["far"], finals["far"], tok, jnp.bfloat16)
    near_q, near_k, near_v = slot_back(*args["near"], finals["near"], tok, jnp.bfloat16)
    far_q, near_q, far_k, far_v, near_k, near_v, own_final = lax.optimization_barrier(
        (far_q, near_q, far_k, far_v, near_k, near_v, final)
    )
    from_far = up_even(far_q)
    from_near = down_even(near_q)
    own_q, own_k, own_v = slot_back(*args["own"], own_final, tok, jnp.float32)

    back_kg, back_vg = swap_cores((far_k[tok:] + own_k[tok:], far_v[tok:] + own_v[tok:]))
    key_grad = far_k[:tok] + own_k[:tok] + near_k + back_kg
    value_grad = far_v[:tok] + own_v[:tok] + near_v + back_vg
    query_grad = own_q + from_far.astype(jnp.float32) + from_near.astype(jnp.float32)
    return (
        query_grad.astype(jnp.bfloat16),
        key_grad.astype(jnp.bfloat16),
        value_grad.astype(jnp.bfloat16),
    )


def solution(mesh):
    placed = (
        P(("group", "tm"), None),
        P(("group", "tm"), None),
        P(("group", "tm"), None),
        P(("group", "tm"), None),
        P(("group", "tm"), None),
    )
    return jax.shard_map(
        local,
        mesh=mesh,
        in_specs=placed,
        out_specs=(P(("group", "tm"), None), P(("group", "tm"), None), P(("group", "tm"), None)),
        check_vma=False,
    )
```

```python
import jax
import jax.numpy as jnp
import numpy as np
from jax import lax
from jax.experimental import pallas as pl
from jax.experimental.pallas import tpu as pltpu
from jax.sharding import PartitionSpec as P

HEADS = 12
HDIM = 128
BLOCK = 64
REACH = 2
FRAMES = 2
BANDS = 2
NEG = -1e30
LIST_ROWS = 16


def permute(value, rule):
    count = lax.axis_size("tm")
    pairs = []
    for source in range(count):
        target = rule(source)
        if 0 <= target < count:
            pairs.append((source, target))
    return lax.ppermute(value, "tm", pairs)


def swap_cores(value):
    return permute(value, lambda s: s ^ 1)


def down_even(value):
    return permute(value, lambda s: s - 2 if s % 2 == 0 else s + 2)


def up_even(value):
    return permute(value, lambda s: s + 2 if s % 2 == 0 else s - 2)


def pick_table(offset):
    blocks = FRAMES * BANDS
    slot = REACH - offset
    table = np.zeros((blocks, 30, blocks), np.float32)
    own = np.zeros((blocks, blocks), bool)
    if abs(offset) <= REACH:
        for qb in range(blocks):
            for kb in range(blocks):
                cand = (slot * FRAMES + kb // BANDS) * 3 + kb % BANDS - qb % BANDS + 1
                table[qb, cand, kb] = 1.0
                own[qb, kb] = offset == 0 and qb == kb
    return table, own


def parity_tables(even, even_offsets, odd_offsets):
    tables, owns = [], []
    for off_e, off_o in zip(even_offsets, odd_offsets):
        t_e, o_e = pick_table(off_e)
        t_o, o_o = pick_table(off_o)
        tables.append(jnp.where(even, jnp.asarray(t_e), jnp.asarray(t_o)))
        owns.append(jnp.where(even, jnp.asarray(o_e), jnp.asarray(o_o)))
    return jnp.concatenate(tables, axis=2), jnp.concatenate(owns, axis=1)


SCALE = HDIM ** (-0.5)
NT = (((1,), (1,)), ((), ()))


def slot_scores(q_ref, g_ref, k_ref, v_ref):
    q = q_ref[...]
    g = g_ref[...]
    s = lax.dot_general(k_ref[...], q, NT, preferred_element_type=jnp.float32) * SCALE
    dp = lax.dot_general(v_ref[...], g, NT, preferred_element_type=jnp.float32)
    return q, g, s, dp


def stats_kernel(q_ref, g_ref, k_ref, v_ref, m_ref, out_ref):
    _, _, s, dp = slot_scores(q_ref, g_ref, k_ref, v_ref)
    m = m_ref[...] > 0
    masked = jnp.where(m, s, NEG)
    mx = jnp.max(masked, axis=0, keepdims=True)
    e = jnp.where(m, jnp.exp(masked - mx), 0.0)
    total = jnp.sum(e, axis=0, keepdims=True)
    dot = jnp.sum(e * dp, axis=0, keepdims=True)
    out_ref[0] = jnp.concatenate([mx, total, dot], axis=0)


def back_kernel(q_ref, g_ref, k_ref, v_ref, m_ref, f_ref, dq_ref, dk_ref, dv_ref):
    q, g, s, dp = slot_scores(q_ref, g_ref, k_ref, v_ref)
    m = m_ref[...] > 0
    fin = f_ref[0]
    p = jnp.where(m, jnp.exp(s - fin[0:1]), 0.0)
    ds = (p * (dp - fin[1:2])).astype(jnp.bfloat16)
    dk_ref[...] = jnp.dot(ds, q, preferred_element_type=jnp.float32) * SCALE
    dv_ref[...] = jnp.dot(p.astype(jnp.bfloat16), g, preferred_element_type=jnp.float32)
    dq = lax.dot_general(ds, k_ref[...], (((0,), (0,)), ((), ())), preferred_element_type=jnp.float32)
    dq_ref[...] = (dq * SCALE).astype(dq_ref.dtype)


def slot_specs(q_rows, g_rows, nk, tok):
    return [
        pl.BlockSpec((tok, HDIM), lambda h: (q_rows, h)),
        pl.BlockSpec((tok, HDIM), lambda h: (g_rows, h)),
        pl.BlockSpec((nk, HDIM), lambda h: (0, h)),
        pl.BlockSpec((nk, HDIM), lambda h: (0, h)),
        pl.BlockSpec((nk, tok), lambda h: (0, 0)),
    ]


def slot_stats(q_arr, g_arr, q_rows, g_rows, key_arr, value_arr, mask_t, tok):
    nk = key_arr.shape[0]
    flops = 4 * tok * nk * HDIM * HEADS
    return pl.pallas_call(
        stats_kernel,
        grid=(HEADS,),
        in_specs=slot_specs(q_rows, g_rows, nk, tok),
        out_specs=pl.BlockSpec((1, 3, tok), lambda h: (h, 0, 0)),
        out_shape=jax.ShapeDtypeStruct((HEADS, 3, tok), jnp.float32),
        cost_estimate=pl.CostEstimate(
            flops=flops, transcendentals=tok * nk * HEADS, bytes_accessed=4 * (tok + nk) * HDIM * HEADS
        ),
    )(q_arr, g_arr, key_arr, value_arr, mask_t)


def slot_back(q_arr, g_arr, q_rows, g_rows, key_arr, value_arr, mask_t, fin, tok, dq_type):
    nk = key_arr.shape[0]
    width = HEADS * HDIM
    flops = 10 * tok * nk * HDIM * HEADS
    return pl.pallas_call(
        back_kernel,
        grid=(HEADS,),
        in_specs=slot_specs(q_rows, g_rows, nk, tok)
        + [pl.BlockSpec((1, 2, tok), lambda h: (h, 0, 0))],
        out_specs=[
            pl.BlockSpec((tok, HDIM), lambda h: (0, h)),
            pl.BlockSpec((nk, HDIM), lambda h: (0, h)),
            pl.BlockSpec((nk, HDIM), lambda h: (0, h)),
        ],
        out_shape=[
            jax.ShapeDtypeStruct((tok, width), dq_type),
            jax.ShapeDtypeStruct((nk, width), jnp.float32),
            jax.ShapeDtypeStruct((nk, width), jnp.float32),
        ],
        cost_estimate=pl.CostEstimate(
            flops=flops, transcendentals=tok * nk * HEADS, bytes_accessed=12 * (tok + nk) * HDIM * HEADS
        ),
    )(q_arr, g_arr, key_arr, value_arr, mask_t, fin)


def local(queries, keys, values, grad_out, block_list):
    groups = lax.axis_size("tm")
    here = lax.axis_index("tm")
    even = here % 2 == 0
    up = jnp.where(even, 1, -1)
    tok, width = queries.shape
    blocks = FRAMES * BANDS
    cands = block_list.shape[1]

    flags = (block_list > 0).astype(jnp.bfloat16).reshape(1, blocks * cands)
    flags = jnp.pad(flags, ((0, LIST_ROWS - 1), (0, width - blocks * cands)))
    pack = jnp.concatenate([queries, grad_out, flags], axis=0)

    far_data = down_even(pack)
    near_data = up_even(pack)
    partner_keys, partner_values = swap_cores((keys, values))
    key_both = jnp.concatenate([keys, partner_keys], axis=0)
    value_both = jnp.concatenate([values, partner_values], axis=0)

    slots = {
        "own": (queries, grad_out, 0, 0, block_list, 0, True, (0, -1), (0, 1)),
        "far": (far_data, far_data, 0, 1, None, 2 * up, True, (2, 1), (-2, -1)),
        "near": (near_data, near_data, 0, 1, None, -2 * up, False, (-2,), (2,)),
    }

    args = {}
    stats_out = {}
    for name, (q_arr, g_arr, q_rows, g_rows, rows, q_off, both, offs_e, offs_o) in slots.items():
        if rows is None:
            rows = q_arr[2 * tok, : blocks * cands].reshape(blocks, cands)
        key_arr, value_arr = (key_both, value_both) if both else (keys, values)
        nkb = key_arr.shape[0] // BLOCK
        source = here + q_off
        valid = (source >= 0) & (source < groups)
        table, own = parity_tables(even, offs_e, offs_o)
        chosen = jnp.einsum("qc,qck->qk", (rows > 0).astype(jnp.float32), table) > 0
        mask4 = (chosen & valid) | own
        mask_t = jnp.broadcast_to(
            mask4.T[:, None, :, None], (nkb, BLOCK, blocks, BLOCK)
        ).reshape(nkb * BLOCK, tok).astype(jnp.float32)
        args[name] = (q_arr, g_arr, q_rows, g_rows, key_arr, value_arr, mask_t)
        stats_out[name] = slot_stats(*args[name], tok)

    stats_in = [
        (stats_out["own"], 0),
        (up_even(stats_out["far"]), -2 * up),
        (down_even(stats_out["near"]), 2 * up),
    ]
    maxes, sums, dots = [], [], []
    for stats, offset in stats_in:
        source = here + offset
        valid = (source >= 0) & (source < groups)
        maxes.append(jnp.where(valid, stats[:, 0], NEG))
        sums.append(jnp.where(valid, stats[:, 1], 0.0))
        dots.append(jnp.where(valid, stats[:, 2], 0.0))
    maxes, sums, dots = jnp.stack(maxes), jnp.stack(sums), jnp.stack(dots)
    top = jnp.max(maxes, axis=0)
    scale = jnp.exp(maxes - top[None])
    total = jnp.sum(sums * scale, axis=0)
    log_total = top + jnp.log(total)
    deltas = jnp.sum(dots * scale, axis=0) / total
    final = jnp.stack([log_total, deltas], axis=1)
    finals = {"far": down_even(final), "near": up_even(final)}

    own_q, own_k, own_v = slot_back(*args["own"], final, tok, jnp.float32)
    far_fin, near_fin, own_k, own_v = lax.optimization_barrier(
        (finals["far"], finals["near"], own_k, own_v)
    )
    finals = {"far": far_fin, "near": near_fin}
    far_q, far_k, far_v = slot_back(*args["far"], finals["far"], tok, jnp.bfloat16)
    near_q, near_k, near_v = slot_back(*args["near"], finals["near"], tok, jnp.bfloat16)
    from_far = up_even(far_q)
    from_near = down_even(near_q)

    back_kg, back_vg = swap_cores((far_k[tok:] + own_k[tok:], far_v[tok:] + own_v[tok:]))
    key_grad = far_k[:tok] + own_k[:tok] + near_k + back_kg
    value_grad = far_v[:tok] + own_v[:tok] + near_v + back_vg
    query_grad = own_q + from_far.astype(jnp.float32) + from_near.astype(jnp.float32)
    return (
        query_grad.astype(jnp.bfloat16),
        key_grad.astype(jnp.bfloat16),
        value_grad.astype(jnp.bfloat16),
    )


def solution(mesh):
    placed = (
        P(("group", "tm"), None),
        P(("group", "tm"), None),
        P(("group", "tm"), None),
        P(("group", "tm"), None),
        P(("group", "tm"), None),
    )
    return jax.shard_map(
        local,
        mesh=mesh,
        in_specs=placed,
        out_specs=(P(("group", "tm"), None), P(("group", "tm"), None), P(("group", "tm"), None)),
        check_vma=False,
    )
```

```python
import jax
import jax.numpy as jnp
import numpy as np
from jax import lax
from jax.experimental import pallas as pl
from jax.experimental.pallas import tpu as pltpu
from jax.sharding import PartitionSpec as P

HEADS = 12
HDIM = 128
BLOCK = 64
REACH = 2
FRAMES = 2
BANDS = 2
NEG = -1e30
LIST_ROWS = 16


def permute(value, rule):
    count = lax.axis_size("tm")
    pairs = []
    for source in range(count):
        target = rule(source)
        if 0 <= target < count:
            pairs.append((source, target))
    return lax.ppermute(value, "tm", pairs)


def swap_cores(value):
    return permute(value, lambda s: s ^ 1)


def down_even(value):
    return permute(value, lambda s: s - 2 if s % 2 == 0 else s + 2)


def up_even(value):
    return permute(value, lambda s: s + 2 if s % 2 == 0 else s - 2)


def pick_table(offset):
    blocks = FRAMES * BANDS
    slot = REACH - offset
    table = np.zeros((blocks, 30, blocks), np.float32)
    own = np.zeros((blocks, blocks), bool)
    if abs(offset) <= REACH:
        for qb in range(blocks):
            for kb in range(blocks):
                cand = (slot * FRAMES + kb // BANDS) * 3 + kb % BANDS - qb % BANDS + 1
                table[qb, cand, kb] = 1.0
                own[qb, kb] = offset == 0 and qb == kb
    return table, own


def parity_tables(even, even_offsets, odd_offsets):
    tables, owns = [], []
    for off_e, off_o in zip(even_offsets, odd_offsets):
        t_e, o_e = pick_table(off_e)
        t_o, o_o = pick_table(off_o)
        tables.append(jnp.where(even, jnp.asarray(t_e), jnp.asarray(t_o)))
        owns.append(jnp.where(even, jnp.asarray(o_e), jnp.asarray(o_o)))
    return jnp.concatenate(tables, axis=2), jnp.concatenate(owns, axis=1)


SCALE = HDIM ** (-0.5)
NT = (((1,), (1,)), ((), ()))
STEP_HEADS = 4


def slot_scores(q, g, k, v):
    s = lax.dot_general(k, q, NT, preferred_element_type=jnp.float32) * SCALE
    dp = lax.dot_general(v, g, NT, preferred_element_type=jnp.float32)
    return s, dp


def head_cols(j):
    return slice(j * HDIM, (j + 1) * HDIM)


def stats_kernel(q_ref, g_ref, k_ref, v_ref, m_ref, out_ref):
    m = m_ref[...] > 0
    for j in range(STEP_HEADS):
        cols = head_cols(j)
        s, dp = slot_scores(q_ref[:, cols], g_ref[:, cols], k_ref[:, cols], v_ref[:, cols])
        masked = jnp.where(m, s, NEG)
        mx = jnp.max(masked, axis=0, keepdims=True)
        e = jnp.where(m, jnp.exp(masked - mx), 0.0)
        total = jnp.sum(e, axis=0, keepdims=True)
        dot = jnp.sum(e * dp, axis=0, keepdims=True)
        out_ref[j] = jnp.concatenate([mx, total, dot], axis=0)


def back_kernel(q_ref, g_ref, k_ref, v_ref, m_ref, f_ref, dq_ref, dk_ref, dv_ref):
    m = m_ref[...] > 0
    for j in range(STEP_HEADS):
        cols = head_cols(j)
        q = q_ref[:, cols]
        g = g_ref[:, cols]
        k = k_ref[:, cols]
        s, dp = slot_scores(q, g, k, v_ref[:, cols])
        fin = f_ref[j]
        p = jnp.where(m, jnp.exp(s - fin[0:1]), 0.0)
        ds = (p * (dp - fin[1:2])).astype(jnp.bfloat16)
        dk_ref[:, cols] = jnp.dot(ds, q, preferred_element_type=jnp.float32) * SCALE
        dv_ref[:, cols] = jnp.dot(p.astype(jnp.bfloat16), g, preferred_element_type=jnp.float32)
        dq = lax.dot_general(ds, k, (((0,), (0,)), ((), ())), preferred_element_type=jnp.float32)
        dq_ref[:, cols] = (dq * SCALE).astype(dq_ref.dtype)


def slot_specs(q_rows, g_rows, nk, tok):
    cols = STEP_HEADS * HDIM
    return [
        pl.BlockSpec((tok, cols), lambda h: (q_rows, h)),
        pl.BlockSpec((tok, cols), lambda h: (g_rows, h)),
        pl.BlockSpec((nk, cols), lambda h: (0, h)),
        pl.BlockSpec((nk, cols), lambda h: (0, h)),
        pl.BlockSpec((nk, tok), lambda h: (0, 0)),
    ]


def slot_stats(q_arr, g_arr, q_rows, g_rows, key_arr, value_arr, mask_t, tok):
    nk = key_arr.shape[0]
    flops = 4 * tok * nk * HDIM * HEADS
    return pl.pallas_call(
        stats_kernel,
        grid=(HEADS // STEP_HEADS,),
        in_specs=slot_specs(q_rows, g_rows, nk, tok),
        out_specs=pl.BlockSpec((STEP_HEADS, 3, tok), lambda h: (h, 0, 0)),
        out_shape=jax.ShapeDtypeStruct((HEADS, 3, tok), jnp.float32),
        cost_estimate=pl.CostEstimate(
            flops=flops, transcendentals=tok * nk * HEADS, bytes_accessed=4 * (tok + nk) * HDIM * HEADS
        ),
    )(q_arr, g_arr, key_arr, value_arr, mask_t)


def slot_back(q_arr, g_arr, q_rows, g_rows, key_arr, value_arr, mask_t, fin, tok, dq_type):
    nk = key_arr.shape[0]
    width = HEADS * HDIM
    flops = 10 * tok * nk * HDIM * HEADS
    return pl.pallas_call(
        back_kernel,
        grid=(HEADS // STEP_HEADS,),
        in_specs=slot_specs(q_rows, g_rows, nk, tok)
        + [pl.BlockSpec((STEP_HEADS, 2, tok), lambda h: (h, 0, 0))],
        out_specs=[
            pl.BlockSpec((tok, STEP_HEADS * HDIM), lambda h: (0, h)),
            pl.BlockSpec((nk, STEP_HEADS * HDIM), lambda h: (0, h)),
            pl.BlockSpec((nk, STEP_HEADS * HDIM), lambda h: (0, h)),
        ],
        out_shape=[
            jax.ShapeDtypeStruct((tok, width), dq_type),
            jax.ShapeDtypeStruct((nk, width), jnp.float32),
            jax.ShapeDtypeStruct((nk, width), jnp.float32),
        ],
        cost_estimate=pl.CostEstimate(
            flops=flops, transcendentals=tok * nk * HEADS, bytes_accessed=12 * (tok + nk) * HDIM * HEADS
        ),
    )(q_arr, g_arr, key_arr, value_arr, mask_t, fin)


def local(queries, keys, values, grad_out, block_list):
    groups = lax.axis_size("tm")
    here = lax.axis_index("tm")
    even = here % 2 == 0
    up = jnp.where(even, 1, -1)
    tok, width = queries.shape
    blocks = FRAMES * BANDS
    cands = block_list.shape[1]

    flags = (block_list > 0).astype(jnp.bfloat16).reshape(1, blocks * cands)
    flags = jnp.pad(flags, ((0, LIST_ROWS - 1), (0, width - blocks * cands)))
    pack = jnp.concatenate([queries, grad_out, flags], axis=0)

    far_data = down_even(pack)
    near_data = up_even(pack)
    partner_keys, partner_values = swap_cores((keys, values))
    key_both = jnp.concatenate([keys, partner_keys], axis=0)
    value_both = jnp.concatenate([values, partner_values], axis=0)

    slots = {
        "own": (queries, grad_out, 0, 0, block_list, 0, True, (0, -1), (0, 1)),
        "far": (far_data, far_data, 0, 1, None, 2 * up, True, (2, 1), (-2, -1)),
        "near": (near_data, near_data, 0, 1, None, -2 * up, False, (-2,), (2,)),
    }

    args = {}
    stats_out = {}
    for name, (q_arr, g_arr, q_rows, g_rows, rows, q_off, both, offs_e, offs_o) in slots.items():
        if rows is None:
            rows = q_arr[2 * tok, : blocks * cands].reshape(blocks, cands)
        key_arr, value_arr = (key_both, value_both) if both else (keys, values)
        nkb = key_arr.shape[0] // BLOCK
        source = here + q_off
        valid = (source >= 0) & (source < groups)
        table, own = parity_tables(even, offs_e, offs_o)
        chosen = jnp.einsum("qc,qck->qk", (rows > 0).astype(jnp.float32), table) > 0
        mask4 = (chosen & valid) | own
        mask_t = jnp.broadcast_to(
            mask4.T[:, None, :, None], (nkb, BLOCK, blocks, BLOCK)
        ).reshape(nkb * BLOCK, tok).astype(jnp.float32)
        args[name] = (q_arr, g_arr, q_rows, g_rows, key_arr, value_arr, mask_t)
        stats_out[name] = slot_stats(*args[name], tok)

    stats_in = [
        (stats_out["own"], 0),
        (up_even(stats_out["far"]), -2 * up),
        (down_even(stats_out["near"]), 2 * up),
    ]
    maxes, sums, dots = [], [], []
    for stats, offset in stats_in:
        source = here + offset
        valid = (source >= 0) & (source < groups)
        maxes.append(jnp.where(valid, stats[:, 0], NEG))
        sums.append(jnp.where(valid, stats[:, 1], 0.0))
        dots.append(jnp.where(valid, stats[:, 2], 0.0))
    maxes, sums, dots = jnp.stack(maxes), jnp.stack(sums), jnp.stack(dots)
    top = jnp.max(maxes, axis=0)
    scale = jnp.exp(maxes - top[None])
    total = jnp.sum(sums * scale, axis=0)
    log_total = top + jnp.log(total)
    deltas = jnp.sum(dots * scale, axis=0) / total
    final = jnp.stack([log_total, deltas], axis=1)
    finals = {"far": down_even(final), "near": up_even(final)}

    own_q, own_k, own_v = slot_back(*args["own"], final, tok, jnp.float32)
    far_fin, near_fin, own_k, own_v = lax.optimization_barrier(
        (finals["far"], finals["near"], own_k, own_v)
    )
    finals = {"far": far_fin, "near": near_fin}
    far_q, far_k, far_v = slot_back(*args["far"], finals["far"], tok, jnp.bfloat16)
    near_q, near_k, near_v = slot_back(*args["near"], finals["near"], tok, jnp.bfloat16)
    from_far = up_even(far_q)
    from_near = down_even(near_q)

    back_kg, back_vg = swap_cores((far_k[tok:] + own_k[tok:], far_v[tok:] + own_v[tok:]))
    key_grad = far_k[:tok] + own_k[:tok] + near_k + back_kg
    value_grad = far_v[:tok] + own_v[:tok] + near_v + back_vg
    query_grad = own_q + from_far.astype(jnp.float32) + from_near.astype(jnp.float32)
    return (
        query_grad.astype(jnp.bfloat16),
        key_grad.astype(jnp.bfloat16),
        value_grad.astype(jnp.bfloat16),
    )


def solution(mesh):
    placed = (
        P(("group", "tm"), None),
        P(("group", "tm"), None),
        P(("group", "tm"), None),
        P(("group", "tm"), None),
        P(("group", "tm"), None),
    )
    return jax.shard_map(
        local,
        mesh=mesh,
        in_specs=placed,
        out_specs=(P(("group", "tm"), None), P(("group", "tm"), None), P(("group", "tm"), None)),
        check_vma=False,
    )
```

```python
import jax
import jax.numpy as jnp
import numpy as np
from jax import lax
from jax.experimental import pallas as pl
from jax.experimental.pallas import tpu as pltpu
from jax.sharding import PartitionSpec as P

HEADS = 12
HDIM = 128
BLOCK = 64
REACH = 2
FRAMES = 2
BANDS = 2
NEG = -1e30
LIST_ROWS = 16


def permute(value, rule):
    count = lax.axis_size("tm")
    pairs = []
    for source in range(count):
        target = rule(source)
        if 0 <= target < count:
            pairs.append((source, target))
    return lax.ppermute(value, "tm", pairs)


def swap_cores(value):
    return permute(value, lambda s: s ^ 1)


def down_even(value):
    return permute(value, lambda s: s - 2 if s % 2 == 0 else s + 2)


def up_even(value):
    return permute(value, lambda s: s + 2 if s % 2 == 0 else s - 2)


def pick_table(offset):
    blocks = FRAMES * BANDS
    slot = REACH - offset
    table = np.zeros((blocks, 30, blocks), np.float32)
    own = np.zeros((blocks, blocks), bool)
    if abs(offset) <= REACH:
        for qb in range(blocks):
            for kb in range(blocks):
                cand = (slot * FRAMES + kb // BANDS) * 3 + kb % BANDS - qb % BANDS + 1
                table[qb, cand, kb] = 1.0
                own[qb, kb] = offset == 0 and qb == kb
    return table, own


def parity_tables(even, even_offsets, odd_offsets):
    tables, owns = [], []
    for off_e, off_o in zip(even_offsets, odd_offsets):
        t_e, o_e = pick_table(off_e)
        t_o, o_o = pick_table(off_o)
        tables.append(jnp.where(even, jnp.asarray(t_e), jnp.asarray(t_o)))
        owns.append(jnp.where(even, jnp.asarray(o_e), jnp.asarray(o_o)))
    return jnp.concatenate(tables, axis=2), jnp.concatenate(owns, axis=1)


SCALE = HDIM ** (-0.5)
NT = (((1,), (1,)), ((), ()))
STEP_HEADS = 6


def slot_scores(q, g, k, v):
    s = lax.dot_general(k, q, NT, preferred_element_type=jnp.float32) * SCALE
    dp = lax.dot_general(v, g, NT, preferred_element_type=jnp.float32)
    return s, dp


def head_cols(j):
    return slice(j * HDIM, (j + 1) * HDIM)


def stats_kernel(q_ref, g_ref, k_ref, v_ref, m_ref, out_ref):
    m = m_ref[...] > 0
    for j in range(STEP_HEADS):
        cols = head_cols(j)
        s, dp = slot_scores(q_ref[:, cols], g_ref[:, cols], k_ref[:, cols], v_ref[:, cols])
        masked = jnp.where(m, s, NEG)
        mx = jnp.max(masked, axis=0, keepdims=True)
        e = jnp.where(m, jnp.exp(masked - mx), 0.0)
        total = jnp.sum(e, axis=0, keepdims=True)
        dot = jnp.sum(e * dp, axis=0, keepdims=True)
        out_ref[j] = jnp.concatenate([mx, total, dot], axis=0)


def back_kernel(q_ref, g_ref, k_ref, v_ref, m_ref, f_ref, dq_ref, dk_ref, dv_ref):
    m = m_ref[...] > 0
    for j in range(STEP_HEADS):
        cols = head_cols(j)
        q = q_ref[:, cols]
        g = g_ref[:, cols]
        k = k_ref[:, cols]
        s, dp = slot_scores(q, g, k, v_ref[:, cols])
        fin = f_ref[j]
        p = jnp.where(m, jnp.exp(s - fin[0:1]), 0.0)
        ds = (p * (dp - fin[1:2])).astype(jnp.bfloat16)
        dk_ref[:, cols] = jnp.dot(ds, q, preferred_element_type=jnp.float32) * SCALE
        dv_ref[:, cols] = jnp.dot(p.astype(jnp.bfloat16), g, preferred_element_type=jnp.float32)
        dq = lax.dot_general(ds, k, (((0,), (0,)), ((), ())), preferred_element_type=jnp.float32)
        dq_ref[:, cols] = (dq * SCALE).astype(dq_ref.dtype)


def slot_specs(q_rows, g_rows, nk, tok):
    cols = STEP_HEADS * HDIM
    return [
        pl.BlockSpec((tok, cols), lambda h: (q_rows, h)),
        pl.BlockSpec((tok, cols), lambda h: (g_rows, h)),
        pl.BlockSpec((nk, cols), lambda h: (0, h)),
        pl.BlockSpec((nk, cols), lambda h: (0, h)),
        pl.BlockSpec((nk, tok), lambda h: (0, 0)),
    ]


def slot_stats(q_arr, g_arr, q_rows, g_rows, key_arr, value_arr, mask_t, tok):
    nk = key_arr.shape[0]
    flops = 4 * tok * nk * HDIM * HEADS
    return pl.pallas_call(
        stats_kernel,
        grid=(HEADS // STEP_HEADS,),
        in_specs=slot_specs(q_rows, g_rows, nk, tok),
        out_specs=pl.BlockSpec((STEP_HEADS, 3, tok), lambda h: (h, 0, 0)),
        out_shape=jax.ShapeDtypeStruct((HEADS, 3, tok), jnp.float32),
        cost_estimate=pl.CostEstimate(
            flops=flops, transcendentals=tok * nk * HEADS, bytes_accessed=4 * (tok + nk) * HDIM * HEADS
        ),
    )(q_arr, g_arr, key_arr, value_arr, mask_t)


def slot_back(q_arr, g_arr, q_rows, g_rows, key_arr, value_arr, mask_t, fin, tok, dq_type):
    nk = key_arr.shape[0]
    width = HEADS * HDIM
    flops = 10 * tok * nk * HDIM * HEADS
    return pl.pallas_call(
        back_kernel,
        grid=(HEADS // STEP_HEADS,),
        in_specs=slot_specs(q_rows, g_rows, nk, tok)
        + [pl.BlockSpec((STEP_HEADS, 2, tok), lambda h: (h, 0, 0))],
        out_specs=[
            pl.BlockSpec((tok, STEP_HEADS * HDIM), lambda h: (0, h)),
            pl.BlockSpec((nk, STEP_HEADS * HDIM), lambda h: (0, h)),
            pl.BlockSpec((nk, STEP_HEADS * HDIM), lambda h: (0, h)),
        ],
        out_shape=[
            jax.ShapeDtypeStruct((tok, width), dq_type),
            jax.ShapeDtypeStruct((nk, width), jnp.float32),
            jax.ShapeDtypeStruct((nk, width), jnp.float32),
        ],
        cost_estimate=pl.CostEstimate(
            flops=flops, transcendentals=tok * nk * HEADS, bytes_accessed=12 * (tok + nk) * HDIM * HEADS
        ),
    )(q_arr, g_arr, key_arr, value_arr, mask_t, fin)


def local(queries, keys, values, grad_out, block_list):
    groups = lax.axis_size("tm")
    here = lax.axis_index("tm")
    even = here % 2 == 0
    up = jnp.where(even, 1, -1)
    tok, width = queries.shape
    blocks = FRAMES * BANDS
    cands = block_list.shape[1]

    flags = (block_list > 0).astype(jnp.bfloat16).reshape(1, blocks * cands)
    flags = jnp.pad(flags, ((0, LIST_ROWS - 1), (0, width - blocks * cands)))
    pack = jnp.concatenate([queries, grad_out, flags], axis=0)

    far_data = down_even(pack)
    near_data = up_even(pack)
    partner_keys, partner_values = swap_cores((keys, values))
    key_both = jnp.concatenate([keys, partner_keys], axis=0)
    value_both = jnp.concatenate([values, partner_values], axis=0)

    slots = {
        "own": (queries, grad_out, 0, 0, block_list, 0, True, (0, -1), (0, 1)),
        "far": (far_data, far_data, 0, 1, None, 2 * up, True, (2, 1), (-2, -1)),
        "near": (near_data, near_data, 0, 1, None, -2 * up, False, (-2,), (2,)),
    }

    args = {}
    stats_out = {}
    for name, (q_arr, g_arr, q_rows, g_rows, rows, q_off, both, offs_e, offs_o) in slots.items():
        if rows is None:
            rows = q_arr[2 * tok, : blocks * cands].reshape(blocks, cands)
        key_arr, value_arr = (key_both, value_both) if both else (keys, values)
        nkb = key_arr.shape[0] // BLOCK
        source = here + q_off
        valid = (source >= 0) & (source < groups)
        table, own = parity_tables(even, offs_e, offs_o)
        chosen = jnp.einsum("qc,qck->qk", (rows > 0).astype(jnp.float32), table) > 0
        mask4 = (chosen & valid) | own
        mask_t = jnp.broadcast_to(
            mask4.T[:, None, :, None], (nkb, BLOCK, blocks, BLOCK)
        ).reshape(nkb * BLOCK, tok).astype(jnp.float32)
        args[name] = (q_arr, g_arr, q_rows, g_rows, key_arr, value_arr, mask_t)
        stats_out[name] = slot_stats(*args[name], tok)

    stats_in = [
        (stats_out["own"], 0),
        (up_even(stats_out["far"]), -2 * up),
        (down_even(stats_out["near"]), 2 * up),
    ]
    maxes, sums, dots = [], [], []
    for stats, offset in stats_in:
        source = here + offset
        valid = (source >= 0) & (source < groups)
        maxes.append(jnp.where(valid, stats[:, 0], NEG))
        sums.append(jnp.where(valid, stats[:, 1], 0.0))
        dots.append(jnp.where(valid, stats[:, 2], 0.0))
    maxes, sums, dots = jnp.stack(maxes), jnp.stack(sums), jnp.stack(dots)
    top = jnp.max(maxes, axis=0)
    scale = jnp.exp(maxes - top[None])
    total = jnp.sum(sums * scale, axis=0)
    log_total = top + jnp.log(total)
    deltas = jnp.sum(dots * scale, axis=0) / total
    final = jnp.stack([log_total, deltas], axis=1)
    finals = {"far": down_even(final), "near": up_even(final)}

    own_q, own_k, own_v = slot_back(*args["own"], final, tok, jnp.float32)
    far_fin, near_fin, own_k, own_v = lax.optimization_barrier(
        (finals["far"], finals["near"], own_k, own_v)
    )
    finals = {"far": far_fin, "near": near_fin}
    far_q, far_k, far_v = slot_back(*args["far"], finals["far"], tok, jnp.bfloat16)
    near_q, near_k, near_v = slot_back(*args["near"], finals["near"], tok, jnp.bfloat16)
    from_far = up_even(far_q)
    from_near = down_even(near_q)

    back_kg, back_vg = swap_cores((far_k[tok:] + own_k[tok:], far_v[tok:] + own_v[tok:]))
    key_grad = far_k[:tok] + own_k[:tok] + near_k + back_kg
    value_grad = far_v[:tok] + own_v[:tok] + near_v + back_vg
    query_grad = own_q + from_far.astype(jnp.float32) + from_near.astype(jnp.float32)
    return (
        query_grad.astype(jnp.bfloat16),
        key_grad.astype(jnp.bfloat16),
        value_grad.astype(jnp.bfloat16),
    )


def solution(mesh):
    placed = (
        P(("group", "tm"), None),
        P(("group", "tm"), None),
        P(("group", "tm"), None),
        P(("group", "tm"), None),
        P(("group", "tm"), None),
    )
    return jax.shard_map(
        local,
        mesh=mesh,
        in_specs=placed,
        out_specs=(P(("group", "tm"), None), P(("group", "tm"), None), P(("group", "tm"), None)),
        check_vma=False,
    )
```

```python
import jax
import jax.numpy as jnp
import numpy as np
from jax import lax
from jax.experimental import pallas as pl
from jax.experimental.pallas import tpu as pltpu
from jax.sharding import PartitionSpec as P

HEADS = 12
HDIM = 128
BLOCK = 64
REACH = 2
FRAMES = 2
BANDS = 2
NEG = -1e30
LIST_ROWS = 16


def permute(value, rule):
    count = lax.axis_size("tm")
    pairs = []
    for source in range(count):
        target = rule(source)
        if 0 <= target < count:
            pairs.append((source, target))
    return lax.ppermute(value, "tm", pairs)


def swap_cores(value):
    return permute(value, lambda s: s ^ 1)


def down_even(value):
    return permute(value, lambda s: s - 2 if s % 2 == 0 else s + 2)


def up_even(value):
    return permute(value, lambda s: s + 2 if s % 2 == 0 else s - 2)


def pick_table(offset):
    blocks = FRAMES * BANDS
    slot = REACH - offset
    table = np.zeros((blocks, 30, blocks), np.float32)
    own = np.zeros((blocks, blocks), bool)
    if abs(offset) <= REACH:
        for qb in range(blocks):
            for kb in range(blocks):
                cand = (slot * FRAMES + kb // BANDS) * 3 + kb % BANDS - qb % BANDS + 1
                table[qb, cand, kb] = 1.0
                own[qb, kb] = offset == 0 and qb == kb
    return table, own


def parity_tables(even, even_offsets, odd_offsets):
    tables, owns = [], []
    for off_e, off_o in zip(even_offsets, odd_offsets):
        t_e, o_e = pick_table(off_e)
        t_o, o_o = pick_table(off_o)
        tables.append(jnp.where(even, jnp.asarray(t_e), jnp.asarray(t_o)))
        owns.append(jnp.where(even, jnp.asarray(o_e), jnp.asarray(o_o)))
    return jnp.concatenate(tables, axis=2), jnp.concatenate(owns, axis=1)


SCALE = HDIM ** (-0.5)
NT = (((1,), (1,)), ((), ()))
STEP_HEADS = 4


def slot_scores(q, g, k, v):
    s = lax.dot_general(k, q, NT, preferred_element_type=jnp.float32) * SCALE
    dp = lax.dot_general(v, g, NT, preferred_element_type=jnp.float32)
    return s, dp


def head_cols(j):
    return slice(j * HDIM, (j + 1) * HDIM)


def stats_kernel(q_ref, g_ref, k_ref, v_ref, m_ref, out_ref):
    m = m_ref[...] > 0
    for j in range(STEP_HEADS):
        cols = head_cols(j)
        s, dp = slot_scores(q_ref[:, cols], g_ref[:, cols], k_ref[:, cols], v_ref[:, cols])
        masked = jnp.where(m, s, NEG)
        mx = jnp.max(masked, axis=0, keepdims=True)
        e = jnp.where(m, jnp.exp(masked - mx), 0.0)
        total = jnp.sum(e, axis=0, keepdims=True)
        dot = jnp.sum(e * dp, axis=0, keepdims=True)
        out_ref[j] = jnp.concatenate([mx, total, dot], axis=0)


def back_kernel(q_ref, g_ref, k_ref, v_ref, m_ref, f_ref, dq_ref, dk_ref, dv_ref):
    m = m_ref[...] > 0
    for j in range(STEP_HEADS):
        cols = head_cols(j)
        q = q_ref[:, cols]
        g = g_ref[:, cols]
        k = k_ref[:, cols]
        s, dp = slot_scores(q, g, k, v_ref[:, cols])
        fin = f_ref[j]
        p = jnp.where(m, jnp.exp(s - fin[0:1]), 0.0)
        ds = (p * (dp - fin[1:2])).astype(jnp.bfloat16)
        dk_ref[:, cols] = jnp.dot(ds, q, preferred_element_type=jnp.float32) * SCALE
        dv_ref[:, cols] = jnp.dot(p.astype(jnp.bfloat16), g, preferred_element_type=jnp.float32)
        dq = lax.dot_general(ds, k, (((0,), (0,)), ((), ())), preferred_element_type=jnp.float32)
        dq_ref[:, cols] = (dq * SCALE).astype(dq_ref.dtype)


def slot_specs(q_rows, g_rows, nk, tok):
    cols = STEP_HEADS * HDIM
    return [
        pl.BlockSpec((tok, cols), lambda h: (q_rows, h)),
        pl.BlockSpec((tok, cols), lambda h: (g_rows, h)),
        pl.BlockSpec((nk, cols), lambda h: (0, h)),
        pl.BlockSpec((nk, cols), lambda h: (0, h)),
        pl.BlockSpec((nk, tok), lambda h: (0, 0)),
    ]


def slot_stats(q_arr, g_arr, q_rows, g_rows, key_arr, value_arr, mask_t, tok):
    nk = key_arr.shape[0]
    flops = 4 * tok * nk * HDIM * HEADS
    return pl.pallas_call(
        stats_kernel,
        grid=(HEADS // STEP_HEADS,),
        in_specs=slot_specs(q_rows, g_rows, nk, tok),
        out_specs=pl.BlockSpec((STEP_HEADS, 3, tok), lambda h: (h, 0, 0)),
        out_shape=jax.ShapeDtypeStruct((HEADS, 3, tok), jnp.float32),
        cost_estimate=pl.CostEstimate(
            flops=flops, transcendentals=tok * nk * HEADS, bytes_accessed=4 * (tok + nk) * HDIM * HEADS
        ),
    )(q_arr, g_arr, key_arr, value_arr, mask_t)


def slot_back(q_arr, g_arr, q_rows, g_rows, key_arr, value_arr, mask_t, fin, tok, dq_type):
    nk = key_arr.shape[0]
    width = HEADS * HDIM
    flops = 10 * tok * nk * HDIM * HEADS
    return pl.pallas_call(
        back_kernel,
        grid=(HEADS // STEP_HEADS,),
        in_specs=slot_specs(q_rows, g_rows, nk, tok)
        + [pl.BlockSpec((STEP_HEADS, 2, tok), lambda h: (h, 0, 0))],
        out_specs=[
            pl.BlockSpec((tok, STEP_HEADS * HDIM), lambda h: (0, h)),
            pl.BlockSpec((nk, STEP_HEADS * HDIM), lambda h: (0, h)),
            pl.BlockSpec((nk, STEP_HEADS * HDIM), lambda h: (0, h)),
        ],
        out_shape=[
            jax.ShapeDtypeStruct((tok, width), dq_type),
            jax.ShapeDtypeStruct((nk, width), jnp.float32),
            jax.ShapeDtypeStruct((nk, width), jnp.float32),
        ],
        cost_estimate=pl.CostEstimate(
            flops=flops, transcendentals=tok * nk * HEADS, bytes_accessed=12 * (tok + nk) * HDIM * HEADS
        ),
    )(q_arr, g_arr, key_arr, value_arr, mask_t, fin)


def local(queries, keys, values, grad_out, block_list):
    groups = lax.axis_size("tm")
    here = lax.axis_index("tm")
    even = here % 2 == 0
    up = jnp.where(even, 1, -1)
    tok, width = queries.shape
    blocks = FRAMES * BANDS
    cands = block_list.shape[1]

    flags = (block_list > 0).astype(jnp.bfloat16).reshape(1, blocks * cands)
    flags = jnp.pad(flags, ((0, LIST_ROWS - 1), (0, width - blocks * cands)))
    pack = jnp.concatenate([queries, grad_out, flags], axis=0)

    far_data = down_even(pack)
    near_data = up_even(pack)
    partner_keys, partner_values = swap_cores((keys, values))
    key_both = jnp.concatenate([keys, partner_keys], axis=0)
    value_both = jnp.concatenate([values, partner_values], axis=0)

    slots = {
        "own": (queries, grad_out, 0, 0, block_list, 0, True, (0, -1), (0, 1)),
        "far": (far_data, far_data, 0, 1, None, 2 * up, True, (2, 1), (-2, -1)),
        "near": (near_data, near_data, 0, 1, None, -2 * up, False, (-2,), (2,)),
    }

    args = {}
    stats_out = {}
    for name, (q_arr, g_arr, q_rows, g_rows, rows, q_off, both, offs_e, offs_o) in slots.items():
        if rows is None:
            rows = q_arr[2 * tok, : blocks * cands].reshape(blocks, cands)
        key_arr, value_arr = (key_both, value_both) if both else (keys, values)
        nkb = key_arr.shape[0] // BLOCK
        source = here + q_off
        valid = (source >= 0) & (source < groups)
        table, own = parity_tables(even, offs_e, offs_o)
        chosen = jnp.einsum("qc,qck->qk", (rows > 0).astype(jnp.float32), table) > 0
        mask4 = (chosen & valid) | own
        mask_t = jnp.broadcast_to(
            mask4.T[:, None, :, None], (nkb, BLOCK, blocks, BLOCK)
        ).reshape(nkb * BLOCK, tok).astype(jnp.float32)
        args[name] = (q_arr, g_arr, q_rows, g_rows, key_arr, value_arr, mask_t)
        stats_out[name] = slot_stats(*args[name], tok)

    stats_in = [
        (stats_out["own"], 0),
        (up_even(stats_out["far"]), -2 * up),
        (down_even(stats_out["near"]), 2 * up),
    ]
    maxes, sums, dots = [], [], []
    for stats, offset in stats_in:
        source = here + offset
        valid = (source >= 0) & (source < groups)
        maxes.append(jnp.where(valid, stats[:, 0], NEG))
        sums.append(jnp.where(valid, stats[:, 1], 0.0))
        dots.append(jnp.where(valid, stats[:, 2], 0.0))
    maxes, sums, dots = jnp.stack(maxes), jnp.stack(sums), jnp.stack(dots)
    top = jnp.max(maxes, axis=0)
    scale = jnp.exp(maxes - top[None])
    total = jnp.sum(sums * scale, axis=0)
    log_total = top + jnp.log(total)
    deltas = jnp.sum(dots * scale, axis=0) / total
    final = jnp.stack([log_total, deltas], axis=1)
    finals = {"far": down_even(final), "near": up_even(final)}

    own_q, own_k, own_v = slot_back(*args["own"], final, tok, jnp.float32)
    far_fin, near_fin, own_k, own_v = lax.optimization_barrier(
        (finals["far"], finals["near"], own_k, own_v)
    )
    finals = {"far": far_fin, "near": near_fin}
    far_q, far_k, far_v = slot_back(*args["far"], finals["far"], tok, jnp.bfloat16)
    near_q, near_k, near_v = slot_back(*args["near"], finals["near"], tok, jnp.bfloat16)
    from_far = up_even(far_q)
    from_near = down_even(near_q)

    back_kg, back_vg = swap_cores((far_k[tok:] + own_k[tok:], far_v[tok:] + own_v[tok:]))
    key_grad = (far_k[:tok] + own_k[:tok] + near_k + back_kg).astype(jnp.bfloat16)
    value_grad = (far_v[:tok] + own_v[:tok] + near_v + back_vg).astype(jnp.bfloat16)
    from_far, from_near, key_grad, value_grad = lax.optimization_barrier(
        (from_far, from_near, key_grad, value_grad)
    )
    query_grad = own_q + from_far.astype(jnp.float32) + from_near.astype(jnp.float32)
    return query_grad.astype(jnp.bfloat16), key_grad, value_grad


def solution(mesh):
    placed = (
        P(("group", "tm"), None),
        P(("group", "tm"), None),
        P(("group", "tm"), None),
        P(("group", "tm"), None),
        P(("group", "tm"), None),
    )
    return jax.shard_map(
        local,
        mesh=mesh,
        in_specs=placed,
        out_specs=(P(("group", "tm"), None), P(("group", "tm"), None), P(("group", "tm"), None)),
        check_vma=False,
    )
```

```python
import jax
import jax.numpy as jnp
import numpy as np
from jax import lax
from jax.experimental import pallas as pl
from jax.experimental.pallas import tpu as pltpu
from jax.sharding import PartitionSpec as P

HEADS = 12
HDIM = 128
BLOCK = 64
REACH = 2
FRAMES = 2
BANDS = 2
NEG = -1e30
LIST_ROWS = 16


def permute(value, rule):
    count = lax.axis_size("tm")
    pairs = []
    for source in range(count):
        target = rule(source)
        if 0 <= target < count:
            pairs.append((source, target))
    return lax.ppermute(value, "tm", pairs)


def swap_cores(value):
    return permute(value, lambda s: s ^ 1)


def down_even(value):
    return permute(value, lambda s: s - 2 if s % 2 == 0 else s + 2)


def up_even(value):
    return permute(value, lambda s: s + 2 if s % 2 == 0 else s - 2)


def pick_table(offset):
    blocks = FRAMES * BANDS
    slot = REACH - offset
    table = np.zeros((blocks, 30, blocks), np.float32)
    own = np.zeros((blocks, blocks), bool)
    if abs(offset) <= REACH:
        for qb in range(blocks):
            for kb in range(blocks):
                cand = (slot * FRAMES + kb // BANDS) * 3 + kb % BANDS - qb % BANDS + 1
                table[qb, cand, kb] = 1.0
                own[qb, kb] = offset == 0 and qb == kb
    return table, own


def parity_tables(even, even_offsets, odd_offsets):
    tables, owns = [], []
    for off_e, off_o in zip(even_offsets, odd_offsets):
        t_e, o_e = pick_table(off_e)
        t_o, o_o = pick_table(off_o)
        tables.append(jnp.where(even, jnp.asarray(t_e), jnp.asarray(t_o)))
        owns.append(jnp.where(even, jnp.asarray(o_e), jnp.asarray(o_o)))
    return jnp.concatenate(tables, axis=2), jnp.concatenate(owns, axis=1)


SCALE = HDIM ** (-0.5)
NT = (((1,), (1,)), ((), ()))
STEP_HEADS = 4


def slot_scores(q, g, k, v):
    s = lax.dot_general(k, q, NT, preferred_element_type=jnp.float32) * SCALE
    dp = lax.dot_general(v, g, NT, preferred_element_type=jnp.float32)
    return s, dp


def head_cols(j):
    return slice(j * HDIM, (j + 1) * HDIM)


def stats_kernel(q_ref, g_ref, k_ref, v_ref, m_ref, out_ref):
    m = m_ref[...] > 0
    for j in range(STEP_HEADS):
        cols = head_cols(j)
        s, dp = slot_scores(q_ref[:, cols], g_ref[:, cols], k_ref[:, cols], v_ref[:, cols])
        masked = jnp.where(m, s, NEG)
        mx = jnp.max(masked, axis=0, keepdims=True)
        e = jnp.where(m, jnp.exp(masked - mx), 0.0)
        total = jnp.sum(e, axis=0, keepdims=True)
        dot = jnp.sum(e * dp, axis=0, keepdims=True)
        out_ref[j] = jnp.concatenate([mx, total, dot], axis=0)


def back_kernel(q_ref, g_ref, k_ref, v_ref, m_ref, f_ref, dq_ref, dk_ref, dv_ref):
    m = m_ref[...] > 0
    for j in range(STEP_HEADS):
        cols = head_cols(j)
        q = q_ref[:, cols]
        g = g_ref[:, cols]
        k = k_ref[:, cols]
        s, dp = slot_scores(q, g, k, v_ref[:, cols])
        fin = f_ref[j]
        p = jnp.where(m, jnp.exp(s - fin[0:1]), 0.0)
        ds = (p * (dp - fin[1:2])).astype(jnp.bfloat16)
        dk_ref[:, cols] = jnp.dot(ds, q, preferred_element_type=jnp.float32) * SCALE
        dv_ref[:, cols] = jnp.dot(p.astype(jnp.bfloat16), g, preferred_element_type=jnp.float32)
        dq = lax.dot_general(ds, k, (((0,), (0,)), ((), ())), preferred_element_type=jnp.float32)
        dq_ref[:, cols] = (dq * SCALE).astype(dq_ref.dtype)


def slot_specs(q_rows, g_rows, nk, tok):
    cols = STEP_HEADS * HDIM
    return [
        pl.BlockSpec((tok, cols), lambda h: (q_rows, h)),
        pl.BlockSpec((tok, cols), lambda h: (g_rows, h)),
        pl.BlockSpec((nk, cols), lambda h: (0, h)),
        pl.BlockSpec((nk, cols), lambda h: (0, h)),
        pl.BlockSpec((nk, tok), lambda h: (0, 0)),
    ]


def slot_stats(q_arr, g_arr, q_rows, g_rows, key_arr, value_arr, mask_t, tok):
    nk = key_arr.shape[0]
    flops = 4 * tok * nk * HDIM * HEADS
    return pl.pallas_call(
        stats_kernel,
        grid=(HEADS // STEP_HEADS,),
        in_specs=slot_specs(q_rows, g_rows, nk, tok),
        out_specs=pl.BlockSpec((STEP_HEADS, 3, tok), lambda h: (h, 0, 0)),
        out_shape=jax.ShapeDtypeStruct((HEADS, 3, tok), jnp.float32),
        cost_estimate=pl.CostEstimate(
            flops=flops, transcendentals=tok * nk * HEADS, bytes_accessed=4 * (tok + nk) * HDIM * HEADS
        ),
    )(q_arr, g_arr, key_arr, value_arr, mask_t)


def slot_back(q_arr, g_arr, q_rows, g_rows, key_arr, value_arr, mask_t, fin, tok, dq_type):
    nk = key_arr.shape[0]
    width = HEADS * HDIM
    flops = 10 * tok * nk * HDIM * HEADS
    return pl.pallas_call(
        back_kernel,
        grid=(HEADS // STEP_HEADS,),
        in_specs=slot_specs(q_rows, g_rows, nk, tok)
        + [pl.BlockSpec((STEP_HEADS, 2, tok), lambda h: (h, 0, 0))],
        out_specs=[
            pl.BlockSpec((tok, STEP_HEADS * HDIM), lambda h: (0, h)),
            pl.BlockSpec((nk, STEP_HEADS * HDIM), lambda h: (0, h)),
            pl.BlockSpec((nk, STEP_HEADS * HDIM), lambda h: (0, h)),
        ],
        out_shape=[
            jax.ShapeDtypeStruct((tok, width), dq_type),
            jax.ShapeDtypeStruct((nk, width), jnp.float32),
            jax.ShapeDtypeStruct((nk, width), jnp.float32),
        ],
        cost_estimate=pl.CostEstimate(
            flops=flops, transcendentals=tok * nk * HEADS, bytes_accessed=12 * (tok + nk) * HDIM * HEADS
        ),
    )(q_arr, g_arr, key_arr, value_arr, mask_t, fin)


def local(queries, keys, values, grad_out, block_list):
    groups = lax.axis_size("tm")
    here = lax.axis_index("tm")
    even = here % 2 == 0
    up = jnp.where(even, 1, -1)
    tok, width = queries.shape
    blocks = FRAMES * BANDS
    cands = block_list.shape[1]

    flags = (block_list > 0).astype(jnp.bfloat16).reshape(1, blocks * cands)
    flags = jnp.pad(flags, ((0, LIST_ROWS - 1), (0, width - blocks * cands)))
    pack = jnp.concatenate([queries, grad_out, flags], axis=0)

    far_data = down_even(pack)
    near_data = up_even(pack)
    partner_keys, partner_values = swap_cores((keys, values))
    key_both = jnp.concatenate([keys, partner_keys], axis=0)
    value_both = jnp.concatenate([values, partner_values], axis=0)

    slots = {
        "own": (queries, grad_out, 0, 0, block_list, 0, True, (0, -1), (0, 1)),
        "far": (far_data, far_data, 0, 1, None, 2 * up, True, (2, 1), (-2, -1)),
        "near": (near_data, near_data, 0, 1, None, -2 * up, False, (-2,), (2,)),
    }

    args = {}
    stats_out = {}
    for name, (q_arr, g_arr, q_rows, g_rows, rows, q_off, both, offs_e, offs_o) in slots.items():
        if rows is None:
            rows = q_arr[2 * tok, : blocks * cands].reshape(blocks, cands)
        key_arr, value_arr = (key_both, value_both) if both else (keys, values)
        nkb = key_arr.shape[0] // BLOCK
        source = here + q_off
        valid = (source >= 0) & (source < groups)
        table, own = parity_tables(even, offs_e, offs_o)
        chosen = jnp.einsum("qc,qck->qk", (rows > 0).astype(jnp.float32), table) > 0
        mask4 = (chosen & valid) | own
        mask_t = jnp.broadcast_to(
            mask4.T[:, None, :, None], (nkb, BLOCK, blocks, BLOCK)
        ).reshape(nkb * BLOCK, tok).astype(jnp.float32)
        args[name] = (q_arr, g_arr, q_rows, g_rows, key_arr, value_arr, mask_t)
        stats_out[name] = slot_stats(*args[name], tok)

    stats_in = [
        (stats_out["own"], 0),
        (up_even(stats_out["far"]), -2 * up),
        (down_even(stats_out["near"]), 2 * up),
    ]
    maxes, sums, dots = [], [], []
    for stats, offset in stats_in:
        source = here + offset
        valid = (source >= 0) & (source < groups)
        maxes.append(jnp.where(valid, stats[:, 0], NEG))
        sums.append(jnp.where(valid, stats[:, 1], 0.0))
        dots.append(jnp.where(valid, stats[:, 2], 0.0))
    maxes, sums, dots = jnp.stack(maxes), jnp.stack(sums), jnp.stack(dots)
    top = jnp.max(maxes, axis=0)
    scale = jnp.exp(maxes - top[None])
    total = jnp.sum(sums * scale, axis=0)
    log_total = top + jnp.log(total)
    deltas = jnp.sum(dots * scale, axis=0) / total
    final = jnp.stack([log_total, deltas], axis=1)
    finals = {"far": down_even(final), "near": up_even(final)}

    own_q, own_k, own_v = slot_back(*args["own"], final, tok, jnp.float32)
    far_fin, near_fin, own_k, own_v = lax.optimization_barrier(
        (finals["far"], finals["near"], own_k, own_v)
    )
    finals = {"far": far_fin, "near": near_fin}
    far_q, far_k, far_v = slot_back(*args["far"], finals["far"], tok, jnp.bfloat16)
    near_q, near_k, near_v = slot_back(*args["near"], finals["near"], tok, jnp.bfloat16)
    from_far = up_even(far_q)
    from_near = down_even(near_q)

    def low(x):
        return x.astype(jnp.bfloat16).astype(jnp.float32)

    back_kg, back_vg = swap_cores(
        (low(far_k[tok:]) + low(own_k[tok:]), low(far_v[tok:]) + low(own_v[tok:]))
    )
    key_grad = (low(far_k[:tok]) + low(own_k[:tok]) + low(near_k) + back_kg).astype(jnp.bfloat16)
    value_grad = (low(far_v[:tok]) + low(own_v[:tok]) + low(near_v) + back_vg).astype(jnp.bfloat16)
    from_far, from_near, key_grad, value_grad = lax.optimization_barrier(
        (from_far, from_near, key_grad, value_grad)
    )
    query_grad = own_q + from_far.astype(jnp.float32) + from_near.astype(jnp.float32)
    return query_grad.astype(jnp.bfloat16), key_grad, value_grad


def solution(mesh):
    placed = (
        P(("group", "tm"), None),
        P(("group", "tm"), None),
        P(("group", "tm"), None),
        P(("group", "tm"), None),
        P(("group", "tm"), None),
    )
    return jax.shard_map(
        local,
        mesh=mesh,
        in_specs=placed,
        out_specs=(P(("group", "tm"), None), P(("group", "tm"), None), P(("group", "tm"), None)),
        check_vma=False,
    )
```

```python
import jax
import jax.numpy as jnp
import numpy as np
from jax import lax
from jax.experimental import pallas as pl
from jax.experimental.pallas import tpu as pltpu
from jax.sharding import PartitionSpec as P

HEADS = 12
HDIM = 128
BLOCK = 64
REACH = 2
FRAMES = 2
BANDS = 2
NEG = -1e30
LIST_ROWS = 16


def permute(value, rule):
    count = lax.axis_size("tm")
    pairs = []
    for source in range(count):
        target = rule(source)
        if 0 <= target < count:
            pairs.append((source, target))
    return lax.ppermute(value, "tm", pairs)


def swap_cores(value):
    return permute(value, lambda s: s ^ 1)


def down_even(value):
    return permute(value, lambda s: s - 2 if s % 2 == 0 else s + 2)


def up_even(value):
    return permute(value, lambda s: s + 2 if s % 2 == 0 else s - 2)


def pick_table(offset):
    blocks = FRAMES * BANDS
    slot = REACH - offset
    table = np.zeros((blocks, 30, blocks), np.float32)
    own = np.zeros((blocks, blocks), bool)
    if abs(offset) <= REACH:
        for qb in range(blocks):
            for kb in range(blocks):
                cand = (slot * FRAMES + kb // BANDS) * 3 + kb % BANDS - qb % BANDS + 1
                table[qb, cand, kb] = 1.0
                own[qb, kb] = offset == 0 and qb == kb
    return table, own


def parity_tables(even, even_offsets, odd_offsets):
    tables, owns = [], []
    for off_e, off_o in zip(even_offsets, odd_offsets):
        t_e, o_e = pick_table(off_e)
        t_o, o_o = pick_table(off_o)
        tables.append(jnp.where(even, jnp.asarray(t_e), jnp.asarray(t_o)))
        owns.append(jnp.where(even, jnp.asarray(o_e), jnp.asarray(o_o)))
    return jnp.concatenate(tables, axis=2), jnp.concatenate(owns, axis=1)


SCALE = HDIM ** (-0.5)
NT = (((1,), (1,)), ((), ()))
STEP_HEADS = 4


def slot_scores(q, g, k, v):
    s = lax.dot_general(k, q, NT, preferred_element_type=jnp.float32) * SCALE
    dp = lax.dot_general(v, g, NT, preferred_element_type=jnp.float32)
    return s, dp


def head_cols(j):
    return slice(j * HDIM, (j + 1) * HDIM)


def stats_kernel(q_ref, g_ref, k_ref, v_ref, m_ref, out_ref):
    m = m_ref[...] > 0
    for j in range(STEP_HEADS):
        cols = head_cols(j)
        s, dp = slot_scores(q_ref[:, cols], g_ref[:, cols], k_ref[:, cols], v_ref[:, cols])
        masked = jnp.where(m, s, NEG)
        mx = jnp.max(masked, axis=0, keepdims=True)
        e = jnp.where(m, jnp.exp(masked - mx), 0.0)
        total = jnp.sum(e, axis=0, keepdims=True)
        dot = jnp.sum(e * dp, axis=0, keepdims=True)
        out_ref[j] = jnp.concatenate([mx, total, dot], axis=0)


def back_kernel(q_ref, g_ref, k_ref, v_ref, m_ref, f_ref, dq_ref, dk_ref, dv_ref):
    m = m_ref[...] > 0
    for j in range(STEP_HEADS):
        cols = head_cols(j)
        q = q_ref[:, cols]
        g = g_ref[:, cols]
        k = k_ref[:, cols]
        s, dp = slot_scores(q, g, k, v_ref[:, cols])
        fin = f_ref[j]
        p = jnp.where(m, jnp.exp(s - fin[0:1]), 0.0)
        ds = (p * (dp - fin[1:2])).astype(jnp.bfloat16)
        dk_ref[:, cols] = jnp.dot(ds, q, preferred_element_type=jnp.float32) * SCALE
        dv_ref[:, cols] = jnp.dot(p.astype(jnp.bfloat16), g, preferred_element_type=jnp.float32)
        dq = lax.dot_general(ds, k, (((0,), (0,)), ((), ())), preferred_element_type=jnp.float32)
        dq_ref[:, cols] = (dq * SCALE).astype(dq_ref.dtype)


def slot_specs(q_rows, g_rows, nk, tok):
    cols = STEP_HEADS * HDIM
    return [
        pl.BlockSpec((tok, cols), lambda h: (q_rows, h)),
        pl.BlockSpec((tok, cols), lambda h: (g_rows, h)),
        pl.BlockSpec((nk, cols), lambda h: (0, h)),
        pl.BlockSpec((nk, cols), lambda h: (0, h)),
        pl.BlockSpec((nk, tok), lambda h: (0, 0)),
    ]


def slot_stats(q_arr, g_arr, q_rows, g_rows, key_arr, value_arr, mask_t, tok):
    nk = key_arr.shape[0]
    flops = 4 * tok * nk * HDIM * HEADS
    return pl.pallas_call(
        stats_kernel,
        grid=(HEADS // STEP_HEADS,),
        in_specs=slot_specs(q_rows, g_rows, nk, tok),
        out_specs=pl.BlockSpec((STEP_HEADS, 3, tok), lambda h: (h, 0, 0)),
        out_shape=jax.ShapeDtypeStruct((HEADS, 3, tok), jnp.float32),
        cost_estimate=pl.CostEstimate(
            flops=flops, transcendentals=tok * nk * HEADS, bytes_accessed=4 * (tok + nk) * HDIM * HEADS
        ),
    )(q_arr, g_arr, key_arr, value_arr, mask_t)


def slot_back(q_arr, g_arr, q_rows, g_rows, key_arr, value_arr, mask_t, fin, tok, dq_type):
    nk = key_arr.shape[0]
    width = HEADS * HDIM
    flops = 10 * tok * nk * HDIM * HEADS
    return pl.pallas_call(
        back_kernel,
        grid=(HEADS // STEP_HEADS,),
        in_specs=slot_specs(q_rows, g_rows, nk, tok)
        + [pl.BlockSpec((STEP_HEADS, 2, tok), lambda h: (h, 0, 0))],
        out_specs=[
            pl.BlockSpec((tok, STEP_HEADS * HDIM), lambda h: (0, h)),
            pl.BlockSpec((nk, STEP_HEADS * HDIM), lambda h: (0, h)),
            pl.BlockSpec((nk, STEP_HEADS * HDIM), lambda h: (0, h)),
        ],
        out_shape=[
            jax.ShapeDtypeStruct((tok, width), dq_type),
            jax.ShapeDtypeStruct((nk, width), jnp.float32),
            jax.ShapeDtypeStruct((nk, width), jnp.float32),
        ],
        cost_estimate=pl.CostEstimate(
            flops=flops, transcendentals=tok * nk * HEADS, bytes_accessed=12 * (tok + nk) * HDIM * HEADS
        ),
    )(q_arr, g_arr, key_arr, value_arr, mask_t, fin)


def local(queries, keys, values, grad_out, block_list):
    groups = lax.axis_size("tm")
    here = lax.axis_index("tm")
    even = here % 2 == 0
    up = jnp.where(even, 1, -1)
    tok, width = queries.shape
    blocks = FRAMES * BANDS
    cands = block_list.shape[1]

    flags = (block_list > 0).astype(jnp.bfloat16).reshape(1, blocks * cands)
    flags = jnp.pad(flags, ((0, LIST_ROWS - 1), (0, width - blocks * cands)))
    far_q_data = down_even(queries)
    near_q_data = up_even(queries)
    pack = jnp.concatenate([grad_out, flags], axis=0)
    far_data = down_even(pack)
    near_data = up_even(pack)
    partner_keys, partner_values = swap_cores((keys, values))
    key_both = jnp.concatenate([keys, partner_keys], axis=0)
    value_both = jnp.concatenate([values, partner_values], axis=0)

    slots = {
        "own": (queries, grad_out, 0, 0, block_list, 0, True, (0, -1), (0, 1)),
        "far": (far_q_data, far_data, 0, 0, None, 2 * up, True, (2, 1), (-2, -1)),
        "near": (near_q_data, near_data, 0, 0, None, -2 * up, False, (-2,), (2,)),
    }

    args = {}
    stats_out = {}
    for name, (q_arr, g_arr, q_rows, g_rows, rows, q_off, both, offs_e, offs_o) in slots.items():
        if rows is None:
            rows = g_arr[tok, : blocks * cands].reshape(blocks, cands)
        key_arr, value_arr = (key_both, value_both) if both else (keys, values)
        nkb = key_arr.shape[0] // BLOCK
        source = here + q_off
        valid = (source >= 0) & (source < groups)
        table, own = parity_tables(even, offs_e, offs_o)
        chosen = jnp.einsum("qc,qck->qk", (rows > 0).astype(jnp.float32), table) > 0
        mask4 = (chosen & valid) | own
        mask_t = jnp.broadcast_to(
            mask4.T[:, None, :, None], (nkb, BLOCK, blocks, BLOCK)
        ).reshape(nkb * BLOCK, tok).astype(jnp.float32)
        args[name] = (q_arr, g_arr, q_rows, g_rows, key_arr, value_arr, mask_t)
        stats_out[name] = slot_stats(*args[name], tok)

    stats_in = [
        (stats_out["own"], 0),
        (up_even(stats_out["far"]), -2 * up),
        (down_even(stats_out["near"]), 2 * up),
    ]
    maxes, sums, dots = [], [], []
    for stats, offset in stats_in:
        source = here + offset
        valid = (source >= 0) & (source < groups)
        maxes.append(jnp.where(valid, stats[:, 0], NEG))
        sums.append(jnp.where(valid, stats[:, 1], 0.0))
        dots.append(jnp.where(valid, stats[:, 2], 0.0))
    maxes, sums, dots = jnp.stack(maxes), jnp.stack(sums), jnp.stack(dots)
    top = jnp.max(maxes, axis=0)
    scale = jnp.exp(maxes - top[None])
    total = jnp.sum(sums * scale, axis=0)
    log_total = top + jnp.log(total)
    deltas = jnp.sum(dots * scale, axis=0) / total
    final = jnp.stack([log_total, deltas], axis=1)
    finals = {"far": down_even(final), "near": up_even(final)}

    own_q, own_k, own_v = slot_back(*args["own"], final, tok, jnp.float32)
    far_fin, near_fin, own_k, own_v = lax.optimization_barrier(
        (finals["far"], finals["near"], own_k, own_v)
    )
    finals = {"far": far_fin, "near": near_fin}
    far_q, far_k, far_v = slot_back(*args["far"], finals["far"], tok, jnp.bfloat16)
    near_q, near_k, near_v = slot_back(*args["near"], finals["near"], tok, jnp.bfloat16)
    from_far = up_even(far_q)
    from_near = down_even(near_q)

    def low(x):
        return x.astype(jnp.bfloat16).astype(jnp.float32)

    back_kg, back_vg = swap_cores(
        (low(far_k[tok:]) + low(own_k[tok:]), low(far_v[tok:]) + low(own_v[tok:]))
    )
    key_grad = (low(far_k[:tok]) + low(own_k[:tok]) + low(near_k) + back_kg).astype(jnp.bfloat16)
    value_grad = (low(far_v[:tok]) + low(own_v[:tok]) + low(near_v) + back_vg).astype(jnp.bfloat16)
    from_far, from_near, key_grad, value_grad = lax.optimization_barrier(
        (from_far, from_near, key_grad, value_grad)
    )
    query_grad = own_q + from_far.astype(jnp.float32) + from_near.astype(jnp.float32)
    return query_grad.astype(jnp.bfloat16), key_grad, value_grad


def solution(mesh):
    placed = (
        P(("group", "tm"), None),
        P(("group", "tm"), None),
        P(("group", "tm"), None),
        P(("group", "tm"), None),
        P(("group", "tm"), None),
    )
    return jax.shard_map(
        local,
        mesh=mesh,
        in_specs=placed,
        out_specs=(P(("group", "tm"), None), P(("group", "tm"), None), P(("group", "tm"), None)),
        check_vma=False,
    )
```

```python
import jax
import jax.numpy as jnp
import numpy as np
from jax import lax
from jax.experimental import pallas as pl
from jax.experimental.pallas import tpu as pltpu
from jax.sharding import PartitionSpec as P

HEADS = 12
HDIM = 128
BLOCK = 64
REACH = 2
FRAMES = 2
BANDS = 2
NEG = -1e30
LIST_ROWS = 16


def permute(value, rule):
    count = lax.axis_size("tm")
    pairs = []
    for source in range(count):
        target = rule(source)
        if 0 <= target < count:
            pairs.append((source, target))
    return lax.ppermute(value, "tm", pairs)


def swap_cores(value):
    return permute(value, lambda s: s ^ 1)


def down_even(value):
    return permute(value, lambda s: s - 2 if s % 2 == 0 else s + 2)


def up_even(value):
    return permute(value, lambda s: s + 2 if s % 2 == 0 else s - 2)


def pick_table(offset):
    blocks = FRAMES * BANDS
    slot = REACH - offset
    table = np.zeros((blocks, 30, blocks), np.float32)
    own = np.zeros((blocks, blocks), bool)
    if abs(offset) <= REACH:
        for qb in range(blocks):
            for kb in range(blocks):
                cand = (slot * FRAMES + kb // BANDS) * 3 + kb % BANDS - qb % BANDS + 1
                table[qb, cand, kb] = 1.0
                own[qb, kb] = offset == 0 and qb == kb
    return table, own


def parity_tables(even, even_offsets, odd_offsets):
    tables, owns = [], []
    for off_e, off_o in zip(even_offsets, odd_offsets):
        t_e, o_e = pick_table(off_e)
        t_o, o_o = pick_table(off_o)
        tables.append(jnp.where(even, jnp.asarray(t_e), jnp.asarray(t_o)))
        owns.append(jnp.where(even, jnp.asarray(o_e), jnp.asarray(o_o)))
    return jnp.concatenate(tables, axis=2), jnp.concatenate(owns, axis=1)


SCALE = HDIM ** (-0.5)
NT = (((1,), (1,)), ((), ()))
STEP_HEADS = 4


def slot_scores(q, g, k, v):
    s = lax.dot_general(k, q, NT, preferred_element_type=jnp.float32) * SCALE
    dp = lax.dot_general(v, g, NT, preferred_element_type=jnp.float32)
    return s, dp


def head_cols(j):
    return slice(j * HDIM, (j + 1) * HDIM)


def stats_kernel(q_ref, g_ref, k_ref, v_ref, m_ref, out_ref):
    m = m_ref[...] > 0
    for j in range(STEP_HEADS):
        cols = head_cols(j)
        s, dp = slot_scores(q_ref[:, cols], g_ref[:, cols], k_ref[:, cols], v_ref[:, cols])
        masked = jnp.where(m, s, NEG)
        mx = jnp.max(masked, axis=0, keepdims=True)
        e = jnp.where(m, jnp.exp(masked - mx), 0.0)
        total = jnp.sum(e, axis=0, keepdims=True)
        dot = jnp.sum(e * dp, axis=0, keepdims=True)
        out_ref[j] = jnp.concatenate([mx, total, dot], axis=0)


def back_kernel(q_ref, g_ref, k_ref, v_ref, m_ref, f_ref, dq_ref, dk_ref, dv_ref):
    m = m_ref[...] > 0
    for j in range(STEP_HEADS):
        cols = head_cols(j)
        q = q_ref[:, cols]
        g = g_ref[:, cols]
        k = k_ref[:, cols]
        s, dp = slot_scores(q, g, k, v_ref[:, cols])
        fin = f_ref[j]
        p = jnp.where(m, jnp.exp(s - fin[0:1]), 0.0)
        ds = (p * (dp - fin[1:2])).astype(jnp.bfloat16)
        dk_ref[:, cols] = jnp.dot(ds, q, preferred_element_type=jnp.float32) * SCALE
        dv_ref[:, cols] = jnp.dot(p.astype(jnp.bfloat16), g, preferred_element_type=jnp.float32)
        dq = lax.dot_general(ds, k, (((0,), (0,)), ((), ())), preferred_element_type=jnp.float32)
        dq_ref[:, cols] = (dq * SCALE).astype(dq_ref.dtype)


def dq_kernel(q_ref, g_ref, k_ref, v_ref, m_ref, f_ref, dq_ref):
    m = m_ref[...] > 0
    for j in range(STEP_HEADS):
        cols = head_cols(j)
        k = k_ref[:, cols]
        s, dp = slot_scores(q_ref[:, cols], g_ref[:, cols], k, v_ref[:, cols])
        fin = f_ref[j]
        p = jnp.where(m, jnp.exp(s - fin[0:1]), 0.0)
        ds = (p * (dp - fin[1:2])).astype(jnp.bfloat16)
        dq = lax.dot_general(ds, k, (((0,), (0,)), ((), ())), preferred_element_type=jnp.float32)
        dq_ref[:, cols] = (dq * SCALE).astype(dq_ref.dtype)


def kv_kernel(q_ref, g_ref, k_ref, v_ref, m_ref, f_ref, dk_ref, dv_ref):
    m = m_ref[...] > 0
    for j in range(STEP_HEADS):
        cols = head_cols(j)
        q = q_ref[:, cols]
        g = g_ref[:, cols]
        s, dp = slot_scores(q, g, k_ref[:, cols], v_ref[:, cols])
        fin = f_ref[j]
        p = jnp.where(m, jnp.exp(s - fin[0:1]), 0.0)
        ds = (p * (dp - fin[1:2])).astype(jnp.bfloat16)
        dk_ref[:, cols] = jnp.dot(ds, q, preferred_element_type=jnp.float32) * SCALE
        dv_ref[:, cols] = jnp.dot(p.astype(jnp.bfloat16), g, preferred_element_type=jnp.float32)


def slot_specs(q_rows, g_rows, nk, tok):
    cols = STEP_HEADS * HDIM
    return [
        pl.BlockSpec((tok, cols), lambda h: (q_rows, h)),
        pl.BlockSpec((tok, cols), lambda h: (g_rows, h)),
        pl.BlockSpec((nk, cols), lambda h: (0, h)),
        pl.BlockSpec((nk, cols), lambda h: (0, h)),
        pl.BlockSpec((nk, tok), lambda h: (0, 0)),
    ]


def slot_stats(q_arr, g_arr, q_rows, g_rows, key_arr, value_arr, mask_t, tok):
    nk = key_arr.shape[0]
    flops = 4 * tok * nk * HDIM * HEADS
    return pl.pallas_call(
        stats_kernel,
        grid=(HEADS // STEP_HEADS,),
        in_specs=slot_specs(q_rows, g_rows, nk, tok),
        out_specs=pl.BlockSpec((STEP_HEADS, 3, tok), lambda h: (h, 0, 0)),
        out_shape=jax.ShapeDtypeStruct((HEADS, 3, tok), jnp.float32),
        cost_estimate=pl.CostEstimate(
            flops=flops, transcendentals=tok * nk * HEADS, bytes_accessed=4 * (tok + nk) * HDIM * HEADS
        ),
    )(q_arr, g_arr, key_arr, value_arr, mask_t)


def slot_back(q_arr, g_arr, q_rows, g_rows, key_arr, value_arr, mask_t, fin, tok, dq_type):
    nk = key_arr.shape[0]
    width = HEADS * HDIM
    flops = 10 * tok * nk * HDIM * HEADS
    return pl.pallas_call(
        back_kernel,
        grid=(HEADS // STEP_HEADS,),
        in_specs=slot_specs(q_rows, g_rows, nk, tok)
        + [pl.BlockSpec((STEP_HEADS, 2, tok), lambda h: (h, 0, 0))],
        out_specs=[
            pl.BlockSpec((tok, STEP_HEADS * HDIM), lambda h: (0, h)),
            pl.BlockSpec((nk, STEP_HEADS * HDIM), lambda h: (0, h)),
            pl.BlockSpec((nk, STEP_HEADS * HDIM), lambda h: (0, h)),
        ],
        out_shape=[
            jax.ShapeDtypeStruct((tok, width), dq_type),
            jax.ShapeDtypeStruct((nk, width), jnp.float32),
            jax.ShapeDtypeStruct((nk, width), jnp.float32),
        ],
        cost_estimate=pl.CostEstimate(
            flops=flops, transcendentals=tok * nk * HEADS, bytes_accessed=12 * (tok + nk) * HDIM * HEADS
        ),
    )(q_arr, g_arr, key_arr, value_arr, mask_t, fin)


def slot_part(kernel, q_arr, g_arr, q_rows, g_rows, key_arr, value_arr, mask_t, fin, tok, outs):
    nk = key_arr.shape[0]
    cols = STEP_HEADS * HDIM
    rows = {"q": tok, "k": nk, "v": nk}
    flops = 6 * tok * nk * HDIM * HEADS
    return pl.pallas_call(
        kernel,
        grid=(HEADS // STEP_HEADS,),
        in_specs=slot_specs(q_rows, g_rows, nk, tok)
        + [pl.BlockSpec((STEP_HEADS, 2, tok), lambda h: (h, 0, 0))],
        out_specs=[pl.BlockSpec((rows[o], cols), lambda h: (0, h)) for o, _ in outs],
        out_shape=[jax.ShapeDtypeStruct((rows[o], HEADS * HDIM), t) for o, t in outs],
        cost_estimate=pl.CostEstimate(
            flops=flops, transcendentals=tok * nk * HEADS, bytes_accessed=6 * (tok + nk) * HDIM * HEADS
        ),
    )(q_arr, g_arr, key_arr, value_arr, mask_t, fin)


def local(queries, keys, values, grad_out, block_list):
    groups = lax.axis_size("tm")
    here = lax.axis_index("tm")
    even = here % 2 == 0
    up = jnp.where(even, 1, -1)
    tok, width = queries.shape
    blocks = FRAMES * BANDS
    cands = block_list.shape[1]

    flags = (block_list > 0).astype(jnp.bfloat16).reshape(1, blocks * cands)
    flags = jnp.pad(flags, ((0, LIST_ROWS - 1), (0, width - blocks * cands)))
    far_q_data = down_even(queries)
    near_q_data = up_even(queries)
    pack = jnp.concatenate([grad_out, flags], axis=0)
    far_data = down_even(pack)
    near_data = up_even(pack)
    partner_keys, partner_values = swap_cores((keys, values))
    key_both = jnp.concatenate([keys, partner_keys], axis=0)
    value_both = jnp.concatenate([values, partner_values], axis=0)

    slots = {
        "own": (queries, grad_out, 0, 0, block_list, 0, True, (0, -1), (0, 1)),
        "far": (far_q_data, far_data, 0, 0, None, 2 * up, True, (2, 1), (-2, -1)),
        "near": (near_q_data, near_data, 0, 0, None, -2 * up, False, (-2,), (2,)),
    }

    args = {}
    stats_out = {}
    for name, (q_arr, g_arr, q_rows, g_rows, rows, q_off, both, offs_e, offs_o) in slots.items():
        if rows is None:
            rows = g_arr[tok, : blocks * cands].reshape(blocks, cands)
        key_arr, value_arr = (key_both, value_both) if both else (keys, values)
        nkb = key_arr.shape[0] // BLOCK
        source = here + q_off
        valid = (source >= 0) & (source < groups)
        table, own = parity_tables(even, offs_e, offs_o)
        chosen = jnp.einsum("qc,qck->qk", (rows > 0).astype(jnp.float32), table) > 0
        mask4 = (chosen & valid) | own
        mask_t = jnp.broadcast_to(
            mask4.T[:, None, :, None], (nkb, BLOCK, blocks, BLOCK)
        ).reshape(nkb * BLOCK, tok).astype(jnp.float32)
        args[name] = (q_arr, g_arr, q_rows, g_rows, key_arr, value_arr, mask_t)
        stats_out[name] = slot_stats(*args[name], tok)

    stats_in = [
        (stats_out["own"], 0),
        (up_even(stats_out["far"]), -2 * up),
        (down_even(stats_out["near"]), 2 * up),
    ]
    maxes, sums, dots = [], [], []
    for stats, offset in stats_in:
        source = here + offset
        valid = (source >= 0) & (source < groups)
        maxes.append(jnp.where(valid, stats[:, 0], NEG))
        sums.append(jnp.where(valid, stats[:, 1], 0.0))
        dots.append(jnp.where(valid, stats[:, 2], 0.0))
    maxes, sums, dots = jnp.stack(maxes), jnp.stack(sums), jnp.stack(dots)
    top = jnp.max(maxes, axis=0)
    scale = jnp.exp(maxes - top[None])
    total = jnp.sum(sums * scale, axis=0)
    log_total = top + jnp.log(total)
    deltas = jnp.sum(dots * scale, axis=0) / total
    final = jnp.stack([log_total, deltas], axis=1)
    finals = {"far": down_even(final), "near": up_even(final)}

    own_q, own_k, own_v = slot_back(*args["own"], final, tok, jnp.float32)
    far_fin, near_fin, own_k, own_v = lax.optimization_barrier(
        (finals["far"], finals["near"], own_k, own_v)
    )
    finals = {"far": far_fin, "near": near_fin}
    far_q, far_k, far_v = slot_back(*args["far"], finals["far"], tok, jnp.bfloat16)
    (near_q,) = slot_part(dq_kernel, *args["near"], finals["near"], tok, [("q", jnp.bfloat16)])
    near_k, near_v = slot_part(
        kv_kernel, *args["near"], finals["near"], tok, [("k", jnp.float32), ("v", jnp.float32)]
    )
    from_far = up_even(far_q)
    from_near = down_even(near_q)

    def low(x):
        return x.astype(jnp.bfloat16).astype(jnp.float32)

    back_kg, back_vg = swap_cores(
        (low(far_k[tok:]) + low(own_k[tok:]), low(far_v[tok:]) + low(own_v[tok:]))
    )
    key_grad = (low(far_k[:tok]) + low(own_k[:tok]) + low(near_k) + back_kg).astype(jnp.bfloat16)
    value_grad = (low(far_v[:tok]) + low(own_v[:tok]) + low(near_v) + back_vg).astype(jnp.bfloat16)
    from_far, from_near, key_grad, value_grad = lax.optimization_barrier(
        (from_far, from_near, key_grad, value_grad)
    )
    query_grad = own_q + from_far.astype(jnp.float32) + from_near.astype(jnp.float32)
    return query_grad.astype(jnp.bfloat16), key_grad, value_grad


def solution(mesh):
    placed = (
        P(("group", "tm"), None),
        P(("group", "tm"), None),
        P(("group", "tm"), None),
        P(("group", "tm"), None),
        P(("group", "tm"), None),
    )
    return jax.shard_map(
        local,
        mesh=mesh,
        in_specs=placed,
        out_specs=(P(("group", "tm"), None), P(("group", "tm"), None), P(("group", "tm"), None)),
        check_vma=False,
    )
```

```python
import jax
import jax.numpy as jnp
import numpy as np
from jax import lax
from jax.experimental import pallas as pl
from jax.experimental.pallas import tpu as pltpu
from jax.sharding import PartitionSpec as P

HEADS = 12
HDIM = 128
BLOCK = 64
REACH = 2
FRAMES = 2
BANDS = 2
NEG = -1e30
LIST_ROWS = 16


def permute(value, rule):
    count = lax.axis_size("tm")
    pairs = []
    for source in range(count):
        target = rule(source)
        if 0 <= target < count:
            pairs.append((source, target))
    return lax.ppermute(value, "tm", pairs)


def swap_cores(value):
    return permute(value, lambda s: s ^ 1)


def down_even(value):
    return permute(value, lambda s: s - 2 if s % 2 == 0 else s + 2)


def up_even(value):
    return permute(value, lambda s: s + 2 if s % 2 == 0 else s - 2)


def pick_table(offset):
    blocks = FRAMES * BANDS
    slot = REACH - offset
    table = np.zeros((blocks, 30, blocks), np.float32)
    own = np.zeros((blocks, blocks), bool)
    if abs(offset) <= REACH:
        for qb in range(blocks):
            for kb in range(blocks):
                cand = (slot * FRAMES + kb // BANDS) * 3 + kb % BANDS - qb % BANDS + 1
                table[qb, cand, kb] = 1.0
                own[qb, kb] = offset == 0 and qb == kb
    return table, own


def parity_tables(even, even_offsets, odd_offsets):
    tables, owns = [], []
    for off_e, off_o in zip(even_offsets, odd_offsets):
        t_e, o_e = pick_table(off_e)
        t_o, o_o = pick_table(off_o)
        tables.append(jnp.where(even, jnp.asarray(t_e), jnp.asarray(t_o)))
        owns.append(jnp.where(even, jnp.asarray(o_e), jnp.asarray(o_o)))
    return jnp.concatenate(tables, axis=2), jnp.concatenate(owns, axis=1)


SCALE = HDIM ** (-0.5)
NT = (((1,), (1,)), ((), ()))
STEP_HEADS = 4


def slot_scores(q, g, k, v):
    s = lax.dot_general(k, q, NT, preferred_element_type=jnp.float32) * SCALE
    dp = lax.dot_general(v, g, NT, preferred_element_type=jnp.float32)
    return s, dp


def head_cols(j):
    return slice(j * HDIM, (j + 1) * HDIM)


def stats_kernel(q_ref, g_ref, k_ref, v_ref, m_ref, out_ref):
    m = m_ref[...] > 0
    for j in range(STEP_HEADS):
        cols = head_cols(j)
        s, dp = slot_scores(q_ref[:, cols], g_ref[:, cols], k_ref[:, cols], v_ref[:, cols])
        masked = jnp.where(m, s, NEG)
        mx = jnp.max(masked, axis=0, keepdims=True)
        e = jnp.where(m, jnp.exp(masked - mx), 0.0)
        total = jnp.sum(e, axis=0, keepdims=True)
        out_ref[j] = jnp.concatenate([mx, total], axis=0)


def delta_kernel(q_ref, g_ref, k_ref, v_ref, m_ref, f_ref, out_ref):
    m = m_ref[...] > 0
    for j in range(STEP_HEADS):
        cols = head_cols(j)
        s, dp = slot_scores(q_ref[:, cols], g_ref[:, cols], k_ref[:, cols], v_ref[:, cols])
        p = jnp.where(m, jnp.exp(s - f_ref[j]), 0.0)
        low = lax.reduce_precision(p, exponent_bits=8, mantissa_bits=7)
        out_ref[j] = jnp.sum(low * dp, axis=0, keepdims=True)


def back_kernel(q_ref, g_ref, k_ref, v_ref, m_ref, f_ref, dq_ref, dk_ref, dv_ref):
    m = m_ref[...] > 0
    for j in range(STEP_HEADS):
        cols = head_cols(j)
        q = q_ref[:, cols]
        g = g_ref[:, cols]
        k = k_ref[:, cols]
        s, dp = slot_scores(q, g, k, v_ref[:, cols])
        fin = f_ref[j]
        p = jnp.where(m, jnp.exp(s - fin[0:1]), 0.0)
        ds = (p * (dp - fin[1:2])).astype(jnp.bfloat16)
        dk_ref[:, cols] = jnp.dot(ds, q, preferred_element_type=jnp.float32) * SCALE
        dv_ref[:, cols] = jnp.dot(p.astype(jnp.bfloat16), g, preferred_element_type=jnp.float32)
        dq = lax.dot_general(ds, k, (((0,), (0,)), ((), ())), preferred_element_type=jnp.float32)
        dq_ref[:, cols] = (dq * SCALE).astype(dq_ref.dtype)


def slot_specs(q_rows, g_rows, nk, tok):
    cols = STEP_HEADS * HDIM
    return [
        pl.BlockSpec((tok, cols), lambda h: (q_rows, h)),
        pl.BlockSpec((tok, cols), lambda h: (g_rows, h)),
        pl.BlockSpec((nk, cols), lambda h: (0, h)),
        pl.BlockSpec((nk, cols), lambda h: (0, h)),
        pl.BlockSpec((nk, tok), lambda h: (0, 0)),
    ]


def slot_stats(q_arr, g_arr, q_rows, g_rows, key_arr, value_arr, mask_t, tok):
    nk = key_arr.shape[0]
    flops = 4 * tok * nk * HDIM * HEADS
    return pl.pallas_call(
        stats_kernel,
        grid=(HEADS // STEP_HEADS,),
        in_specs=slot_specs(q_rows, g_rows, nk, tok),
        out_specs=pl.BlockSpec((STEP_HEADS, 2, tok), lambda h: (h, 0, 0)),
        out_shape=jax.ShapeDtypeStruct((HEADS, 2, tok), jnp.float32),
        cost_estimate=pl.CostEstimate(
            flops=flops, transcendentals=tok * nk * HEADS, bytes_accessed=4 * (tok + nk) * HDIM * HEADS
        ),
    )(q_arr, g_arr, key_arr, value_arr, mask_t)


def slot_delta(q_arr, g_arr, q_rows, g_rows, key_arr, value_arr, mask_t, lse, tok):
    nk = key_arr.shape[0]
    flops = 4 * tok * nk * HDIM * HEADS
    return pl.pallas_call(
        delta_kernel,
        grid=(HEADS // STEP_HEADS,),
        in_specs=slot_specs(q_rows, g_rows, nk, tok)
        + [pl.BlockSpec((STEP_HEADS, 1, tok), lambda h: (h, 0, 0))],
        out_specs=pl.BlockSpec((STEP_HEADS, 1, tok), lambda h: (h, 0, 0)),
        out_shape=jax.ShapeDtypeStruct((HEADS, 1, tok), jnp.float32),
        cost_estimate=pl.CostEstimate(
            flops=flops, transcendentals=tok * nk * HEADS, bytes_accessed=4 * (tok + nk) * HDIM * HEADS
        ),
    )(q_arr, g_arr, key_arr, value_arr, mask_t, lse)


def slot_back(q_arr, g_arr, q_rows, g_rows, key_arr, value_arr, mask_t, fin, tok, dq_type):
    nk = key_arr.shape[0]
    width = HEADS * HDIM
    flops = 10 * tok * nk * HDIM * HEADS
    return pl.pallas_call(
        back_kernel,
        grid=(HEADS // STEP_HEADS,),
        in_specs=slot_specs(q_rows, g_rows, nk, tok)
        + [pl.BlockSpec((STEP_HEADS, 2, tok), lambda h: (h, 0, 0))],
        out_specs=[
            pl.BlockSpec((tok, STEP_HEADS * HDIM), lambda h: (0, h)),
            pl.BlockSpec((nk, STEP_HEADS * HDIM), lambda h: (0, h)),
            pl.BlockSpec((nk, STEP_HEADS * HDIM), lambda h: (0, h)),
        ],
        out_shape=[
            jax.ShapeDtypeStruct((tok, width), dq_type),
            jax.ShapeDtypeStruct((nk, width), jnp.float32),
            jax.ShapeDtypeStruct((nk, width), jnp.float32),
        ],
        cost_estimate=pl.CostEstimate(
            flops=flops, transcendentals=tok * nk * HEADS, bytes_accessed=12 * (tok + nk) * HDIM * HEADS
        ),
    )(q_arr, g_arr, key_arr, value_arr, mask_t, fin)


def local(queries, keys, values, grad_out, block_list):
    groups = lax.axis_size("tm")
    here = lax.axis_index("tm")
    even = here % 2 == 0
    up = jnp.where(even, 1, -1)
    tok, width = queries.shape
    blocks = FRAMES * BANDS
    cands = block_list.shape[1]

    flags = (block_list > 0).astype(jnp.bfloat16).reshape(1, blocks * cands)
    flags = jnp.pad(flags, ((0, LIST_ROWS - 1), (0, width - blocks * cands)))
    far_q_data = down_even(queries)
    near_q_data = up_even(queries)
    pack = jnp.concatenate([grad_out, flags], axis=0)
    far_data = down_even(pack)
    near_data = up_even(pack)
    partner_keys, partner_values = swap_cores((keys, values))
    key_both = jnp.concatenate([keys, partner_keys], axis=0)
    value_both = jnp.concatenate([values, partner_values], axis=0)

    slots = {
        "own": (queries, grad_out, 0, 0, block_list, 0, True, (0, -1), (0, 1)),
        "far": (far_q_data, far_data, 0, 0, None, 2 * up, True, (2, 1), (-2, -1)),
        "near": (near_q_data, near_data, 0, 0, None, -2 * up, False, (-2,), (2,)),
    }

    args = {}
    stats_out = {}
    for name, (q_arr, g_arr, q_rows, g_rows, rows, q_off, both, offs_e, offs_o) in slots.items():
        if rows is None:
            rows = g_arr[tok, : blocks * cands].reshape(blocks, cands)
        key_arr, value_arr = (key_both, value_both) if both else (keys, values)
        nkb = key_arr.shape[0] // BLOCK
        source = here + q_off
        valid = (source >= 0) & (source < groups)
        table, own = parity_tables(even, offs_e, offs_o)
        chosen = jnp.einsum("qc,qck->qk", (rows > 0).astype(jnp.float32), table) > 0
        mask4 = (chosen & valid) | own
        mask_t = jnp.broadcast_to(
            mask4.T[:, None, :, None], (nkb, BLOCK, blocks, BLOCK)
        ).reshape(nkb * BLOCK, tok).astype(jnp.float32)
        args[name] = (q_arr, g_arr, q_rows, g_rows, key_arr, value_arr, mask_t)
        stats_out[name] = slot_stats(*args[name], tok)

    stats_in = [
        (stats_out["own"], 0),
        (up_even(stats_out["far"]), -2 * up),
        (down_even(stats_out["near"]), 2 * up),
    ]
    maxes, sums = [], []
    for stats, offset in stats_in:
        source = here + offset
        valid = (source >= 0) & (source < groups)
        maxes.append(jnp.where(valid, stats[:, 0], NEG))
        sums.append(jnp.where(valid, stats[:, 1], 0.0))
    maxes, sums = jnp.stack(maxes), jnp.stack(sums)
    top = jnp.max(maxes, axis=0)
    total = jnp.sum(sums * jnp.exp(maxes - top[None]), axis=0)
    log_total = (top + jnp.log(total))[:, None, :]
    lses = {"own": log_total, "far": down_even(log_total), "near": up_even(log_total)}
    parts = {name: slot_delta(*args[name], lses[name], tok) for name in slots}
    deltas = parts["own"] + up_even(parts["far"]) + down_even(parts["near"])
    final = jnp.concatenate([log_total, deltas], axis=1)
    finals = {"far": down_even(final), "near": up_even(final)}

    own_q, own_k, own_v = slot_back(*args["own"], final, tok, jnp.float32)
    far_fin, near_fin, own_k, own_v = lax.optimization_barrier(
        (finals["far"], finals["near"], own_k, own_v)
    )
    finals = {"far": far_fin, "near": near_fin}
    far_q, far_k, far_v = slot_back(*args["far"], finals["far"], tok, jnp.bfloat16)
    near_q, near_k, near_v = slot_back(*args["near"], finals["near"], tok, jnp.bfloat16)
    from_far = up_even(far_q)
    from_near = down_even(near_q)

    def low(x):
        return x.astype(jnp.bfloat16).astype(jnp.float32)

    back_kg, back_vg = swap_cores(
        (low(far_k[tok:]) + low(own_k[tok:]), low(far_v[tok:]) + low(own_v[tok:]))
    )
    key_grad = (low(far_k[:tok]) + low(own_k[:tok]) + low(near_k) + back_kg).astype(jnp.bfloat16)
    value_grad = (low(far_v[:tok]) + low(own_v[:tok]) + low(near_v) + back_vg).astype(jnp.bfloat16)
    from_far, from_near, key_grad, value_grad = lax.optimization_barrier(
        (from_far, from_near, key_grad, value_grad)
    )
    query_grad = own_q + from_far.astype(jnp.float32) + from_near.astype(jnp.float32)
    return query_grad.astype(jnp.bfloat16), key_grad, value_grad


def solution(mesh):
    placed = (
        P(("group", "tm"), None),
        P(("group", "tm"), None),
        P(("group", "tm"), None),
        P(("group", "tm"), None),
        P(("group", "tm"), None),
    )
    return jax.shard_map(
        local,
        mesh=mesh,
        in_specs=placed,
        out_specs=(P(("group", "tm"), None), P(("group", "tm"), None), P(("group", "tm"), None)),
        check_vma=False,
    )
```

```python
import jax
import jax.numpy as jnp
import numpy as np
from jax import lax
from jax.experimental import pallas as pl
from jax.experimental.pallas import tpu as pltpu
from jax.sharding import PartitionSpec as P

HEADS = 12
HDIM = 128
BLOCK = 64
REACH = 2
FRAMES = 2
BANDS = 2
NEG = -1e30
LIST_ROWS = 16


def permute(value, rule):
    count = lax.axis_size("tm")
    pairs = []
    for source in range(count):
        target = rule(source)
        if 0 <= target < count:
            pairs.append((source, target))
    return lax.ppermute(value, "tm", pairs)


def swap_cores(value):
    return permute(value, lambda s: s ^ 1)


def down_even(value):
    return permute(value, lambda s: s - 2 if s % 2 == 0 else s + 2)


def up_even(value):
    return permute(value, lambda s: s + 2 if s % 2 == 0 else s - 2)


def pick_table(offset):
    blocks = FRAMES * BANDS
    slot = REACH - offset
    table = np.zeros((blocks, 30, blocks), np.float32)
    own = np.zeros((blocks, blocks), bool)
    if abs(offset) <= REACH:
        for qb in range(blocks):
            for kb in range(blocks):
                cand = (slot * FRAMES + kb // BANDS) * 3 + kb % BANDS - qb % BANDS + 1
                table[qb, cand, kb] = 1.0
                own[qb, kb] = offset == 0 and qb == kb
    return table, own


def parity_tables(even, even_offsets, odd_offsets):
    tables, owns = [], []
    for off_e, off_o in zip(even_offsets, odd_offsets):
        t_e, o_e = pick_table(off_e)
        t_o, o_o = pick_table(off_o)
        tables.append(jnp.where(even, jnp.asarray(t_e), jnp.asarray(t_o)))
        owns.append(jnp.where(even, jnp.asarray(o_e), jnp.asarray(o_o)))
    return jnp.concatenate(tables, axis=2), jnp.concatenate(owns, axis=1)


SCALE = HDIM ** (-0.5)
NT = (((1,), (1,)), ((), ()))
STEP_HEADS = 4


def slot_scores(q, g, k, v):
    s = lax.dot_general(k, q, NT, preferred_element_type=jnp.float32) * SCALE
    dp = lax.dot_general(v, g, NT, preferred_element_type=jnp.float32)
    return s, dp


def head_cols(j):
    return slice(j * HDIM, (j + 1) * HDIM)


def stats_kernel(q_ref, g_ref, k_ref, v_ref, m_ref, out_ref):
    m = m_ref[...] > 0
    for j in range(STEP_HEADS):
        cols = head_cols(j)
        s, dp = slot_scores(q_ref[:, cols], g_ref[:, cols], k_ref[:, cols], v_ref[:, cols])
        masked = jnp.where(m, s, NEG)
        mx = jnp.max(masked, axis=0, keepdims=True)
        e = jnp.where(m, jnp.exp(masked - mx), 0.0)
        total = jnp.sum(e, axis=0, keepdims=True)
        out_ref[j] = jnp.concatenate([mx, total], axis=0)


def delta_kernel(q_ref, g_ref, k_ref, v_ref, m_ref, f_ref, out_ref):
    m = m_ref[...] > 0
    for j in range(STEP_HEADS):
        cols = head_cols(j)
        s, dp = slot_scores(q_ref[:, cols], g_ref[:, cols], k_ref[:, cols], v_ref[:, cols])
        p = jnp.where(m, jnp.exp(s - f_ref[j]), 0.0)
        low = lax.reduce_precision(p, exponent_bits=8, mantissa_bits=7)
        out_ref[j] = jnp.sum(low * dp, axis=0, keepdims=True)


def back_kernel(q_ref, g_ref, k_ref, v_ref, m_ref, f_ref, dq_ref, dk_ref, dv_ref):
    m = m_ref[...] > 0
    for j in range(STEP_HEADS):
        cols = head_cols(j)
        q = q_ref[:, cols]
        g = g_ref[:, cols]
        k = k_ref[:, cols]
        s, dp = slot_scores(q, g, k, v_ref[:, cols])
        fin = f_ref[j]
        p = jnp.where(m, jnp.exp(s - fin[0:1]), 0.0)
        ds = (p * (dp - fin[1:2])).astype(jnp.bfloat16)
        dk_ref[:, cols] = jnp.dot(ds, q, preferred_element_type=jnp.float32) * SCALE
        dv_ref[:, cols] = jnp.dot(p.astype(jnp.bfloat16), g, preferred_element_type=jnp.float32)
        dq = lax.dot_general(ds, k, (((0,), (0,)), ((), ())), preferred_element_type=jnp.float32)
        dq_ref[:, cols] = (dq * SCALE).astype(dq_ref.dtype)


def slot_specs(q_rows, g_rows, nk, tok):
    cols = STEP_HEADS * HDIM
    return [
        pl.BlockSpec((tok, cols), lambda h: (q_rows, h)),
        pl.BlockSpec((tok, cols), lambda h: (g_rows, h)),
        pl.BlockSpec((nk, cols), lambda h: (0, h)),
        pl.BlockSpec((nk, cols), lambda h: (0, h)),
        pl.BlockSpec((nk, tok), lambda h: (0, 0)),
    ]


def slot_stats(q_arr, g_arr, q_rows, g_rows, key_arr, value_arr, mask_t, tok):
    nk = key_arr.shape[0]
    flops = 4 * tok * nk * HDIM * HEADS
    return pl.pallas_call(
        stats_kernel,
        grid=(HEADS // STEP_HEADS,),
        in_specs=slot_specs(q_rows, g_rows, nk, tok),
        out_specs=pl.BlockSpec((STEP_HEADS, 2, tok), lambda h: (h, 0, 0)),
        out_shape=jax.ShapeDtypeStruct((HEADS, 2, tok), jnp.float32),
        cost_estimate=pl.CostEstimate(
            flops=flops, transcendentals=tok * nk * HEADS, bytes_accessed=4 * (tok + nk) * HDIM * HEADS
        ),
    )(q_arr, g_arr, key_arr, value_arr, mask_t)


def slot_delta(q_arr, g_arr, q_rows, g_rows, key_arr, value_arr, mask_t, lse, tok):
    nk = key_arr.shape[0]
    flops = 4 * tok * nk * HDIM * HEADS
    return pl.pallas_call(
        delta_kernel,
        grid=(HEADS // STEP_HEADS,),
        in_specs=slot_specs(q_rows, g_rows, nk, tok)
        + [pl.BlockSpec((STEP_HEADS, 1, tok), lambda h: (h, 0, 0))],
        out_specs=pl.BlockSpec((STEP_HEADS, 1, tok), lambda h: (h, 0, 0)),
        out_shape=jax.ShapeDtypeStruct((HEADS, 1, tok), jnp.float32),
        cost_estimate=pl.CostEstimate(
            flops=flops, transcendentals=tok * nk * HEADS, bytes_accessed=4 * (tok + nk) * HDIM * HEADS
        ),
    )(q_arr, g_arr, key_arr, value_arr, mask_t, lse)


def slot_back(q_arr, g_arr, q_rows, g_rows, key_arr, value_arr, mask_t, fin, tok, dq_type):
    nk = key_arr.shape[0]
    width = HEADS * HDIM
    flops = 10 * tok * nk * HDIM * HEADS
    return pl.pallas_call(
        back_kernel,
        grid=(HEADS // STEP_HEADS,),
        in_specs=slot_specs(q_rows, g_rows, nk, tok)
        + [pl.BlockSpec((STEP_HEADS, 2, tok), lambda h: (h, 0, 0))],
        out_specs=[
            pl.BlockSpec((tok, STEP_HEADS * HDIM), lambda h: (0, h)),
            pl.BlockSpec((nk, STEP_HEADS * HDIM), lambda h: (0, h)),
            pl.BlockSpec((nk, STEP_HEADS * HDIM), lambda h: (0, h)),
        ],
        out_shape=[
            jax.ShapeDtypeStruct((tok, width), dq_type),
            jax.ShapeDtypeStruct((nk, width), jnp.float32),
            jax.ShapeDtypeStruct((nk, width), jnp.float32),
        ],
        cost_estimate=pl.CostEstimate(
            flops=flops, transcendentals=tok * nk * HEADS, bytes_accessed=12 * (tok + nk) * HDIM * HEADS
        ),
    )(q_arr, g_arr, key_arr, value_arr, mask_t, fin)


def local(queries, keys, values, grad_out, block_list):
    groups = lax.axis_size("tm")
    here = lax.axis_index("tm")
    even = here % 2 == 0
    up = jnp.where(even, 1, -1)
    tok, width = queries.shape
    blocks = FRAMES * BANDS
    cands = block_list.shape[1]

    flags = (block_list > 0).astype(jnp.bfloat16).reshape(1, blocks * cands)
    flags = jnp.pad(flags, ((0, LIST_ROWS - 1), (0, width - blocks * cands)))
    far_q_data = down_even(queries)
    near_q_data = up_even(queries)
    pack = jnp.concatenate([grad_out, flags], axis=0)
    far_data = down_even(pack)
    near_data = up_even(pack)
    partner_keys, partner_values = swap_cores((keys, values))
    key_both = jnp.concatenate([keys, partner_keys], axis=0)
    value_both = jnp.concatenate([values, partner_values], axis=0)

    slots = {
        "own": (queries, grad_out, 0, 0, block_list, 0, True, (0, -1), (0, 1)),
        "far": (far_q_data, far_data, 0, 0, None, 2 * up, True, (2, 1), (-2, -1)),
        "near": (near_q_data, near_data, 0, 0, None, -2 * up, False, (-2,), (2,)),
    }

    args = {}
    stats_out = {}
    for name in ("own", "far", "near"):
        if name == "far":
            fq, fg, nq, ng, stats_out["own"] = lax.optimization_barrier(
                (far_q_data, far_data, near_q_data, near_data, stats_out["own"])
            )
            slots["far"] = (fq, fg) + slots["far"][2:]
            slots["near"] = (nq, ng) + slots["near"][2:]
        q_arr, g_arr, q_rows, g_rows, rows, q_off, both, offs_e, offs_o = slots[name]
        if rows is None:
            rows = g_arr[tok, : blocks * cands].reshape(blocks, cands)
        key_arr, value_arr = (key_both, value_both) if both else (keys, values)
        nkb = key_arr.shape[0] // BLOCK
        source = here + q_off
        valid = (source >= 0) & (source < groups)
        table, own = parity_tables(even, offs_e, offs_o)
        chosen = jnp.einsum("qc,qck->qk", (rows > 0).astype(jnp.float32), table) > 0
        mask4 = (chosen & valid) | own
        mask_t = jnp.broadcast_to(
            mask4.T[:, None, :, None], (nkb, BLOCK, blocks, BLOCK)
        ).reshape(nkb * BLOCK, tok).astype(jnp.float32)
        args[name] = (q_arr, g_arr, q_rows, g_rows, key_arr, value_arr, mask_t)
        stats_out[name] = slot_stats(*args[name], tok)

    stats_in = [
        (stats_out["own"], 0),
        (up_even(stats_out["far"]), -2 * up),
        (down_even(stats_out["near"]), 2 * up),
    ]
    maxes, sums = [], []
    for stats, offset in stats_in:
        source = here + offset
        valid = (source >= 0) & (source < groups)
        maxes.append(jnp.where(valid, stats[:, 0], NEG))
        sums.append(jnp.where(valid, stats[:, 1], 0.0))
    maxes, sums = jnp.stack(maxes), jnp.stack(sums)
    top = jnp.max(maxes, axis=0)
    total = jnp.sum(sums * jnp.exp(maxes - top[None]), axis=0)
    log_total = (top + jnp.log(total))[:, None, :]
    lses = {"own": log_total, "far": down_even(log_total), "near": up_even(log_total)}
    parts = {name: slot_delta(*args[name], lses[name], tok) for name in slots}
    deltas = parts["own"] + up_even(parts["far"]) + down_even(parts["near"])
    final = jnp.concatenate([log_total, deltas], axis=1)
    finals = {"far": down_even(final), "near": up_even(final)}

    own_q, own_k, own_v = slot_back(*args["own"], final, tok, jnp.float32)
    far_fin, near_fin, own_k, own_v = lax.optimization_barrier(
        (finals["far"], finals["near"], own_k, own_v)
    )
    finals = {"far": far_fin, "near": near_fin}
    far_q, far_k, far_v = slot_back(*args["far"], finals["far"], tok, jnp.bfloat16)
    near_q, near_k, near_v = slot_back(*args["near"], finals["near"], tok, jnp.bfloat16)
    from_far = up_even(far_q)
    from_near = down_even(near_q)

    def low(x):
        return x.astype(jnp.bfloat16).astype(jnp.float32)

    back_kg, back_vg = swap_cores(
        (low(far_k[tok:]) + low(own_k[tok:]), low(far_v[tok:]) + low(own_v[tok:]))
    )
    key_grad = (low(far_k[:tok]) + low(own_k[:tok]) + low(near_k) + back_kg).astype(jnp.bfloat16)
    value_grad = (low(far_v[:tok]) + low(own_v[:tok]) + low(near_v) + back_vg).astype(jnp.bfloat16)
    from_far, from_near, key_grad, value_grad = lax.optimization_barrier(
        (from_far, from_near, key_grad, value_grad)
    )
    query_grad = own_q + from_far.astype(jnp.float32) + from_near.astype(jnp.float32)
    return query_grad.astype(jnp.bfloat16), key_grad, value_grad


def solution(mesh):
    placed = (
        P(("group", "tm"), None),
        P(("group", "tm"), None),
        P(("group", "tm"), None),
        P(("group", "tm"), None),
        P(("group", "tm"), None),
    )
    return jax.shard_map(
        local,
        mesh=mesh,
        in_specs=placed,
        out_specs=(P(("group", "tm"), None), P(("group", "tm"), None), P(("group", "tm"), None)),
        check_vma=False,
    )
```

```python
import jax
import jax.numpy as jnp
import numpy as np
from jax import lax
from jax.experimental import pallas as pl
from jax.experimental.pallas import tpu as pltpu
from jax.sharding import PartitionSpec as P

HEADS = 12
HDIM = 128
BLOCK = 64
REACH = 2
FRAMES = 2
BANDS = 2
NEG = -1e30
LIST_ROWS = 16


def permute(value, rule):
    count = lax.axis_size("tm")
    pairs = []
    for source in range(count):
        target = rule(source)
        if 0 <= target < count:
            pairs.append((source, target))
    return lax.ppermute(value, "tm", pairs)


def swap_cores(value):
    return permute(value, lambda s: s ^ 1)


def down_even(value):
    return permute(value, lambda s: s - 2 if s % 2 == 0 else s + 2)


def up_even(value):
    return permute(value, lambda s: s + 2 if s % 2 == 0 else s - 2)


def pick_table(offset):
    blocks = FRAMES * BANDS
    slot = REACH - offset
    table = np.zeros((blocks, 30, blocks), np.float32)
    own = np.zeros((blocks, blocks), bool)
    if abs(offset) <= REACH:
        for qb in range(blocks):
            for kb in range(blocks):
                cand = (slot * FRAMES + kb // BANDS) * 3 + kb % BANDS - qb % BANDS + 1
                table[qb, cand, kb] = 1.0
                own[qb, kb] = offset == 0 and qb == kb
    return table, own


def parity_tables(even, even_offsets, odd_offsets):
    tables, owns = [], []
    for off_e, off_o in zip(even_offsets, odd_offsets):
        t_e, o_e = pick_table(off_e)
        t_o, o_o = pick_table(off_o)
        tables.append(jnp.where(even, jnp.asarray(t_e), jnp.asarray(t_o)))
        owns.append(jnp.where(even, jnp.asarray(o_e), jnp.asarray(o_o)))
    return jnp.concatenate(tables, axis=2), jnp.concatenate(owns, axis=1)


SCALE = HDIM ** (-0.5)
NT = (((1,), (1,)), ((), ()))
STEP_HEADS = 4


def slot_scores(q, g, k, v):
    s = lax.dot_general(k, q, NT, preferred_element_type=jnp.float32) * SCALE
    dp = lax.dot_general(v, g, NT, preferred_element_type=jnp.float32)
    return s, dp


def head_cols(j):
    return slice(j * HDIM, (j + 1) * HDIM)


def stats_kernel(q_ref, k_ref, m_ref, out_ref):
    m = m_ref[...] > 0
    for j in range(STEP_HEADS):
        cols = head_cols(j)
        s = lax.dot_general(k_ref[:, cols], q_ref[:, cols], NT, preferred_element_type=jnp.float32)
        s = s * SCALE
        masked = jnp.where(m, s, NEG)
        mx = jnp.max(masked, axis=0, keepdims=True)
        e = jnp.where(m, jnp.exp(masked - mx), 0.0)
        total = jnp.sum(e, axis=0, keepdims=True)
        out_ref[j] = jnp.concatenate([mx, total], axis=0)


def delta_kernel(q_ref, g_ref, k_ref, v_ref, m_ref, f_ref, out_ref):
    m = m_ref[...] > 0
    for j in range(STEP_HEADS):
        cols = head_cols(j)
        s, dp = slot_scores(q_ref[:, cols], g_ref[:, cols], k_ref[:, cols], v_ref[:, cols])
        p = jnp.where(m, jnp.exp(s - f_ref[j]), 0.0)
        low = lax.reduce_precision(p, exponent_bits=8, mantissa_bits=7)
        out_ref[j] = jnp.sum(low * dp, axis=0, keepdims=True)


def back_kernel(q_ref, g_ref, k_ref, v_ref, m_ref, f_ref, dq_ref, dk_ref, dv_ref):
    m = m_ref[...] > 0
    for j in range(STEP_HEADS):
        cols = head_cols(j)
        q = q_ref[:, cols]
        g = g_ref[:, cols]
        k = k_ref[:, cols]
        s, dp = slot_scores(q, g, k, v_ref[:, cols])
        fin = f_ref[j]
        p = jnp.where(m, jnp.exp(s - fin[0:1]), 0.0)
        ds = (p * (dp - fin[1:2])).astype(jnp.bfloat16)
        dk_ref[:, cols] = jnp.dot(ds, q, preferred_element_type=jnp.float32) * SCALE
        dv_ref[:, cols] = jnp.dot(p.astype(jnp.bfloat16), g, preferred_element_type=jnp.float32)
        dq = lax.dot_general(ds, k, (((0,), (0,)), ((), ())), preferred_element_type=jnp.float32)
        dq_ref[:, cols] = (dq * SCALE).astype(dq_ref.dtype)


def slot_specs(q_rows, g_rows, nk, tok):
    cols = STEP_HEADS * HDIM
    return [
        pl.BlockSpec((tok, cols), lambda h: (q_rows, h)),
        pl.BlockSpec((tok, cols), lambda h: (g_rows, h)),
        pl.BlockSpec((nk, cols), lambda h: (0, h)),
        pl.BlockSpec((nk, cols), lambda h: (0, h)),
        pl.BlockSpec((nk, tok), lambda h: (0, 0)),
    ]


def slot_stats(q_arr, g_arr, q_rows, g_rows, key_arr, value_arr, mask_t, tok):
    nk = key_arr.shape[0]
    flops = 2 * tok * nk * HDIM * HEADS
    return pl.pallas_call(
        stats_kernel,
        grid=(HEADS // STEP_HEADS,),
        in_specs=[slot_specs(q_rows, g_rows, nk, tok)[i] for i in (0, 2, 4)],
        out_specs=pl.BlockSpec((STEP_HEADS, 2, tok), lambda h: (h, 0, 0)),
        out_shape=jax.ShapeDtypeStruct((HEADS, 2, tok), jnp.float32),
        cost_estimate=pl.CostEstimate(
            flops=flops, transcendentals=tok * nk * HEADS, bytes_accessed=4 * (tok + nk) * HDIM * HEADS
        ),
    )(q_arr, key_arr, mask_t)


def slot_delta(q_arr, g_arr, q_rows, g_rows, key_arr, value_arr, mask_t, lse, tok):
    nk = key_arr.shape[0]
    flops = 4 * tok * nk * HDIM * HEADS
    return pl.pallas_call(
        delta_kernel,
        grid=(HEADS // STEP_HEADS,),
        in_specs=slot_specs(q_rows, g_rows, nk, tok)
        + [pl.BlockSpec((STEP_HEADS, 1, tok), lambda h: (h, 0, 0))],
        out_specs=pl.BlockSpec((STEP_HEADS, 1, tok), lambda h: (h, 0, 0)),
        out_shape=jax.ShapeDtypeStruct((HEADS, 1, tok), jnp.float32),
        cost_estimate=pl.CostEstimate(
            flops=flops, transcendentals=tok * nk * HEADS, bytes_accessed=4 * (tok + nk) * HDIM * HEADS
        ),
    )(q_arr, g_arr, key_arr, value_arr, mask_t, lse)


def slot_back(q_arr, g_arr, q_rows, g_rows, key_arr, value_arr, mask_t, fin, tok, dq_type):
    nk = key_arr.shape[0]
    width = HEADS * HDIM
    flops = 10 * tok * nk * HDIM * HEADS
    return pl.pallas_call(
        back_kernel,
        grid=(HEADS // STEP_HEADS,),
        in_specs=slot_specs(q_rows, g_rows, nk, tok)
        + [pl.BlockSpec((STEP_HEADS, 2, tok), lambda h: (h, 0, 0))],
        out_specs=[
            pl.BlockSpec((tok, STEP_HEADS * HDIM), lambda h: (0, h)),
            pl.BlockSpec((nk, STEP_HEADS * HDIM), lambda h: (0, h)),
            pl.BlockSpec((nk, STEP_HEADS * HDIM), lambda h: (0, h)),
        ],
        out_shape=[
            jax.ShapeDtypeStruct((tok, width), dq_type),
            jax.ShapeDtypeStruct((nk, width), jnp.float32),
            jax.ShapeDtypeStruct((nk, width), jnp.float32),
        ],
        cost_estimate=pl.CostEstimate(
            flops=flops, transcendentals=tok * nk * HEADS, bytes_accessed=12 * (tok + nk) * HDIM * HEADS
        ),
    )(q_arr, g_arr, key_arr, value_arr, mask_t, fin)


def local(queries, keys, values, grad_out, block_list):
    groups = lax.axis_size("tm")
    here = lax.axis_index("tm")
    even = here % 2 == 0
    up = jnp.where(even, 1, -1)
    tok, width = queries.shape
    blocks = FRAMES * BANDS
    cands = block_list.shape[1]

    flags = (block_list > 0).astype(jnp.bfloat16).reshape(1, blocks * cands)
    flags = jnp.pad(flags, ((0, LIST_ROWS - 1), (0, width - blocks * cands)))
    far_q_data = down_even(queries)
    near_q_data = up_even(queries)
    pack = jnp.concatenate([grad_out, flags], axis=0)
    far_data = down_even(pack)
    near_data = up_even(pack)
    partner_keys, partner_values = swap_cores((keys, values))
    key_both = jnp.concatenate([keys, partner_keys], axis=0)
    value_both = jnp.concatenate([values, partner_values], axis=0)

    slots = {
        "own": (queries, grad_out, 0, 0, block_list, 0, True, (0, -1), (0, 1)),
        "far": (far_q_data, far_data, 0, 0, None, 2 * up, True, (2, 1), (-2, -1)),
        "near": (near_q_data, near_data, 0, 0, None, -2 * up, False, (-2,), (2,)),
    }

    args = {}
    stats_out = {}
    for name in ("own", "far", "near"):
        if name == "far":
            fq, fg, nq, ng, stats_out["own"] = lax.optimization_barrier(
                (far_q_data, far_data, near_q_data, near_data, stats_out["own"])
            )
            slots["far"] = (fq, fg) + slots["far"][2:]
            slots["near"] = (nq, ng) + slots["near"][2:]
        q_arr, g_arr, q_rows, g_rows, rows, q_off, both, offs_e, offs_o = slots[name]
        if rows is None:
            rows = g_arr[tok, : blocks * cands].reshape(blocks, cands)
        key_arr, value_arr = (key_both, value_both) if both else (keys, values)
        nkb = key_arr.shape[0] // BLOCK
        source = here + q_off
        valid = (source >= 0) & (source < groups)
        table, own = parity_tables(even, offs_e, offs_o)
        chosen = jnp.einsum("qc,qck->qk", (rows > 0).astype(jnp.float32), table) > 0
        mask4 = (chosen & valid) | own
        mask_t = jnp.broadcast_to(
            mask4.T[:, None, :, None], (nkb, BLOCK, blocks, BLOCK)
        ).reshape(nkb * BLOCK, tok).astype(jnp.float32)
        args[name] = (q_arr, g_arr, q_rows, g_rows, key_arr, value_arr, mask_t)
        stats_out[name] = slot_stats(*args[name], tok)

    stats_in = [
        (stats_out["own"], 0),
        (up_even(stats_out["far"]), -2 * up),
        (down_even(stats_out["near"]), 2 * up),
    ]
    maxes, sums = [], []
    for stats, offset in stats_in:
        source = here + offset
        valid = (source >= 0) & (source < groups)
        maxes.append(jnp.where(valid, stats[:, 0], NEG))
        sums.append(jnp.where(valid, stats[:, 1], 0.0))
    maxes, sums = jnp.stack(maxes), jnp.stack(sums)
    top = jnp.max(maxes, axis=0)
    total = jnp.sum(sums * jnp.exp(maxes - top[None]), axis=0)
    log_total = (top + jnp.log(total))[:, None, :]
    lses = {"own": log_total, "far": down_even(log_total), "near": up_even(log_total)}
    parts = {name: slot_delta(*args[name], lses[name], tok) for name in slots}
    deltas = parts["own"] + up_even(parts["far"]) + down_even(parts["near"])
    final = jnp.concatenate([log_total, deltas], axis=1)
    finals = {"far": down_even(final), "near": up_even(final)}

    own_q, own_k, own_v = slot_back(*args["own"], final, tok, jnp.float32)
    far_fin, near_fin, own_k, own_v = lax.optimization_barrier(
        (finals["far"], finals["near"], own_k, own_v)
    )
    finals = {"far": far_fin, "near": near_fin}
    far_q, far_k, far_v = slot_back(*args["far"], finals["far"], tok, jnp.bfloat16)
    near_q, near_k, near_v = slot_back(*args["near"], finals["near"], tok, jnp.bfloat16)
    from_far = up_even(far_q)
    from_near = down_even(near_q)

    def low(x):
        return x.astype(jnp.bfloat16).astype(jnp.float32)

    back_kg, back_vg = swap_cores(
        (low(far_k[tok:]) + low(own_k[tok:]), low(far_v[tok:]) + low(own_v[tok:]))
    )
    key_grad = (low(far_k[:tok]) + low(own_k[:tok]) + low(near_k) + back_kg).astype(jnp.bfloat16)
    value_grad = (low(far_v[:tok]) + low(own_v[:tok]) + low(near_v) + back_vg).astype(jnp.bfloat16)
    from_far, from_near, key_grad, value_grad = lax.optimization_barrier(
        (from_far, from_near, key_grad, value_grad)
    )
    query_grad = own_q + from_far.astype(jnp.float32) + from_near.astype(jnp.float32)
    return query_grad.astype(jnp.bfloat16), key_grad, value_grad


def solution(mesh):
    placed = (
        P(("group", "tm"), None),
        P(("group", "tm"), None),
        P(("group", "tm"), None),
        P(("group", "tm"), None),
        P(("group", "tm"), None),
    )
    return jax.shard_map(
        local,
        mesh=mesh,
        in_specs=placed,
        out_specs=(P(("group", "tm"), None), P(("group", "tm"), None), P(("group", "tm"), None)),
        check_vma=False,
    )
```

```python
import jax
import jax.numpy as jnp
import numpy as np
from jax import lax
from jax.experimental import pallas as pl
from jax.experimental.pallas import tpu as pltpu
from jax.sharding import PartitionSpec as P

HEADS = 12
HDIM = 128
BLOCK = 64
REACH = 2
FRAMES = 2
BANDS = 2
NEG = -1e30
LIST_ROWS = 16


def permute(value, rule):
    count = lax.axis_size("tm")
    pairs = []
    for source in range(count):
        target = rule(source)
        if 0 <= target < count:
            pairs.append((source, target))
    return lax.ppermute(value, "tm", pairs)


def swap_cores(value):
    return permute(value, lambda s: s ^ 1)


def down_even(value):
    return permute(value, lambda s: s - 2 if s % 2 == 0 else s + 2)


def up_even(value):
    return permute(value, lambda s: s + 2 if s % 2 == 0 else s - 2)


def pick_table(offset):
    blocks = FRAMES * BANDS
    slot = REACH - offset
    table = np.zeros((blocks, 30, blocks), np.float32)
    own = np.zeros((blocks, blocks), bool)
    if abs(offset) <= REACH:
        for qb in range(blocks):
            for kb in range(blocks):
                cand = (slot * FRAMES + kb // BANDS) * 3 + kb % BANDS - qb % BANDS + 1
                table[qb, cand, kb] = 1.0
                own[qb, kb] = offset == 0 and qb == kb
    return table, own


def parity_tables(even, even_offsets, odd_offsets):
    tables, owns = [], []
    for off_e, off_o in zip(even_offsets, odd_offsets):
        t_e, o_e = pick_table(off_e)
        t_o, o_o = pick_table(off_o)
        tables.append(jnp.where(even, jnp.asarray(t_e), jnp.asarray(t_o)))
        owns.append(jnp.where(even, jnp.asarray(o_e), jnp.asarray(o_o)))
    return jnp.concatenate(tables, axis=2), jnp.concatenate(owns, axis=1)


SCALE = HDIM ** (-0.5)
NT = (((1,), (1,)), ((), ()))
STEP_HEADS = 4


def slot_scores(q, g, k, v):
    s = lax.dot_general(k, q, NT, preferred_element_type=jnp.float32) * SCALE
    dp = lax.dot_general(v, g, NT, preferred_element_type=jnp.float32)
    return s, dp


def head_cols(j):
    return slice(j * HDIM, (j + 1) * HDIM)


def stats_kernel(q_ref, k_ref, m_ref, out_ref):
    m = m_ref[...] > 0
    for j in range(STEP_HEADS):
        cols = head_cols(j)
        s = lax.dot_general(k_ref[:, cols], q_ref[:, cols], NT, preferred_element_type=jnp.float32)
        s = s * SCALE
        masked = jnp.where(m, s, NEG)
        mx = jnp.max(masked, axis=0, keepdims=True)
        e = jnp.where(m, jnp.exp(masked - mx), 0.0)
        total = jnp.sum(e, axis=0, keepdims=True)
        out_ref[j] = jnp.concatenate([mx, total], axis=0)


def delta_kernel(q_ref, g_ref, k_ref, v_ref, m_ref, f_ref, out_ref):
    m = m_ref[...] > 0
    for j in range(STEP_HEADS):
        cols = head_cols(j)
        s, dp = slot_scores(q_ref[:, cols], g_ref[:, cols], k_ref[:, cols], v_ref[:, cols])
        p = jnp.where(m, jnp.exp(s - f_ref[j]), 0.0)
        low = lax.reduce_precision(p, exponent_bits=8, mantissa_bits=7)
        out_ref[j] = jnp.sum(low * dp, axis=0, keepdims=True)


def back_kernel(q_ref, g_ref, k_ref, v_ref, m_ref, f_ref, dq_ref, dk_ref, dv_ref):
    m = m_ref[...] > 0
    for j in range(STEP_HEADS):
        cols = head_cols(j)
        q = q_ref[:, cols]
        g = g_ref[:, cols]
        k = k_ref[:, cols]
        s, dp = slot_scores(q, g, k, v_ref[:, cols])
        fin = f_ref[j]
        p = jnp.where(m, jnp.exp(s - fin[0:1]), 0.0)
        ds = (p * (dp - fin[1:2])).astype(jnp.bfloat16)
        dk = jnp.dot(ds, q, preferred_element_type=jnp.float32) * SCALE
        dk_ref[:, cols] = dk.astype(dk_ref.dtype)
        dv = jnp.dot(p.astype(jnp.bfloat16), g, preferred_element_type=jnp.float32)
        dv_ref[:, cols] = dv.astype(dv_ref.dtype)
        dq = lax.dot_general(ds, k, (((0,), (0,)), ((), ())), preferred_element_type=jnp.float32)
        dq_ref[:, cols] = (dq * SCALE).astype(dq_ref.dtype)


def slot_specs(q_rows, g_rows, nk, tok):
    cols = STEP_HEADS * HDIM
    return [
        pl.BlockSpec((tok, cols), lambda h: (q_rows, h)),
        pl.BlockSpec((tok, cols), lambda h: (g_rows, h)),
        pl.BlockSpec((nk, cols), lambda h: (0, h)),
        pl.BlockSpec((nk, cols), lambda h: (0, h)),
        pl.BlockSpec((nk, tok), lambda h: (0, 0)),
    ]


def slot_stats(q_arr, g_arr, q_rows, g_rows, key_arr, value_arr, mask_t, tok):
    nk = key_arr.shape[0]
    flops = 2 * tok * nk * HDIM * HEADS
    return pl.pallas_call(
        stats_kernel,
        grid=(HEADS // STEP_HEADS,),
        in_specs=[slot_specs(q_rows, g_rows, nk, tok)[i] for i in (0, 2, 4)],
        out_specs=pl.BlockSpec((STEP_HEADS, 2, tok), lambda h: (h, 0, 0)),
        out_shape=jax.ShapeDtypeStruct((HEADS, 2, tok), jnp.float32),
        cost_estimate=pl.CostEstimate(
            flops=flops, transcendentals=tok * nk * HEADS, bytes_accessed=4 * (tok + nk) * HDIM * HEADS
        ),
    )(q_arr, key_arr, mask_t)


def slot_delta(q_arr, g_arr, q_rows, g_rows, key_arr, value_arr, mask_t, lse, tok):
    nk = key_arr.shape[0]
    flops = 4 * tok * nk * HDIM * HEADS
    return pl.pallas_call(
        delta_kernel,
        grid=(HEADS // STEP_HEADS,),
        in_specs=slot_specs(q_rows, g_rows, nk, tok)
        + [pl.BlockSpec((STEP_HEADS, 1, tok), lambda h: (h, 0, 0))],
        out_specs=pl.BlockSpec((STEP_HEADS, 1, tok), lambda h: (h, 0, 0)),
        out_shape=jax.ShapeDtypeStruct((HEADS, 1, tok), jnp.float32),
        cost_estimate=pl.CostEstimate(
            flops=flops, transcendentals=tok * nk * HEADS, bytes_accessed=4 * (tok + nk) * HDIM * HEADS
        ),
    )(q_arr, g_arr, key_arr, value_arr, mask_t, lse)


def slot_back(q_arr, g_arr, q_rows, g_rows, key_arr, value_arr, mask_t, fin, tok, dq_type):
    nk = key_arr.shape[0]
    width = HEADS * HDIM
    flops = 10 * tok * nk * HDIM * HEADS
    return pl.pallas_call(
        back_kernel,
        grid=(HEADS // STEP_HEADS,),
        in_specs=slot_specs(q_rows, g_rows, nk, tok)
        + [pl.BlockSpec((STEP_HEADS, 2, tok), lambda h: (h, 0, 0))],
        out_specs=[
            pl.BlockSpec((tok, STEP_HEADS * HDIM), lambda h: (0, h)),
            pl.BlockSpec((nk, STEP_HEADS * HDIM), lambda h: (0, h)),
            pl.BlockSpec((nk, STEP_HEADS * HDIM), lambda h: (0, h)),
        ],
        out_shape=[
            jax.ShapeDtypeStruct((tok, width), dq_type),
            jax.ShapeDtypeStruct((nk, width), jnp.bfloat16),
            jax.ShapeDtypeStruct((nk, width), jnp.bfloat16),
        ],
        cost_estimate=pl.CostEstimate(
            flops=flops, transcendentals=tok * nk * HEADS, bytes_accessed=12 * (tok + nk) * HDIM * HEADS
        ),
    )(q_arr, g_arr, key_arr, value_arr, mask_t, fin)


def local(queries, keys, values, grad_out, block_list):
    groups = lax.axis_size("tm")
    here = lax.axis_index("tm")
    even = here % 2 == 0
    up = jnp.where(even, 1, -1)
    tok, width = queries.shape
    blocks = FRAMES * BANDS
    cands = block_list.shape[1]

    flags = (block_list > 0).astype(jnp.bfloat16).reshape(1, blocks * cands)
    flags = jnp.pad(flags, ((0, LIST_ROWS - 1), (0, width - blocks * cands)))
    far_q_data = down_even(queries)
    near_q_data = up_even(queries)
    pack = jnp.concatenate([grad_out, flags], axis=0)
    far_data = down_even(pack)
    near_data = up_even(pack)
    partner_keys, partner_values = swap_cores((keys, values))
    key_both = jnp.concatenate([keys, partner_keys], axis=0)
    value_both = jnp.concatenate([values, partner_values], axis=0)

    slots = {
        "own": (queries, grad_out, 0, 0, block_list, 0, True, (0, -1), (0, 1)),
        "far": (far_q_data, far_data, 0, 0, None, 2 * up, True, (2, 1), (-2, -1)),
        "near": (near_q_data, near_data, 0, 0, None, -2 * up, False, (-2,), (2,)),
    }

    args = {}
    stats_out = {}
    for name in ("own", "far", "near"):
        if name == "far":
            fq, fg, nq, ng, stats_out["own"] = lax.optimization_barrier(
                (far_q_data, far_data, near_q_data, near_data, stats_out["own"])
            )
            slots["far"] = (fq, fg) + slots["far"][2:]
            slots["near"] = (nq, ng) + slots["near"][2:]
        q_arr, g_arr, q_rows, g_rows, rows, q_off, both, offs_e, offs_o = slots[name]
        if rows is None:
            rows = g_arr[tok, : blocks * cands].reshape(blocks, cands)
        key_arr, value_arr = (key_both, value_both) if both else (keys, values)
        nkb = key_arr.shape[0] // BLOCK
        source = here + q_off
        valid = (source >= 0) & (source < groups)
        table, own = parity_tables(even, offs_e, offs_o)
        chosen = jnp.einsum("qc,qck->qk", (rows > 0).astype(jnp.float32), table) > 0
        mask4 = (chosen & valid) | own
        mask_t = jnp.broadcast_to(
            mask4.T[:, None, :, None], (nkb, BLOCK, blocks, BLOCK)
        ).reshape(nkb * BLOCK, tok).astype(jnp.float32)
        args[name] = (q_arr, g_arr, q_rows, g_rows, key_arr, value_arr, mask_t)
        stats_out[name] = slot_stats(*args[name], tok)

    stats_in = [
        (stats_out["own"], 0),
        (up_even(stats_out["far"]), -2 * up),
        (down_even(stats_out["near"]), 2 * up),
    ]
    maxes, sums = [], []
    for stats, offset in stats_in:
        source = here + offset
        valid = (source >= 0) & (source < groups)
        maxes.append(jnp.where(valid, stats[:, 0], NEG))
        sums.append(jnp.where(valid, stats[:, 1], 0.0))
    maxes, sums = jnp.stack(maxes), jnp.stack(sums)
    top = jnp.max(maxes, axis=0)
    total = jnp.sum(sums * jnp.exp(maxes - top[None]), axis=0)
    log_total = (top + jnp.log(total))[:, None, :]
    lses = {"own": log_total, "far": down_even(log_total), "near": up_even(log_total)}
    parts = {name: slot_delta(*args[name], lses[name], tok) for name in slots}
    deltas = parts["own"] + up_even(parts["far"]) + down_even(parts["near"])
    final = jnp.concatenate([log_total, deltas], axis=1)
    finals = {"far": down_even(final), "near": up_even(final)}

    own_q, own_k, own_v = slot_back(*args["own"], final, tok, jnp.float32)
    far_fin, near_fin, own_k, own_v = lax.optimization_barrier(
        (finals["far"], finals["near"], own_k, own_v)
    )
    finals = {"far": far_fin, "near": near_fin}
    far_q, far_k, far_v = slot_back(*args["far"], finals["far"], tok, jnp.bfloat16)
    near_q, near_k, near_v = slot_back(*args["near"], finals["near"], tok, jnp.bfloat16)
    from_far = up_even(far_q)
    from_near = down_even(near_q)

    def low(x):
        return x.astype(jnp.bfloat16).astype(jnp.float32)

    back_kg, back_vg = swap_cores(
        (low(far_k[tok:]) + low(own_k[tok:]), low(far_v[tok:]) + low(own_v[tok:]))
    )
    key_grad = (low(far_k[:tok]) + low(own_k[:tok]) + low(near_k) + back_kg).astype(jnp.bfloat16)
    value_grad = (low(far_v[:tok]) + low(own_v[:tok]) + low(near_v) + back_vg).astype(jnp.bfloat16)
    from_far, from_near, key_grad, value_grad = lax.optimization_barrier(
        (from_far, from_near, key_grad, value_grad)
    )
    query_grad = own_q + from_far.astype(jnp.float32) + from_near.astype(jnp.float32)
    return query_grad.astype(jnp.bfloat16), key_grad, value_grad


def solution(mesh):
    placed = (
        P(("group", "tm"), None),
        P(("group", "tm"), None),
        P(("group", "tm"), None),
        P(("group", "tm"), None),
        P(("group", "tm"), None),
    )
    return jax.shard_map(
        local,
        mesh=mesh,
        in_specs=placed,
        out_specs=(P(("group", "tm"), None), P(("group", "tm"), None), P(("group", "tm"), None)),
        check_vma=False,
    )
```

```python
import jax
import jax.numpy as jnp
import numpy as np
from jax import lax
from jax.experimental import pallas as pl
from jax.experimental.pallas import tpu as pltpu
from jax.sharding import PartitionSpec as P

HEADS = 12
HDIM = 128
BLOCK = 64
REACH = 2
FRAMES = 2
BANDS = 2
NEG = -1e30
LIST_ROWS = 16


def permute(value, rule):
    count = lax.axis_size("tm")
    pairs = []
    for source in range(count):
        target = rule(source)
        if 0 <= target < count:
            pairs.append((source, target))
    return lax.ppermute(value, "tm", pairs)


def swap_cores(value):
    return permute(value, lambda s: s ^ 1)


def down_even(value):
    return permute(value, lambda s: s - 2 if s % 2 == 0 else s + 2)


def up_even(value):
    return permute(value, lambda s: s + 2 if s % 2 == 0 else s - 2)


def pick_table(offset):
    blocks = FRAMES * BANDS
    slot = REACH - offset
    table = np.zeros((blocks, 30, blocks), np.float32)
    own = np.zeros((blocks, blocks), bool)
    if abs(offset) <= REACH:
        for qb in range(blocks):
            for kb in range(blocks):
                cand = (slot * FRAMES + kb // BANDS) * 3 + kb % BANDS - qb % BANDS + 1
                table[qb, cand, kb] = 1.0
                own[qb, kb] = offset == 0 and qb == kb
    return table, own


def parity_tables(even, even_offsets, odd_offsets):
    tables, owns = [], []
    for off_e, off_o in zip(even_offsets, odd_offsets):
        t_e, o_e = pick_table(off_e)
        t_o, o_o = pick_table(off_o)
        tables.append(jnp.where(even, jnp.asarray(t_e), jnp.asarray(t_o)))
        owns.append(jnp.where(even, jnp.asarray(o_e), jnp.asarray(o_o)))
    return jnp.concatenate(tables, axis=2), jnp.concatenate(owns, axis=1)


SCALE = HDIM ** (-0.5)
NT = (((1,), (1,)), ((), ()))
STEP_HEADS = 6


def slot_scores(q, g, k, v):
    s = lax.dot_general(k, q, NT, preferred_element_type=jnp.float32) * SCALE
    dp = lax.dot_general(v, g, NT, preferred_element_type=jnp.float32)
    return s, dp


def head_cols(j):
    return slice(j * HDIM, (j + 1) * HDIM)


def stats_kernel(q_ref, k_ref, m_ref, out_ref):
    m = m_ref[...] > 0
    for j in range(STEP_HEADS):
        cols = head_cols(j)
        s = lax.dot_general(k_ref[:, cols], q_ref[:, cols], NT, preferred_element_type=jnp.float32)
        s = s * SCALE
        masked = jnp.where(m, s, NEG)
        mx = jnp.max(masked, axis=0, keepdims=True)
        e = jnp.where(m, jnp.exp(masked - mx), 0.0)
        total = jnp.sum(e, axis=0, keepdims=True)
        out_ref[j] = jnp.concatenate([mx, total], axis=0)


def delta_kernel(q_ref, g_ref, k_ref, v_ref, m_ref, f_ref, out_ref):
    m = m_ref[...] > 0
    for j in range(STEP_HEADS):
        cols = head_cols(j)
        s, dp = slot_scores(q_ref[:, cols], g_ref[:, cols], k_ref[:, cols], v_ref[:, cols])
        p = jnp.where(m, jnp.exp(s - f_ref[j]), 0.0)
        low = lax.reduce_precision(p, exponent_bits=8, mantissa_bits=7)
        out_ref[j] = jnp.sum(low * dp, axis=0, keepdims=True)


def back_kernel(q_ref, g_ref, k_ref, v_ref, m_ref, f_ref, dq_ref, dk_ref, dv_ref):
    m = m_ref[...] > 0
    for j in range(STEP_HEADS):
        cols = head_cols(j)
        q = q_ref[:, cols]
        g = g_ref[:, cols]
        k = k_ref[:, cols]
        s, dp = slot_scores(q, g, k, v_ref[:, cols])
        fin = f_ref[j]
        p = jnp.where(m, jnp.exp(s - fin[0:1]), 0.0)
        ds = (p * (dp - fin[1:2])).astype(jnp.bfloat16)
        dk_ref[:, cols] = jnp.dot(ds, q, preferred_element_type=jnp.float32) * SCALE
        dv_ref[:, cols] = jnp.dot(p.astype(jnp.bfloat16), g, preferred_element_type=jnp.float32)
        dq = lax.dot_general(ds, k, (((0,), (0,)), ((), ())), preferred_element_type=jnp.float32)
        dq_ref[:, cols] = (dq * SCALE).astype(dq_ref.dtype)


def slot_specs(q_rows, g_rows, nk, tok):
    cols = STEP_HEADS * HDIM
    return [
        pl.BlockSpec((tok, cols), lambda h: (q_rows, h)),
        pl.BlockSpec((tok, cols), lambda h: (g_rows, h)),
        pl.BlockSpec((nk, cols), lambda h: (0, h)),
        pl.BlockSpec((nk, cols), lambda h: (0, h)),
        pl.BlockSpec((nk, tok), lambda h: (0, 0)),
    ]


def slot_stats(q_arr, g_arr, q_rows, g_rows, key_arr, value_arr, mask_t, tok):
    nk = key_arr.shape[0]
    flops = 2 * tok * nk * HDIM * HEADS
    return pl.pallas_call(
        stats_kernel,
        grid=(HEADS // STEP_HEADS,),
        in_specs=[slot_specs(q_rows, g_rows, nk, tok)[i] for i in (0, 2, 4)],
        out_specs=pl.BlockSpec((STEP_HEADS, 2, tok), lambda h: (h, 0, 0)),
        out_shape=jax.ShapeDtypeStruct((HEADS, 2, tok), jnp.float32),
        cost_estimate=pl.CostEstimate(
            flops=flops, transcendentals=tok * nk * HEADS, bytes_accessed=4 * (tok + nk) * HDIM * HEADS
        ),
    )(q_arr, key_arr, mask_t)


def slot_delta(q_arr, g_arr, q_rows, g_rows, key_arr, value_arr, mask_t, lse, tok):
    nk = key_arr.shape[0]
    flops = 4 * tok * nk * HDIM * HEADS
    return pl.pallas_call(
        delta_kernel,
        grid=(HEADS // STEP_HEADS,),
        in_specs=slot_specs(q_rows, g_rows, nk, tok)
        + [pl.BlockSpec((STEP_HEADS, 1, tok), lambda h: (h, 0, 0))],
        out_specs=pl.BlockSpec((STEP_HEADS, 1, tok), lambda h: (h, 0, 0)),
        out_shape=jax.ShapeDtypeStruct((HEADS, 1, tok), jnp.float32),
        cost_estimate=pl.CostEstimate(
            flops=flops, transcendentals=tok * nk * HEADS, bytes_accessed=4 * (tok + nk) * HDIM * HEADS
        ),
    )(q_arr, g_arr, key_arr, value_arr, mask_t, lse)


def slot_back(q_arr, g_arr, q_rows, g_rows, key_arr, value_arr, mask_t, fin, tok, dq_type):
    nk = key_arr.shape[0]
    width = HEADS * HDIM
    flops = 10 * tok * nk * HDIM * HEADS
    return pl.pallas_call(
        back_kernel,
        grid=(HEADS // STEP_HEADS,),
        in_specs=slot_specs(q_rows, g_rows, nk, tok)
        + [pl.BlockSpec((STEP_HEADS, 2, tok), lambda h: (h, 0, 0))],
        out_specs=[
            pl.BlockSpec((tok, STEP_HEADS * HDIM), lambda h: (0, h)),
            pl.BlockSpec((nk, STEP_HEADS * HDIM), lambda h: (0, h)),
            pl.BlockSpec((nk, STEP_HEADS * HDIM), lambda h: (0, h)),
        ],
        out_shape=[
            jax.ShapeDtypeStruct((tok, width), dq_type),
            jax.ShapeDtypeStruct((nk, width), jnp.float32),
            jax.ShapeDtypeStruct((nk, width), jnp.float32),
        ],
        cost_estimate=pl.CostEstimate(
            flops=flops, transcendentals=tok * nk * HEADS, bytes_accessed=12 * (tok + nk) * HDIM * HEADS
        ),
    )(q_arr, g_arr, key_arr, value_arr, mask_t, fin)


def local(queries, keys, values, grad_out, block_list):
    groups = lax.axis_size("tm")
    here = lax.axis_index("tm")
    even = here % 2 == 0
    up = jnp.where(even, 1, -1)
    tok, width = queries.shape
    blocks = FRAMES * BANDS
    cands = block_list.shape[1]

    flags = (block_list > 0).astype(jnp.bfloat16).reshape(1, blocks * cands)
    flags = jnp.pad(flags, ((0, LIST_ROWS - 1), (0, width - blocks * cands)))
    far_q_data = down_even(queries)
    near_q_data = up_even(queries)
    pack = jnp.concatenate([grad_out, flags], axis=0)
    far_data = down_even(pack)
    near_data = up_even(pack)
    partner_keys, partner_values = swap_cores((keys, values))
    key_both = jnp.concatenate([keys, partner_keys], axis=0)
    value_both = jnp.concatenate([values, partner_values], axis=0)

    slots = {
        "own": (queries, grad_out, 0, 0, block_list, 0, True, (0, -1), (0, 1)),
        "far": (far_q_data, far_data, 0, 0, None, 2 * up, True, (2, 1), (-2, -1)),
        "near": (near_q_data, near_data, 0, 0, None, -2 * up, False, (-2,), (2,)),
    }

    args = {}
    stats_out = {}
    for name in ("own", "far", "near"):
        if name == "far":
            fq, fg, nq, ng, stats_out["own"] = lax.optimization_barrier(
                (far_q_data, far_data, near_q_data, near_data, stats_out["own"])
            )
            slots["far"] = (fq, fg) + slots["far"][2:]
            slots["near"] = (nq, ng) + slots["near"][2:]
        q_arr, g_arr, q_rows, g_rows, rows, q_off, both, offs_e, offs_o = slots[name]
        if rows is None:
            rows = g_arr[tok, : blocks * cands].reshape(blocks, cands)
        key_arr, value_arr = (key_both, value_both) if both else (keys, values)
        nkb = key_arr.shape[0] // BLOCK
        source = here + q_off
        valid = (source >= 0) & (source < groups)
        table, own = parity_tables(even, offs_e, offs_o)
        chosen = jnp.einsum("qc,qck->qk", (rows > 0).astype(jnp.float32), table) > 0
        mask4 = (chosen & valid) | own
        mask_t = jnp.broadcast_to(
            mask4.T[:, None, :, None], (nkb, BLOCK, blocks, BLOCK)
        ).reshape(nkb * BLOCK, tok).astype(jnp.float32)
        args[name] = (q_arr, g_arr, q_rows, g_rows, key_arr, value_arr, mask_t)
        stats_out[name] = slot_stats(*args[name], tok)

    stats_in = [
        (stats_out["own"], 0),
        (up_even(stats_out["far"]), -2 * up),
        (down_even(stats_out["near"]), 2 * up),
    ]
    maxes, sums = [], []
    for stats, offset in stats_in:
        source = here + offset
        valid = (source >= 0) & (source < groups)
        maxes.append(jnp.where(valid, stats[:, 0], NEG))
        sums.append(jnp.where(valid, stats[:, 1], 0.0))
    maxes, sums = jnp.stack(maxes), jnp.stack(sums)
    top = jnp.max(maxes, axis=0)
    total = jnp.sum(sums * jnp.exp(maxes - top[None]), axis=0)
    log_total = (top + jnp.log(total))[:, None, :]
    lses = {"own": log_total, "far": down_even(log_total), "near": up_even(log_total)}
    parts = {name: slot_delta(*args[name], lses[name], tok) for name in slots}
    deltas = parts["own"] + up_even(parts["far"]) + down_even(parts["near"])
    final = jnp.concatenate([log_total, deltas], axis=1)
    finals = {"far": down_even(final), "near": up_even(final)}

    own_q, own_k, own_v = slot_back(*args["own"], final, tok, jnp.float32)
    far_fin, near_fin, own_k, own_v = lax.optimization_barrier(
        (finals["far"], finals["near"], own_k, own_v)
    )
    finals = {"far": far_fin, "near": near_fin}
    far_q, far_k, far_v = slot_back(*args["far"], finals["far"], tok, jnp.bfloat16)
    near_q, near_k, near_v = slot_back(*args["near"], finals["near"], tok, jnp.bfloat16)
    from_far = up_even(far_q)
    from_near = down_even(near_q)

    def low(x):
        return x.astype(jnp.bfloat16).astype(jnp.float32)

    back_kg, back_vg = swap_cores(
        (low(far_k[tok:]) + low(own_k[tok:]), low(far_v[tok:]) + low(own_v[tok:]))
    )
    key_grad = (low(far_k[:tok]) + low(own_k[:tok]) + low(near_k) + back_kg).astype(jnp.bfloat16)
    value_grad = (low(far_v[:tok]) + low(own_v[:tok]) + low(near_v) + back_vg).astype(jnp.bfloat16)
    from_far, from_near, key_grad, value_grad = lax.optimization_barrier(
        (from_far, from_near, key_grad, value_grad)
    )
    query_grad = own_q + from_far.astype(jnp.float32) + from_near.astype(jnp.float32)
    return query_grad.astype(jnp.bfloat16), key_grad, value_grad


def solution(mesh):
    placed = (
        P(("group", "tm"), None),
        P(("group", "tm"), None),
        P(("group", "tm"), None),
        P(("group", "tm"), None),
        P(("group", "tm"), None),
    )
    return jax.shard_map(
        local,
        mesh=mesh,
        in_specs=placed,
        out_specs=(P(("group", "tm"), None), P(("group", "tm"), None), P(("group", "tm"), None)),
        check_vma=False,
    )
```
